32 devices in a mesh: row: 2 (over y), col: 4 (over z), chan: 4 (over x, core).
Axes of the slice: x: 2, y: 2, z: 4, core: 2. Of those that a mesh axis runs over, the one named last changes fastest.
Arguments:
- feature: bfloat16 [192, 16, 512], P(None, 'row', 'col'), may hold values from -6 to 6
- kernel: float32 [7, 7, 192], replicated, may hold values from -0.875 to 0.875
- conv_bias: float32 [192], replicated, may hold values from -3 to 3
- norm_gain: float32 [192], replicated, may hold values from 0.5 to 1.5
- norm_bias: float32 [192], replicated, may hold values from -3 to 3
- w_in: bfloat16 [192, 768], P(None, 'chan'), may hold values from -0.4375 to 0.4375
- b_in: float32 [768], P('chan'), may hold values from -3 to 3
- w_out: bfloat16 [768, 192], P('chan'), may hold values from -0.21875 to 0.21875
- b_out: float32 [192], replicated, may hold values from -3 to 3
- layer_scale: float32 [192], replicated, may hold values from 0.3 to 1.5
- cotangent: bfloat16 [192, 16, 512], P(None, 'row', 'col'), may hold values from -6 to 6
Outputs:
- result: bfloat16 [192, 16, 512], P(None, 'row', 'col')
- grad_feature: bfloat16 [192, 16, 512], P(None, 'row', 'col')
- grad_kernel: float32 [7, 7, 192], replicated
- grad_conv_bias: float32 [192], replicated
- norm_gain_gradient: float32 [192], replicated
- grad_ln_bias: float32 [192], replicated
- grad_w_in: float32 [192, 768], P(None, 'chan')
- grad_b_in: float32 [768], P('chan')
- grad_w_out: float32 [768, 192], P('chan')
- grad_b_out: float32 [192], replicated
- grad_layer_scale: float32 [192], replicated
The draws below stay inside these ranges and needn't reach their ends.
All inputs are finite; a program needn't handle non-finite values.
Results may differ from the reference program's by a relative error of at most 0.009.
Values may be sent and summed in bfloat16 or wider, within the bound.
No kernel may reach another device: no remote copies, remote signals or barrier semaphores. Data moves between devices by JAX's collectives and lax.ppermute only.
A program may use at most 64 MiB of HBM per device.

```python
import math
import jax
import jax.numpy as jnp
from jax import lax

C = 192
HID = 768
KS = 7
H = 16
W = 512
N_CHAN = 4


def shard_levels(key, shape, split, smallest, top_value):
    gain = 1.0
    for axis_at, shards_of in split:
        draws = jax.random.uniform(jax.random.fold_in(jax.random.fold_in(key, 6), axis_at), (shards_of,), jnp.float32, smallest / len(split), top_value / len(split))
        gain = gain * jnp.repeat(jnp.exp(draws), shape[axis_at] // shards_of).reshape((-1,) + (1,) * (len(shape) - 1 - axis_at))
    return gain


def normal_values(own_key, extent, deviation, bound, shards=(), dtype=jnp.bfloat16):
    factor_of = shard_levels(own_key, extent, shards, -0.22, 0.18) if shards else 1.0
    drawn = jax.random.normal(own_key, extent, jnp.float32) * deviation * factor_of
    return jnp.minimum(jnp.maximum(drawn, -bound), bound).astype(dtype)


def setup_inputs(seed: int = 0) -> dict:
    seeds = jax.random.split(jax.random.key(seed), 12)
    return {
        "feature": normal_values(seeds[0], (C, H, W), 1.0, 6.0, ((1, 2), (2, 4))),
        "kernel": normal_values(seeds[1], (KS, KS, C), (KS * KS) ** -0.5, 0.875, (), jnp.float32),
        "conv_bias": normal_values(seeds[2], (C,), 0.5, 3.0, (), jnp.float32),
        "norm_gain": jnp.clip(jax.random.uniform(seeds[3], (C,), jnp.float32, 0.5, 1.5), 0.5, 1.5),
        "norm_bias": normal_values(seeds[4], (C,), 0.5, 3.0, (), jnp.float32),
        "w_in": normal_values(seeds[5], (C, HID), C ** -0.5, 0.4375, ((1, 4),)),
        "b_in": normal_values(seeds[6], (HID,), 0.5, 3.0, ((0, 4),), jnp.float32),
        "w_out": normal_values(seeds[7], (HID, C), HID ** -0.5, 0.21875, ((0, 4),)),
        "b_out": normal_values(seeds[8], (C,), 0.5, 3.0, (), jnp.float32),
        "layer_scale": jnp.clip(jnp.exp(jax.random.uniform(seeds[9], (C,), jnp.float32, math.log(0.3), math.log(1.5))), 0.3, 1.5),
        "cotangent": normal_values(seeds[10], (C, H, W), 1.0, 6.0, ((1, 2), (2, 4))),
    }


def depthwise(padded, kernel):
    channel_count = padded.shape[0]
    return lax.conv_general_dilated(padded[None], kernel[:, :, None, :], (1, 1), 'VALID', dimension_numbers=('NCHW', 'HWIO', 'NCHW'), feature_group_count=channel_count, precision=lax.Precision.HIGHEST)[0]

def gelu_parts(pre_act):
    cdf_val = 0.5 * (1.0 + lax.erf(pre_act * 0.7071067811865476))
    density = jnp.exp(-0.5 * pre_act * pre_act) * 0.3989422804014327
    return (pre_act * cdf_val, cdf_val + pre_act * density)

def contract(left, right, dim_left, dim_right):
    return lax.dot_general(left, right, (((dim_left,), (dim_right,)), ((), ())), preferred_element_type=jnp.float32)

def reference(feature, kernel, conv_bias, norm_gain, norm_bias, w_in, b_in, w_out, b_out, layer_scale, cotangent):
    channel_count, height, width = feature.shape
    pixel_count = height * width
    padded = jnp.pad(feature.astype(jnp.float32), ((0, 0), (3, 3), (3, 3)))
    convolved_output = depthwise(padded, kernel) + conv_bias[:, None, None]
    conv_flat = convolved_output.reshape(channel_count, pixel_count)
    mean_val = lax.optimization_barrier(jnp.mean(conv_flat, axis=0))
    centered_values = conv_flat - mean_val
    variance = lax.optimization_barrier(jnp.mean(centered_values * centered_values, axis=0))
    inverse_deviation = lax.rsqrt(variance + 1e-06)
    standardized_input = centered_values * inverse_deviation
    normalized_output = (standardized_input * norm_gain[:, None] + norm_bias[:, None]).astype(jnp.bfloat16)
    hid_share = HID // N_CHAN
    mixed_sum = jnp.zeros((channel_count, pixel_count), jnp.float32)
    for block in range(N_CHAN):
        lower = block * hid_share
        pre_act = contract(w_in[:, lower:lower + hid_share], normalized_output, 0, 0) + b_in[lower:lower + hid_share, None]
        hidden = gelu_parts(pre_act)[0].astype(jnp.bfloat16)
        partial_sum = contract(w_out[lower:lower + hid_share], hidden, 0, 0)
        mixed_sum = mixed_sum + lax.optimization_barrier(partial_sum.astype(jnp.bfloat16)).astype(jnp.float32)
    branch = mixed_sum + b_out[:, None]
    result = (feature.reshape(channel_count, pixel_count).astype(jnp.float32) + layer_scale[:, None] * branch).astype(jnp.bfloat16)
    norm_factor = 1.0 / jnp.sqrt(jnp.float32(pixel_count))
    grad_out = cotangent.reshape(channel_count, pixel_count).astype(jnp.float32)
    g_branch = grad_out * layer_scale[:, None]
    grad_layer_scale = lax.optimization_barrier(jnp.sum(grad_out * branch, axis=1))
    grad_b_out = lax.optimization_barrier(jnp.sum(g_branch, axis=1))
    g_out = g_branch.astype(jnp.bfloat16)
    normalized_gradient = jnp.zeros((channel_count, pixel_count), jnp.float32)
    list_w_in, list_b_in, list_w_out = ([], [], [])
    for block in range(N_CHAN):
        lower = block * hid_share
        w_in_block = w_in[:, lower:lower + hid_share]
        w_out_block = w_out[lower:lower + hid_share]
        pre_act = contract(w_in_block, normalized_output, 0, 0) + b_in[lower:lower + hid_share, None]
        gelu_val, gelu_slope = gelu_parts(pre_act)
        hidden = gelu_val.astype(jnp.bfloat16)
        list_w_out.append(contract(hidden, g_out, 1, 1))
        d_hidden = contract(w_out_block, g_out, 1, 0)
        d_pre = d_hidden * gelu_slope
        list_b_in.append(lax.optimization_barrier(jnp.sum(d_pre, axis=1)))
        g_pre = d_pre.astype(jnp.bfloat16)
        list_w_in.append(contract(normalized_output, g_pre, 1, 1))
        dn_term = contract(w_in_block, g_pre, 1, 0)
        normalized_gradient = normalized_gradient + lax.optimization_barrier(dn_term.astype(jnp.bfloat16)).astype(jnp.float32)
    grad_w_in = jnp.concatenate(list_w_in, axis=1)
    grad_b_in = jnp.concatenate(list_b_in, axis=0)
    grad_w_out = jnp.concatenate(list_w_out, axis=0)
    norm_gain_gradient = lax.optimization_barrier(jnp.sum(normalized_gradient * standardized_input, axis=1))
    grad_ln_bias = lax.optimization_barrier(jnp.sum(normalized_gradient, axis=1))
    standardized_gradient = normalized_gradient * norm_gain[:, None]
    initial_mean = lax.optimization_barrier(jnp.mean(standardized_gradient, axis=0))
    product_mean = lax.optimization_barrier(jnp.mean(standardized_gradient * standardized_input, axis=0))
    convolved_gradient = inverse_deviation * (standardized_gradient - initial_mean - standardized_input * product_mean)
    grad_conv_bias = lax.optimization_barrier(jnp.sum(convolved_gradient, axis=1))
    d_grid = convolved_gradient.reshape(channel_count, height, width)
    pullback = jax.vjp(lambda weights: depthwise(padded, weights), kernel)[1]
    grad_kernel = pullback(d_grid)[0]
    d_padded = jnp.pad(d_grid, ((0, 0), (3, 3), (3, 3)))
    grad_feature = (cotangent.astype(jnp.float32) + depthwise(d_padded, kernel[::-1, ::-1])).astype(jnp.bfloat16)
    return (result.reshape(channel_count, height, width), grad_feature, grad_kernel * norm_factor, grad_conv_bias * norm_factor, norm_gain_gradient * norm_factor, grad_ln_bias * norm_factor, grad_w_in * norm_factor, grad_b_in * norm_factor, grad_w_out * norm_factor, grad_b_out * norm_factor, grad_layer_scale * norm_factor)
```

```python
import jax
import jax.numpy as jnp
from jax import lax
from jax.experimental import pallas as pl
from jax.sharding import PartitionSpec as P


def extended(x, sides, width):
    for axis, dim in sides:
        devices, length = (lax.axis_size(axis), x.shape[dim])
        up = [(i, (i + 1) % devices) for i in range(devices - 1)]
        down = [(j, i) for i, j in up]
        last = lax.slice_in_dim(x, length - width, length, axis=dim)
        leading = lax.slice_in_dim(x, 0, width, axis=dim)
        before = lax.ppermute(last, axis, up)
        after = lax.ppermute(leading, axis, down)
        x = jnp.concatenate([before, x, after], axis=dim)
    return x


def shortened(x):
    return jax.tree.map(lambda a: a.astype(jnp.bfloat16) if a.dtype == jnp.float32 else a, x)


def depthwise(padded, kernel):
    channel_count = padded.shape[0]
    return lax.conv_general_dilated(
        padded[None],
        kernel[:, :, None, :],
        (1, 1),
        "VALID",
        dimension_numbers=("NCHW", "HWIO", "NCHW"),
        feature_group_count=channel_count,
        precision=lax.Precision.HIGHEST,
    )[0]


def gelu_parts(pre_act):
    cdf_val = 0.5 * (1.0 + lax.erf(pre_act * 0.7071067811865476))
    density = jnp.exp(-0.5 * pre_act * pre_act) * 0.3989422804014327
    return (pre_act * cdf_val, cdf_val + pre_act * density)


def contract(left, right, dim_left, dim_right):
    return lax.dot_general(
        left, right, (((dim_left,), (dim_right,)), ((), ())), preferred_element_type=jnp.float32
    )


def layer_norm_forward(conv_flat, norm_gain, norm_bias):
    mean_val = jnp.mean(conv_flat, axis=0)
    centered_values = conv_flat - mean_val
    variance = jnp.mean(centered_values * centered_values, axis=0)
    inverse_deviation = lax.rsqrt(variance + 1e-06)
    standardized_input = centered_values * inverse_deviation
    normalized_output = (standardized_input * norm_gain[:, None] + norm_bias[:, None]).astype(
        jnp.bfloat16
    )
    return (standardized_input, inverse_deviation, normalized_output)


def layer_norm_backward(normalized_gradient, standardized_input, inverse_deviation, norm_gain):
    standardized_gradient = normalized_gradient * norm_gain[:, None]
    initial_mean = jnp.mean(standardized_gradient, axis=0)
    product_mean = jnp.mean(standardized_gradient * standardized_input, axis=0)
    convolved_gradient = inverse_deviation * (
        standardized_gradient - initial_mean - standardized_input * product_mean
    )
    return (
        convolved_gradient,
        jnp.sum(normalized_gradient * standardized_input, axis=1),
        jnp.sum(normalized_gradient, axis=1),
    )


def kernel_grad_body(d_ref, p_ref, o_ref):
    rows, cols, _ = d_ref.shape
    taps = o_ref.shape[0]
    side = int(round(taps ** 0.5))
    o_ref[...] = jnp.zeros(o_ref.shape, o_ref.dtype)

    def row_step(h, carry):
        d_row = d_ref[h]
        for i in range(side):
            for j in range(side):
                prod = d_row * p_ref[h + i, j : j + cols, :]
                part = jnp.sum(prod.reshape(cols // 8, 8, prod.shape[-1]), axis=0)
                o_ref[i * side + j] += part
        return carry

    lax.fori_loop(0, rows, row_step, 0)


def kernel_grad(d_grid, padded):
    d_t = jnp.transpose(d_grid, (1, 2, 0))
    p_t = jnp.transpose(padded, (1, 2, 0))
    side = padded.shape[1] - d_grid.shape[1] + 1
    channel_count = d_grid.shape[0]
    partial = pl.pallas_call(
        kernel_grad_body,
        out_shape=jax.ShapeDtypeStruct((side * side, 8, channel_count), jnp.float32),
    )(d_t, p_t)
    return jnp.sum(partial, axis=1).reshape(side, side, channel_count)


def shards(
    feature,
    kernel,
    conv_bias,
    norm_gain,
    norm_bias,
    w_in,
    b_in,
    w_out,
    b_out,
    layer_scale,
    cotangent,
):
    channel_count, tile_rows, tile_cols = feature.shape
    pixel_count = tile_rows * tile_cols
    blocks = lax.axis_size("chan")
    share = w_in.shape[1]
    own = lax.axis_index("chan")
    w_in_all = lax.all_gather(w_in, "chan", axis=1, tiled=True)
    b_in_all = lax.all_gather(b_in, "chan", axis=0, tiled=True)
    w_out_all = lax.all_gather(w_out, "chan", axis=0, tiled=True)
    padded_bf = extended(feature, (("row", 1), ("col", 2)), 3)
    padded = padded_bf.astype(jnp.float32)
    total_pixels = pixel_count * lax.axis_size("row") * lax.axis_size("col")
    norm_factor = 1.0 / jnp.sqrt(jnp.float32(total_pixels))
    convolved_output = depthwise(padded, kernel) + conv_bias[:, None, None]
    standardized_input, inverse_deviation, normalized_output = layer_norm_forward(
        convolved_output.reshape(channel_count, pixel_count), norm_gain, norm_bias
    )
    pre_act = contract(w_in_all, normalized_output, 0, 0) + b_in_all[:, None]
    gelu_val, gelu_slope = gelu_parts(pre_act)
    hidden = gelu_val.astype(jnp.bfloat16)
    w_out_blocks = w_out_all.reshape(blocks, share, channel_count)
    hidden_blocks = hidden.reshape(blocks, share, pixel_count)
    out_partials = lax.dot_general(
        w_out_blocks,
        hidden_blocks,
        (((1,), (1,)), ((0,), (0,))),
        preferred_element_type=jnp.float32,
    )
    mixed_sum = jnp.sum(out_partials.astype(jnp.bfloat16).astype(jnp.float32), axis=0)
    branch = mixed_sum + b_out[:, None]
    feature_flat = feature.reshape(channel_count, pixel_count)
    result = (
        (feature_flat.astype(jnp.float32) + layer_scale[:, None] * branch)
        .astype(jnp.bfloat16)
        .reshape(channel_count, tile_rows, tile_cols)
    )
    grad_out = cotangent.reshape(channel_count, pixel_count).astype(jnp.float32)
    g_branch = grad_out * layer_scale[:, None]
    grad_layer_scale = jnp.sum(grad_out * branch, axis=1)
    grad_b_out = jnp.sum(g_branch, axis=1)
    g_out = g_branch.astype(jnp.bfloat16)
    d_pre = contract(w_out_all, g_out, 1, 0) * gelu_slope
    g_pre = d_pre.astype(jnp.bfloat16)
    hidden_own = lax.dynamic_slice_in_dim(hidden, own * share, share, axis=0)
    g_pre_own = lax.dynamic_slice_in_dim(g_pre, own * share, share, axis=0)
    d_pre_own = lax.dynamic_slice_in_dim(d_pre, own * share, share, axis=0)
    grad_w_out = contract(hidden_own, g_out, 1, 1)
    grad_b_in = jnp.sum(d_pre_own, axis=1)
    grad_w_in = contract(normalized_output, g_pre_own, 1, 1)
    (grad_w_in, grad_b_in, grad_w_out, grad_b_out, grad_layer_scale) = lax.psum(
        (grad_w_in, grad_b_in, grad_w_out, grad_b_out, grad_layer_scale), ("row", "col")
    )
    w_in_blocks = jnp.transpose(w_in_all.reshape(channel_count, blocks, share), (1, 0, 2))
    g_pre_blocks = g_pre.reshape(blocks, share, pixel_count)
    dn_partials = lax.dot_general(
        w_in_blocks,
        g_pre_blocks,
        (((2,), (1,)), ((0,), (0,))),
        preferred_element_type=jnp.float32,
    )
    normalized_gradient = jnp.sum(dn_partials.astype(jnp.bfloat16).astype(jnp.float32), axis=0)
    convolved_gradient, gain_portion, bias_portion = layer_norm_backward(
        normalized_gradient, standardized_input, inverse_deviation, norm_gain
    )
    grad_conv_bias = jnp.sum(convolved_gradient, axis=1)
    d_grid = convolved_gradient.reshape(channel_count, tile_rows, tile_cols)
    grad_kernel = kernel_grad(d_grid, padded)
    (grad_kernel, grad_conv_bias, gain_portion, bias_portion) = lax.psum(
        (grad_kernel, grad_conv_bias, gain_portion, bias_portion), ("row", "col")
    )
    d_padded = extended(shortened(d_grid), (("row", 1), ("col", 2)), 3).astype(d_grid.dtype)
    grad_feature = (cotangent.astype(jnp.float32) + depthwise(d_padded, kernel[::-1, ::-1])).astype(
        jnp.bfloat16
    )
    return (
        result,
        grad_feature,
        grad_kernel * norm_factor,
        grad_conv_bias * norm_factor,
        gain_portion * norm_factor,
        bias_portion * norm_factor,
        grad_w_in * norm_factor,
        grad_b_in * norm_factor,
        grad_w_out * norm_factor,
        grad_b_out * norm_factor,
        grad_layer_scale * norm_factor,
    )


def solution(mesh):
    return jax.shard_map(
        shards,
        mesh=mesh,
        in_specs=(
            P(None, "row", "col"),
            P(),
            P(),
            P(),
            P(),
            P(None, "chan"),
            P("chan"),
            P("chan", None),
            P(),
            P(),
            P(None, "row", "col"),
        ),
        out_specs=(
            P(None, "row", "col"),
            P(None, "row", "col"),
            P(),
            P(),
            P(),
            P(),
            P(None, "chan"),
            P("chan"),
            P("chan", None),
            P(),
            P(),
        ),
        check_vma=False,
    )
```

```python
import jax
import jax.numpy as jnp
from jax import lax
from jax.experimental import pallas as pl
from jax.sharding import PartitionSpec as P


def extended(x, sides, width):
    for axis, dim in sides:
        devices, length = (lax.axis_size(axis), x.shape[dim])
        up = [(i, (i + 1) % devices) for i in range(devices - 1)]
        down = [(j, i) for i, j in up]
        last = lax.slice_in_dim(x, length - width, length, axis=dim)
        leading = lax.slice_in_dim(x, 0, width, axis=dim)
        before = lax.ppermute(last, axis, up)
        after = lax.ppermute(leading, axis, down)
        x = jnp.concatenate([before, x, after], axis=dim)
    return x


def shortened(x):
    return jax.tree.map(lambda a: a.astype(jnp.bfloat16) if a.dtype == jnp.float32 else a, x)


def depthwise(padded, kernel):
    channel_count = padded.shape[0]
    return lax.conv_general_dilated(
        padded[None],
        kernel[:, :, None, :],
        (1, 1),
        "VALID",
        dimension_numbers=("NCHW", "HWIO", "NCHW"),
        feature_group_count=channel_count,
        precision=lax.Precision.HIGHEST,
    )[0]


def gelu_parts(pre_act):
    cdf_val = 0.5 * (1.0 + lax.erf(pre_act * 0.7071067811865476))
    density = jnp.exp(-0.5 * pre_act * pre_act) * 0.3989422804014327
    return (pre_act * cdf_val, cdf_val + pre_act * density)


def contract(left, right, dim_left, dim_right):
    return lax.dot_general(
        left, right, (((dim_left,), (dim_right,)), ((), ())), preferred_element_type=jnp.float32
    )


def layer_norm_forward(conv_flat, norm_gain, norm_bias):
    mean_val = jnp.mean(conv_flat, axis=0)
    centered_values = conv_flat - mean_val
    variance = jnp.mean(centered_values * centered_values, axis=0)
    inverse_deviation = lax.rsqrt(variance + 1e-06)
    standardized_input = centered_values * inverse_deviation
    normalized_output = (standardized_input * norm_gain[:, None] + norm_bias[:, None]).astype(
        jnp.bfloat16
    )
    return (standardized_input, inverse_deviation, normalized_output)


def layer_norm_backward(normalized_gradient, standardized_input, inverse_deviation, norm_gain):
    standardized_gradient = normalized_gradient * norm_gain[:, None]
    initial_mean = jnp.mean(standardized_gradient, axis=0)
    product_mean = jnp.mean(standardized_gradient * standardized_input, axis=0)
    convolved_gradient = inverse_deviation * (
        standardized_gradient - initial_mean - standardized_input * product_mean
    )
    return (
        convolved_gradient,
        jnp.sum(normalized_gradient * standardized_input, axis=1),
        jnp.sum(normalized_gradient, axis=1),
    )


def kernel_grad_body(d_ref, p_ref, o_ref):
    rows, cols, _ = d_ref.shape
    taps = o_ref.shape[0]
    side = int(round(taps ** 0.5))
    o_ref[...] = jnp.zeros(o_ref.shape, o_ref.dtype)

    def row_step(h, carry):
        d_row = d_ref[h]
        for i in range(side):
            for j in range(side):
                prod = d_row * p_ref[h + i, j : j + cols, :]
                part = jnp.sum(prod.reshape(cols // 8, 8, prod.shape[-1]), axis=0)
                o_ref[i * side + j] += part
        return carry

    lax.fori_loop(0, rows, row_step, 0)


def kernel_grad(d_grid, padded):
    d_t = jnp.transpose(d_grid, (1, 2, 0))
    p_t = jnp.transpose(padded, (1, 2, 0))
    side = padded.shape[1] - d_grid.shape[1] + 1
    channel_count = d_grid.shape[0]
    partial = pl.pallas_call(
        kernel_grad_body,
        out_shape=jax.ShapeDtypeStruct((side * side, 8, channel_count), jnp.float32),
    )(d_t, p_t)
    return jnp.sum(partial, axis=1).reshape(side, side, channel_count)


def butterfly_sum(values, axes):
    shapes = [v.shape for v in values]
    flat = jnp.concatenate([v.reshape(-1) for v in values])
    for axis in axes:
        devices = lax.axis_size(axis)
        if devices & (devices - 1):
            flat = lax.psum(flat, axis)
            continue
        step = 1
        while step < devices:
            flat = flat + lax.ppermute(flat, axis, [(i, i ^ step) for i in range(devices)])
            step *= 2
    out = []
    offset = 0
    for shape in shapes:
        size = 1
        for s in shape:
            size *= s
        out.append(flat[offset : offset + size].reshape(shape))
        offset += size
    return out


def gathered_weights(w_in, b_in, w_out):
    channel_count = w_in.shape[0]
    pieces = []
    rest = b_in
    for _ in range(3):
        piece = rest.astype(jnp.bfloat16)
        rest = rest - piece.astype(jnp.float32)
        pieces.append(piece[:, None])
    packed = jnp.concatenate([w_in.T, w_out] + pieces, axis=1)
    full = lax.all_gather(packed, "chan", axis=0, tiled=True)
    w_in_all = full[:, :channel_count].T
    w_out_all = full[:, channel_count : 2 * channel_count]
    parts = full[:, 2 * channel_count :].astype(jnp.float32)
    b_in_all = (parts[:, 0] + parts[:, 1]) + parts[:, 2]
    return w_in_all, b_in_all, w_out_all


def shards(
    feature,
    kernel,
    conv_bias,
    norm_gain,
    norm_bias,
    w_in,
    b_in,
    w_out,
    b_out,
    layer_scale,
    cotangent,
):
    channel_count, tile_rows, tile_cols = feature.shape
    pixel_count = tile_rows * tile_cols
    blocks = lax.axis_size("chan")
    share = w_in.shape[1]
    own = lax.axis_index("chan")
    w_in_all, b_in_all, w_out_all = gathered_weights(w_in, b_in, w_out)
    padded_bf = extended(feature, (("row", 1), ("col", 2)), 3)
    padded = padded_bf.astype(jnp.float32)
    total_pixels = pixel_count * lax.axis_size("row") * lax.axis_size("col")
    norm_factor = 1.0 / jnp.sqrt(jnp.float32(total_pixels))
    convolved_output = depthwise(padded, kernel) + conv_bias[:, None, None]
    standardized_input, inverse_deviation, normalized_output = layer_norm_forward(
        convolved_output.reshape(channel_count, pixel_count), norm_gain, norm_bias
    )
    pre_act = contract(w_in_all, normalized_output, 0, 0) + b_in_all[:, None]
    gelu_val, gelu_slope = gelu_parts(pre_act)
    hidden = gelu_val.astype(jnp.bfloat16)
    w_out_blocks = w_out_all.reshape(blocks, share, channel_count)
    hidden_blocks = hidden.reshape(blocks, share, pixel_count)
    out_partials = lax.dot_general(
        w_out_blocks,
        hidden_blocks,
        (((1,), (1,)), ((0,), (0,))),
        preferred_element_type=jnp.float32,
    )
    mixed_sum = jnp.sum(out_partials.astype(jnp.bfloat16).astype(jnp.float32), axis=0)
    branch = mixed_sum + b_out[:, None]
    feature_flat = feature.reshape(channel_count, pixel_count)
    result = (
        (feature_flat.astype(jnp.float32) + layer_scale[:, None] * branch)
        .astype(jnp.bfloat16)
        .reshape(channel_count, tile_rows, tile_cols)
    )
    grad_out = cotangent.reshape(channel_count, pixel_count).astype(jnp.float32)
    g_branch = grad_out * layer_scale[:, None]
    grad_layer_scale = jnp.sum(grad_out * branch, axis=1)
    grad_b_out = jnp.sum(g_branch, axis=1)
    g_out = g_branch.astype(jnp.bfloat16)
    d_pre = contract(w_out_all, g_out, 1, 0) * gelu_slope
    g_pre = d_pre.astype(jnp.bfloat16)
    hidden_own = lax.dynamic_slice_in_dim(hidden, own * share, share, axis=0)
    g_pre_own = lax.dynamic_slice_in_dim(g_pre, own * share, share, axis=0)
    d_pre_own = lax.dynamic_slice_in_dim(d_pre, own * share, share, axis=0)
    grad_w_out = contract(hidden_own, g_out, 1, 1)
    grad_b_in = jnp.sum(d_pre_own, axis=1)
    grad_w_in = contract(normalized_output, g_pre_own, 1, 1)
    (grad_w_in, grad_b_in, grad_w_out, grad_b_out, grad_layer_scale) = butterfly_sum(
        (grad_w_in, grad_b_in, grad_w_out, grad_b_out, grad_layer_scale), ("row", "col")
    )
    w_in_blocks = jnp.transpose(w_in_all.reshape(channel_count, blocks, share), (1, 0, 2))
    g_pre_blocks = g_pre.reshape(blocks, share, pixel_count)
    dn_partials = lax.dot_general(
        w_in_blocks,
        g_pre_blocks,
        (((2,), (1,)), ((0,), (0,))),
        preferred_element_type=jnp.float32,
    )
    normalized_gradient = jnp.sum(dn_partials.astype(jnp.bfloat16).astype(jnp.float32), axis=0)
    convolved_gradient, gain_portion, bias_portion = layer_norm_backward(
        normalized_gradient, standardized_input, inverse_deviation, norm_gain
    )
    grad_conv_bias = jnp.sum(convolved_gradient, axis=1)
    d_grid = convolved_gradient.reshape(channel_count, tile_rows, tile_cols)
    grad_kernel = kernel_grad(d_grid, padded)
    (grad_kernel, grad_conv_bias, gain_portion, bias_portion) = butterfly_sum(
        (grad_kernel, grad_conv_bias, gain_portion, bias_portion), ("row", "col")
    )
    d_padded = extended(shortened(d_grid), (("row", 1), ("col", 2)), 3).astype(d_grid.dtype)
    grad_feature = (cotangent.astype(jnp.float32) + depthwise(d_padded, kernel[::-1, ::-1])).astype(
        jnp.bfloat16
    )
    return (
        result,
        grad_feature,
        grad_kernel * norm_factor,
        grad_conv_bias * norm_factor,
        gain_portion * norm_factor,
        bias_portion * norm_factor,
        grad_w_in * norm_factor,
        grad_b_in * norm_factor,
        grad_w_out * norm_factor,
        grad_b_out * norm_factor,
        grad_layer_scale * norm_factor,
    )


def solution(mesh):
    return jax.shard_map(
        shards,
        mesh=mesh,
        in_specs=(
            P(None, "row", "col"),
            P(),
            P(),
            P(),
            P(),
            P(None, "chan"),
            P("chan"),
            P("chan", None),
            P(),
            P(),
            P(None, "row", "col"),
        ),
        out_specs=(
            P(None, "row", "col"),
            P(None, "row", "col"),
            P(),
            P(),
            P(),
            P(),
            P(None, "chan"),
            P("chan"),
            P("chan", None),
            P(),
            P(),
        ),
        check_vma=False,
    )
```

```python
import jax
import jax.numpy as jnp
from jax import lax
from jax.experimental import pallas as pl
from jax.sharding import PartitionSpec as P


def extended(x, sides, width):
    for axis, dim in sides:
        devices, length = (lax.axis_size(axis), x.shape[dim])
        up = [(i, (i + 1) % devices) for i in range(devices - 1)]
        down = [(j, i) for i, j in up]
        last = lax.slice_in_dim(x, length - width, length, axis=dim)
        leading = lax.slice_in_dim(x, 0, width, axis=dim)
        before = lax.ppermute(last, axis, up)
        after = lax.ppermute(leading, axis, down)
        x = jnp.concatenate([before, x, after], axis=dim)
    return x


def shortened(x):
    return jax.tree.map(lambda a: a.astype(jnp.bfloat16) if a.dtype == jnp.float32 else a, x)


def depthwise(padded, kernel):
    channel_count = padded.shape[0]
    return lax.conv_general_dilated(
        padded[None],
        kernel[:, :, None, :],
        (1, 1),
        "VALID",
        dimension_numbers=("NCHW", "HWIO", "NCHW"),
        feature_group_count=channel_count,
        precision=lax.Precision.HIGHEST,
    )[0]


def gelu_parts(pre_act):
    cdf_val = 0.5 * (1.0 + lax.erf(pre_act * 0.7071067811865476))
    density = jnp.exp(-0.5 * pre_act * pre_act) * 0.3989422804014327
    return (pre_act * cdf_val, cdf_val + pre_act * density)


def contract(left, right, dim_left, dim_right):
    return lax.dot_general(
        left, right, (((dim_left,), (dim_right,)), ((), ())), preferred_element_type=jnp.float32
    )


def layer_norm_forward(conv_flat, norm_gain, norm_bias):
    mean_val = jnp.mean(conv_flat, axis=0)
    centered_values = conv_flat - mean_val
    variance = jnp.mean(centered_values * centered_values, axis=0)
    inverse_deviation = lax.rsqrt(variance + 1e-06)
    standardized_input = centered_values * inverse_deviation
    normalized_output = (standardized_input * norm_gain[:, None] + norm_bias[:, None]).astype(
        jnp.bfloat16
    )
    return (standardized_input, inverse_deviation, normalized_output)


def layer_norm_backward(normalized_gradient, standardized_input, inverse_deviation, norm_gain):
    standardized_gradient = normalized_gradient * norm_gain[:, None]
    initial_mean = jnp.mean(standardized_gradient, axis=0)
    product_mean = jnp.mean(standardized_gradient * standardized_input, axis=0)
    convolved_gradient = inverse_deviation * (
        standardized_gradient - initial_mean - standardized_input * product_mean
    )
    return (
        convolved_gradient,
        jnp.sum(normalized_gradient * standardized_input, axis=1),
        jnp.sum(normalized_gradient, axis=1),
    )


def kernel_grad_body(d_ref, p_ref, o_ref):
    rows, cols, _ = d_ref.shape
    taps = o_ref.shape[0]
    side = int(round(taps ** 0.5))
    o_ref[...] = jnp.zeros(o_ref.shape, o_ref.dtype)

    def row_step(h, carry):
        d_row = d_ref[h]
        for i in range(side):
            for j in range(side):
                prod = d_row * p_ref[h + i, j : j + cols, :]
                part = jnp.sum(prod.reshape(cols // 8, 8, prod.shape[-1]), axis=0)
                o_ref[i * side + j] += part
        return carry

    lax.fori_loop(0, rows, row_step, 0)


def kernel_grad(d_grid, padded):
    d_t = jnp.transpose(d_grid, (1, 2, 0))
    p_t = jnp.transpose(padded, (1, 2, 0))
    side = padded.shape[1] - d_grid.shape[1] + 1
    channel_count = d_grid.shape[0]
    partial = pl.pallas_call(
        kernel_grad_body,
        out_shape=jax.ShapeDtypeStruct((side * side, 8, channel_count), jnp.float32),
    )(d_t, p_t)
    return jnp.sum(partial, axis=1).reshape(side, side, channel_count)


def flat_pack(values):
    return jnp.concatenate([v.reshape(-1) for v in values])


def flat_unpack(flat, values):
    out = []
    offset = 0
    for v in values:
        out.append(flat[offset : offset + v.size].reshape(v.shape))
        offset += v.size
    return out


def butterfly_steps(axes):
    steps = []
    for axis in axes:
        devices = lax.axis_size(axis)
        if devices & (devices - 1):
            steps.append((axis, 0))
            continue
        step = 1
        while step < devices:
            steps.append((axis, step))
            step *= 2
    return steps


def butterfly_step(flat, axis, step):
    if step == 0:
        return lax.psum(flat, axis)
    devices = lax.axis_size(axis)
    return flat + lax.ppermute(flat, axis, [(i, i ^ step) for i in range(devices)])


def butterfly_sum(values, axes):
    flat = flat_pack(values)
    for axis, step in butterfly_steps(axes):
        flat = butterfly_step(flat, axis, step)
    return flat_unpack(flat, values)


def gathered_weights(w_in, b_in, w_out):
    channel_count = w_in.shape[0]
    pieces = []
    rest = b_in
    for _ in range(3):
        piece = rest.astype(jnp.bfloat16)
        rest = rest - piece.astype(jnp.float32)
        pieces.append(piece[:, None])
    packed = jnp.concatenate([w_in.T, w_out] + pieces, axis=1)
    full = lax.all_gather(packed, "chan", axis=0, tiled=True)
    w_in_all = full[:, :channel_count].T
    w_out_all = full[:, channel_count : 2 * channel_count]
    parts = full[:, 2 * channel_count :].astype(jnp.float32)
    b_in_all = (parts[:, 0] + parts[:, 1]) + parts[:, 2]
    return w_in_all, b_in_all, w_out_all


def shards(
    feature,
    kernel,
    conv_bias,
    norm_gain,
    norm_bias,
    w_in,
    b_in,
    w_out,
    b_out,
    layer_scale,
    cotangent,
):
    channel_count, tile_rows, tile_cols = feature.shape
    pixel_count = tile_rows * tile_cols
    blocks = lax.axis_size("chan")
    share = w_in.shape[1]
    own = lax.axis_index("chan")
    w_in_all, b_in_all, w_out_all = gathered_weights(w_in, b_in, w_out)
    padded_bf = extended(feature, (("row", 1), ("col", 2)), 3)
    padded = padded_bf.astype(jnp.float32)
    total_pixels = pixel_count * lax.axis_size("row") * lax.axis_size("col")
    norm_factor = 1.0 / jnp.sqrt(jnp.float32(total_pixels))
    convolved_output = depthwise(padded, kernel) + conv_bias[:, None, None]
    standardized_input, inverse_deviation, normalized_output = layer_norm_forward(
        convolved_output.reshape(channel_count, pixel_count), norm_gain, norm_bias
    )
    pre_act = contract(w_in_all, normalized_output, 0, 0) + b_in_all[:, None]
    gelu_val, gelu_slope = gelu_parts(pre_act)
    hidden = gelu_val.astype(jnp.bfloat16)
    w_out_blocks = w_out_all.reshape(blocks, share, channel_count)
    hidden_blocks = hidden.reshape(blocks, share, pixel_count)
    out_partials = lax.dot_general(
        w_out_blocks,
        hidden_blocks,
        (((1,), (1,)), ((0,), (0,))),
        preferred_element_type=jnp.float32,
    )
    mixed_sum = jnp.sum(out_partials.astype(jnp.bfloat16).astype(jnp.float32), axis=0)
    branch = mixed_sum + b_out[:, None]
    feature_flat = feature.reshape(channel_count, pixel_count)
    result = (
        (feature_flat.astype(jnp.float32) + layer_scale[:, None] * branch)
        .astype(jnp.bfloat16)
        .reshape(channel_count, tile_rows, tile_cols)
    )
    grad_out = cotangent.reshape(channel_count, pixel_count).astype(jnp.float32)
    g_branch = grad_out * layer_scale[:, None]
    grad_layer_scale = jnp.sum(grad_out * branch, axis=1)
    grad_b_out = jnp.sum(g_branch, axis=1)
    g_out = g_branch.astype(jnp.bfloat16)
    d_pre = contract(w_out_all, g_out, 1, 0) * gelu_slope
    g_pre = d_pre.astype(jnp.bfloat16)
    hidden_own = lax.dynamic_slice_in_dim(hidden, own * share, share, axis=0)
    g_pre_own = lax.dynamic_slice_in_dim(g_pre, own * share, share, axis=0)
    d_pre_own = lax.dynamic_slice_in_dim(d_pre, own * share, share, axis=0)
    grad_w_out = contract(hidden_own, g_out, 1, 1)
    grad_b_in = jnp.sum(d_pre_own, axis=1)
    grad_w_in = contract(normalized_output, g_pre_own, 1, 1)
    early = (grad_w_in, grad_b_in, grad_w_out, grad_b_out, grad_layer_scale)
    early_flat = flat_pack(early)
    pending = butterfly_steps(("row", "col"))
    w_in_blocks = jnp.transpose(w_in_all.reshape(channel_count, blocks, share), (1, 0, 2))
    g_pre_blocks = g_pre.reshape(blocks, share, pixel_count)
    dn_partials = lax.dot_general(
        w_in_blocks,
        g_pre_blocks,
        (((2,), (1,)), ((0,), (0,))),
        preferred_element_type=jnp.float32,
    )
    normalized_gradient = jnp.sum(dn_partials.astype(jnp.bfloat16).astype(jnp.float32), axis=0)
    if pending:
        early_flat = butterfly_step(early_flat, *pending.pop(0))
        early_flat, normalized_gradient = lax.optimization_barrier((early_flat, normalized_gradient))
    convolved_gradient, gain_portion, bias_portion = layer_norm_backward(
        normalized_gradient, standardized_input, inverse_deviation, norm_gain
    )
    grad_conv_bias = jnp.sum(convolved_gradient, axis=1)
    d_grid = convolved_gradient.reshape(channel_count, tile_rows, tile_cols)
    if pending:
        early_flat = butterfly_step(early_flat, *pending.pop(0))
        early_flat, d_grid = lax.optimization_barrier((early_flat, d_grid))
    grad_kernel = kernel_grad(d_grid, padded)
    (grad_kernel, grad_conv_bias, gain_portion, bias_portion) = butterfly_sum(
        (grad_kernel, grad_conv_bias, gain_portion, bias_portion), ("row", "col")
    )
    d_padded = extended(shortened(d_grid), (("row", 1), ("col", 2)), 3).astype(d_grid.dtype)
    if pending:
        early_flat = butterfly_step(early_flat, *pending.pop(0))
        early_flat, d_padded = lax.optimization_barrier((early_flat, d_padded))
    for axis, step in pending:
        early_flat = butterfly_step(early_flat, axis, step)
    (grad_w_in, grad_b_in, grad_w_out, grad_b_out, grad_layer_scale) = flat_unpack(early_flat, early)
    grad_feature = (cotangent.astype(jnp.float32) + depthwise(d_padded, kernel[::-1, ::-1])).astype(
        jnp.bfloat16
    )
    return (
        result,
        grad_feature,
        grad_kernel * norm_factor,
        grad_conv_bias * norm_factor,
        gain_portion * norm_factor,
        bias_portion * norm_factor,
        grad_w_in * norm_factor,
        grad_b_in * norm_factor,
        grad_w_out * norm_factor,
        grad_b_out * norm_factor,
        grad_layer_scale * norm_factor,
    )


def solution(mesh):
    return jax.shard_map(
        shards,
        mesh=mesh,
        in_specs=(
            P(None, "row", "col"),
            P(),
            P(),
            P(),
            P(),
            P(None, "chan"),
            P("chan"),
            P("chan", None),
            P(),
            P(),
            P(None, "row", "col"),
        ),
        out_specs=(
            P(None, "row", "col"),
            P(None, "row", "col"),
            P(),
            P(),
            P(),
            P(),
            P(None, "chan"),
            P("chan"),
            P("chan", None),
            P(),
            P(),
        ),
        check_vma=False,
    )
```

```python
import jax
import jax.numpy as jnp
from jax import lax
from jax.experimental import pallas as pl
from jax.sharding import PartitionSpec as P


def extended(x, sides, width):
    for axis, dim in sides:
        devices, length = (lax.axis_size(axis), x.shape[dim])
        up = [(i, (i + 1) % devices) for i in range(devices - 1)]
        down = [(j, i) for i, j in up]
        last = lax.slice_in_dim(x, length - width, length, axis=dim)
        leading = lax.slice_in_dim(x, 0, width, axis=dim)
        before = lax.ppermute(last, axis, up)
        after = lax.ppermute(leading, axis, down)
        x = jnp.concatenate([before, x, after], axis=dim)
    return x


def shortened(x):
    return jax.tree.map(lambda a: a.astype(jnp.bfloat16) if a.dtype == jnp.float32 else a, x)


def depthwise(padded, kernel):
    channel_count = padded.shape[0]
    return lax.conv_general_dilated(
        padded[None],
        kernel[:, :, None, :],
        (1, 1),
        "VALID",
        dimension_numbers=("NCHW", "HWIO", "NCHW"),
        feature_group_count=channel_count,
        precision=lax.Precision.HIGHEST,
    )[0]


def gelu_parts(pre_act):
    cdf_val = 0.5 * (1.0 + lax.erf(pre_act * 0.7071067811865476))
    density = jnp.exp(-0.5 * pre_act * pre_act) * 0.3989422804014327
    return (pre_act * cdf_val, cdf_val + pre_act * density)


def contract(left, right, dim_left, dim_right):
    return lax.dot_general(
        left, right, (((dim_left,), (dim_right,)), ((), ())), preferred_element_type=jnp.float32
    )


def layer_norm_forward(conv_flat, norm_gain, norm_bias):
    mean_val = jnp.mean(conv_flat, axis=0)
    centered_values = conv_flat - mean_val
    variance = jnp.mean(centered_values * centered_values, axis=0)
    inverse_deviation = lax.rsqrt(variance + 1e-06)
    standardized_input = centered_values * inverse_deviation
    normalized_output = (standardized_input * norm_gain[:, None] + norm_bias[:, None]).astype(
        jnp.bfloat16
    )
    return (standardized_input, inverse_deviation, normalized_output)


def layer_norm_backward(normalized_gradient, standardized_input, inverse_deviation, norm_gain):
    standardized_gradient = normalized_gradient * norm_gain[:, None]
    initial_mean = jnp.mean(standardized_gradient, axis=0)
    product_mean = jnp.mean(standardized_gradient * standardized_input, axis=0)
    convolved_gradient = inverse_deviation * (
        standardized_gradient - initial_mean - standardized_input * product_mean
    )
    return (
        convolved_gradient,
        jnp.sum(normalized_gradient * standardized_input, axis=1),
        jnp.sum(normalized_gradient, axis=1),
    )


def kernel_grad_body(d_ref, p_ref, o_ref):
    rows, cols, _ = d_ref.shape
    taps = o_ref.shape[0]
    side = int(round(taps ** 0.5))
    o_ref[...] = jnp.zeros(o_ref.shape, o_ref.dtype)

    def row_step(h, carry):
        d_row = d_ref[h]
        for i in range(side):
            for j in range(side):
                prod = d_row * p_ref[h + i, j : j + cols, :]
                part = jnp.sum(prod.reshape(cols // 8, 8, prod.shape[-1]), axis=0)
                o_ref[i * side + j] += part
        return carry

    lax.fori_loop(0, rows, row_step, 0)


def kernel_grad(d_grid, padded):
    d_t = jnp.transpose(d_grid, (1, 2, 0))
    p_t = jnp.transpose(padded, (1, 2, 0))
    side = padded.shape[1] - d_grid.shape[1] + 1
    channel_count = d_grid.shape[0]
    partial = pl.pallas_call(
        kernel_grad_body,
        out_shape=jax.ShapeDtypeStruct((side * side, 8, channel_count), jnp.float32),
    )(d_t, p_t)
    return jnp.sum(partial, axis=1).reshape(side, side, channel_count)


def butterfly_sum(values, axes):
    shapes = [v.shape for v in values]
    flat = jnp.concatenate([v.reshape(-1) for v in values])
    for axis in axes:
        devices = lax.axis_size(axis)
        if devices & (devices - 1):
            flat = lax.psum(flat, axis)
            continue
        step = 1
        while step < devices:
            flat = flat + lax.ppermute(flat, axis, [(i, i ^ step) for i in range(devices)])
            step *= 2
    out = []
    offset = 0
    for shape in shapes:
        size = 1
        for s in shape:
            size *= s
        out.append(flat[offset : offset + size].reshape(shape))
        offset += size
    return out


def gathered_weights(w_in, b_in, w_out):
    channel_count = w_in.shape[0]
    pieces = []
    rest = b_in
    for _ in range(3):
        piece = rest.astype(jnp.bfloat16)
        rest = rest - piece.astype(jnp.float32)
        pieces.append(piece[:, None])
    packed = jnp.concatenate([w_in.T, w_out] + pieces, axis=1)
    full = lax.all_gather(packed, "chan", axis=0, tiled=True)
    w_in_all = full[:, :channel_count].T
    w_out_all = full[:, channel_count : 2 * channel_count]
    parts = full[:, 2 * channel_count :].astype(jnp.float32)
    b_in_all = (parts[:, 0] + parts[:, 1]) + parts[:, 2]
    return w_in_all, b_in_all, w_out_all


def shards(
    feature,
    kernel,
    conv_bias,
    norm_gain,
    norm_bias,
    w_in,
    b_in,
    w_out,
    b_out,
    layer_scale,
    cotangent,
):
    channel_count, tile_rows, tile_cols = feature.shape
    pixel_count = tile_rows * tile_cols
    blocks = lax.axis_size("chan")
    share = w_in.shape[1]
    own = lax.axis_index("chan")
    w_in_all, b_in_all, w_out_all = gathered_weights(w_in, b_in, w_out)
    padded_bf = extended(feature, (("row", 1), ("col", 2)), 3)
    padded = padded_bf.astype(jnp.float32)
    total_pixels = pixel_count * lax.axis_size("row") * lax.axis_size("col")
    norm_factor = 1.0 / jnp.sqrt(jnp.float32(total_pixels))
    convolved_output = depthwise(padded, kernel) + conv_bias[:, None, None]
    standardized_input, inverse_deviation, normalized_output = layer_norm_forward(
        convolved_output.reshape(channel_count, pixel_count), norm_gain, norm_bias
    )
    pre_act = contract(w_in_all, normalized_output, 0, 0) + b_in_all[:, None]
    gelu_val, gelu_slope = gelu_parts(pre_act)
    hidden = gelu_val.astype(jnp.bfloat16)
    w_out_blocks = w_out_all.reshape(blocks, share, channel_count)
    hidden_blocks = hidden.reshape(blocks, share, pixel_count)
    out_partials = lax.dot_general(
        w_out_blocks,
        hidden_blocks,
        (((1,), (1,)), ((0,), (0,))),
        preferred_element_type=jnp.float32,
    )
    mixed_sum = jnp.sum(out_partials.astype(jnp.bfloat16).astype(jnp.float32), axis=0)
    branch = mixed_sum + b_out[:, None]
    feature_flat = feature.reshape(channel_count, pixel_count)
    result = (
        (feature_flat.astype(jnp.float32) + layer_scale[:, None] * branch)
        .astype(jnp.bfloat16)
        .reshape(channel_count, tile_rows, tile_cols)
    )
    grad_out = cotangent.reshape(channel_count, pixel_count).astype(jnp.float32)
    g_branch = grad_out * layer_scale[:, None]
    grad_layer_scale = jnp.sum(grad_out * branch, axis=1)
    grad_b_out = jnp.sum(g_branch, axis=1)
    g_out = g_branch.astype(jnp.bfloat16)
    d_pre = contract(w_out_all, g_out, 1, 0) * gelu_slope
    g_pre = d_pre.astype(jnp.bfloat16)
    hidden_own = lax.dynamic_slice_in_dim(hidden, own * share, share, axis=0)
    g_pre_own = lax.dynamic_slice_in_dim(g_pre, own * share, share, axis=0)
    d_pre_own = lax.dynamic_slice_in_dim(d_pre, own * share, share, axis=0)
    grad_w_out = contract(hidden_own, g_out, 1, 1)
    grad_b_in = jnp.sum(d_pre_own, axis=1)
    grad_w_in = contract(normalized_output, g_pre_own, 1, 1)
    w_in_blocks = jnp.transpose(w_in_all.reshape(channel_count, blocks, share), (1, 0, 2))
    g_pre_blocks = g_pre.reshape(blocks, share, pixel_count)
    dn_partials = lax.dot_general(
        w_in_blocks,
        g_pre_blocks,
        (((2,), (1,)), ((0,), (0,))),
        preferred_element_type=jnp.float32,
    )
    normalized_gradient = jnp.sum(dn_partials.astype(jnp.bfloat16).astype(jnp.float32), axis=0)
    convolved_gradient, gain_portion, bias_portion = layer_norm_backward(
        normalized_gradient, standardized_input, inverse_deviation, norm_gain
    )
    grad_conv_bias = jnp.sum(convolved_gradient, axis=1)
    d_grid = convolved_gradient.reshape(channel_count, tile_rows, tile_cols)
    grad_kernel = kernel_grad(d_grid, padded)
    (
        grad_kernel,
        grad_conv_bias,
        gain_portion,
        bias_portion,
        grad_w_in,
        grad_b_in,
        grad_w_out,
        grad_b_out,
        grad_layer_scale,
    ) = butterfly_sum(
        (
            grad_kernel,
            grad_conv_bias,
            gain_portion,
            bias_portion,
            grad_w_in,
            grad_b_in,
            grad_w_out,
            grad_b_out,
            grad_layer_scale,
        ),
        ("row", "col"),
    )
    d_padded = extended(shortened(d_grid), (("row", 1), ("col", 2)), 3).astype(d_grid.dtype)
    grad_feature = (cotangent.astype(jnp.float32) + depthwise(d_padded, kernel[::-1, ::-1])).astype(
        jnp.bfloat16
    )
    return (
        result,
        grad_feature,
        grad_kernel * norm_factor,
        grad_conv_bias * norm_factor,
        gain_portion * norm_factor,
        bias_portion * norm_factor,
        grad_w_in * norm_factor,
        grad_b_in * norm_factor,
        grad_w_out * norm_factor,
        grad_b_out * norm_factor,
        grad_layer_scale * norm_factor,
    )


def solution(mesh):
    return jax.shard_map(
        shards,
        mesh=mesh,
        in_specs=(
            P(None, "row", "col"),
            P(),
            P(),
            P(),
            P(),
            P(None, "chan"),
            P("chan"),
            P("chan", None),
            P(),
            P(),
            P(None, "row", "col"),
        ),
        out_specs=(
            P(None, "row", "col"),
            P(None, "row", "col"),
            P(),
            P(),
            P(),
            P(),
            P(None, "chan"),
            P("chan"),
            P("chan", None),
            P(),
            P(),
        ),
        check_vma=False,
    )
```

```python
import jax
import jax.numpy as jnp
from jax import lax
from jax.experimental import pallas as pl
from jax.sharding import PartitionSpec as P


def extended(x, sides, width):
    for axis, dim in sides:
        devices, length = (lax.axis_size(axis), x.shape[dim])
        up = [(i, (i + 1) % devices) for i in range(devices - 1)]
        down = [(j, i) for i, j in up]
        last = lax.slice_in_dim(x, length - width, length, axis=dim)
        leading = lax.slice_in_dim(x, 0, width, axis=dim)
        if devices == 2:
            first = lax.axis_index(axis) == 0
            got = lax.ppermute(jnp.where(first, last, leading), axis, [(0, 1), (1, 0)])
            nothing = jnp.zeros_like(got)
            before = jnp.where(first, nothing, got)
            after = jnp.where(first, got, nothing)
        else:
            before = lax.ppermute(last, axis, up)
            after = lax.ppermute(leading, axis, down)
        x = jnp.concatenate([before, x, after], axis=dim)
    return x


def shortened(x):
    return jax.tree.map(lambda a: a.astype(jnp.bfloat16) if a.dtype == jnp.float32 else a, x)


def depthwise(padded, kernel):
    channel_count = padded.shape[0]
    return lax.conv_general_dilated(
        padded[None],
        kernel[:, :, None, :],
        (1, 1),
        "VALID",
        dimension_numbers=("NCHW", "HWIO", "NCHW"),
        feature_group_count=channel_count,
        precision=lax.Precision.HIGHEST,
    )[0]


def gelu_parts(pre_act):
    cdf_val = 0.5 * (1.0 + lax.erf(pre_act * 0.7071067811865476))
    density = jnp.exp(-0.5 * pre_act * pre_act) * 0.3989422804014327
    return (pre_act * cdf_val, cdf_val + pre_act * density)


def contract(left, right, dim_left, dim_right):
    return lax.dot_general(
        left, right, (((dim_left,), (dim_right,)), ((), ())), preferred_element_type=jnp.float32
    )


def layer_norm_forward(conv_flat, norm_gain, norm_bias):
    mean_val = jnp.mean(conv_flat, axis=0)
    centered_values = conv_flat - mean_val
    variance = jnp.mean(centered_values * centered_values, axis=0)
    inverse_deviation = lax.rsqrt(variance + 1e-06)
    standardized_input = centered_values * inverse_deviation
    normalized_output = (standardized_input * norm_gain[:, None] + norm_bias[:, None]).astype(
        jnp.bfloat16
    )
    return (standardized_input, inverse_deviation, normalized_output)


def layer_norm_backward(normalized_gradient, standardized_input, inverse_deviation, norm_gain):
    standardized_gradient = normalized_gradient * norm_gain[:, None]
    initial_mean = jnp.mean(standardized_gradient, axis=0)
    product_mean = jnp.mean(standardized_gradient * standardized_input, axis=0)
    convolved_gradient = inverse_deviation * (
        standardized_gradient - initial_mean - standardized_input * product_mean
    )
    return (
        convolved_gradient,
        jnp.sum(normalized_gradient * standardized_input, axis=1),
        jnp.sum(normalized_gradient, axis=1),
    )


def kernel_grad_body(d_ref, p_ref, o_ref):
    rows, cols, _ = d_ref.shape
    taps = o_ref.shape[0]
    side = int(round(taps ** 0.5))
    o_ref[...] = jnp.zeros(o_ref.shape, o_ref.dtype)

    def row_step(h, carry):
        d_row = d_ref[h]
        for i in range(side):
            for j in range(side):
                prod = d_row * p_ref[h + i, j : j + cols, :]
                part = jnp.sum(prod.reshape(cols // 8, 8, prod.shape[-1]), axis=0)
                o_ref[i * side + j] += part
        return carry

    lax.fori_loop(0, rows, row_step, 0)


def kernel_grad(d_grid, padded):
    d_t = jnp.transpose(d_grid, (1, 2, 0))
    p_t = jnp.transpose(padded, (1, 2, 0))
    side = padded.shape[1] - d_grid.shape[1] + 1
    channel_count = d_grid.shape[0]
    partial = pl.pallas_call(
        kernel_grad_body,
        out_shape=jax.ShapeDtypeStruct((side * side, 8, channel_count), jnp.float32),
    )(d_t, p_t)
    return jnp.sum(partial, axis=1).reshape(side, side, channel_count)


def butterfly_sum(values, axes):
    shapes = [v.shape for v in values]
    flat = jnp.concatenate([v.reshape(-1) for v in values])
    for axis in axes:
        devices = lax.axis_size(axis)
        if devices & (devices - 1):
            flat = lax.psum(flat, axis)
            continue
        step = 1
        while step < devices:
            flat = flat + lax.ppermute(flat, axis, [(i, i ^ step) for i in range(devices)])
            step *= 2
    out = []
    offset = 0
    for shape in shapes:
        size = 1
        for s in shape:
            size *= s
        out.append(flat[offset : offset + size].reshape(shape))
        offset += size
    return out


def gathered_weights(w_in, b_in, w_out):
    channel_count = w_in.shape[0]
    pieces = []
    rest = b_in
    for _ in range(3):
        piece = rest.astype(jnp.bfloat16)
        rest = rest - piece.astype(jnp.float32)
        pieces.append(piece[:, None])
    packed = jnp.concatenate([w_in.T, w_out] + pieces, axis=1)
    full = lax.all_gather(packed, "chan", axis=0, tiled=True)
    w_in_all = full[:, :channel_count].T
    w_out_all = full[:, channel_count : 2 * channel_count]
    parts = full[:, 2 * channel_count :].astype(jnp.float32)
    b_in_all = (parts[:, 0] + parts[:, 1]) + parts[:, 2]
    return w_in_all, b_in_all, w_out_all


def shards(
    feature,
    kernel,
    conv_bias,
    norm_gain,
    norm_bias,
    w_in,
    b_in,
    w_out,
    b_out,
    layer_scale,
    cotangent,
):
    channel_count, tile_rows, tile_cols = feature.shape
    pixel_count = tile_rows * tile_cols
    blocks = lax.axis_size("chan")
    share = w_in.shape[1]
    own = lax.axis_index("chan")
    w_in_all, b_in_all, w_out_all = gathered_weights(w_in, b_in, w_out)
    padded_bf = extended(feature, (("row", 1), ("col", 2)), 3)
    padded = padded_bf.astype(jnp.float32)
    total_pixels = pixel_count * lax.axis_size("row") * lax.axis_size("col")
    norm_factor = 1.0 / jnp.sqrt(jnp.float32(total_pixels))
    convolved_output = depthwise(padded, kernel) + conv_bias[:, None, None]
    standardized_input, inverse_deviation, normalized_output = layer_norm_forward(
        convolved_output.reshape(channel_count, pixel_count), norm_gain, norm_bias
    )
    pre_act = contract(w_in_all, normalized_output, 0, 0) + b_in_all[:, None]
    gelu_val, gelu_slope = gelu_parts(pre_act)
    hidden = gelu_val.astype(jnp.bfloat16)
    w_out_blocks = w_out_all.reshape(blocks, share, channel_count)
    hidden_blocks = hidden.reshape(blocks, share, pixel_count)
    out_partials = lax.dot_general(
        w_out_blocks,
        hidden_blocks,
        (((1,), (1,)), ((0,), (0,))),
        preferred_element_type=jnp.float32,
    )
    mixed_sum = jnp.sum(out_partials.astype(jnp.bfloat16).astype(jnp.float32), axis=0)
    branch = mixed_sum + b_out[:, None]
    feature_flat = feature.reshape(channel_count, pixel_count)
    result = (
        (feature_flat.astype(jnp.float32) + layer_scale[:, None] * branch)
        .astype(jnp.bfloat16)
        .reshape(channel_count, tile_rows, tile_cols)
    )
    grad_out = cotangent.reshape(channel_count, pixel_count).astype(jnp.float32)
    g_branch = grad_out * layer_scale[:, None]
    grad_layer_scale = jnp.sum(grad_out * branch, axis=1)
    grad_b_out = jnp.sum(g_branch, axis=1)
    g_out = g_branch.astype(jnp.bfloat16)
    d_pre = contract(w_out_all, g_out, 1, 0) * gelu_slope
    g_pre = d_pre.astype(jnp.bfloat16)
    hidden_own = lax.dynamic_slice_in_dim(hidden, own * share, share, axis=0)
    g_pre_own = lax.dynamic_slice_in_dim(g_pre, own * share, share, axis=0)
    d_pre_own = lax.dynamic_slice_in_dim(d_pre, own * share, share, axis=0)
    grad_w_out = contract(hidden_own, g_out, 1, 1)
    grad_b_in = jnp.sum(d_pre_own, axis=1)
    grad_w_in = contract(normalized_output, g_pre_own, 1, 1)
    w_in_blocks = jnp.transpose(w_in_all.reshape(channel_count, blocks, share), (1, 0, 2))
    g_pre_blocks = g_pre.reshape(blocks, share, pixel_count)
    dn_partials = lax.dot_general(
        w_in_blocks,
        g_pre_blocks,
        (((2,), (1,)), ((0,), (0,))),
        preferred_element_type=jnp.float32,
    )
    normalized_gradient = jnp.sum(dn_partials.astype(jnp.bfloat16).astype(jnp.float32), axis=0)
    convolved_gradient, gain_portion, bias_portion = layer_norm_backward(
        normalized_gradient, standardized_input, inverse_deviation, norm_gain
    )
    grad_conv_bias = jnp.sum(convolved_gradient, axis=1)
    d_grid = convolved_gradient.reshape(channel_count, tile_rows, tile_cols)
    grad_kernel = kernel_grad(d_grid, padded)
    (
        grad_kernel,
        grad_conv_bias,
        gain_portion,
        bias_portion,
        grad_w_in,
        grad_b_in,
        grad_w_out,
        grad_b_out,
        grad_layer_scale,
    ) = butterfly_sum(
        (
            grad_kernel,
            grad_conv_bias,
            gain_portion,
            bias_portion,
            grad_w_in,
            grad_b_in,
            grad_w_out,
            grad_b_out,
            grad_layer_scale,
        ),
        ("row", "col"),
    )
    d_padded = extended(shortened(d_grid), (("row", 1), ("col", 2)), 3).astype(d_grid.dtype)
    grad_feature = (cotangent.astype(jnp.float32) + depthwise(d_padded, kernel[::-1, ::-1])).astype(
        jnp.bfloat16
    )
    return (
        result,
        grad_feature,
        grad_kernel * norm_factor,
        grad_conv_bias * norm_factor,
        gain_portion * norm_factor,
        bias_portion * norm_factor,
        grad_w_in * norm_factor,
        grad_b_in * norm_factor,
        grad_w_out * norm_factor,
        grad_b_out * norm_factor,
        grad_layer_scale * norm_factor,
    )


def solution(mesh):
    return jax.shard_map(
        shards,
        mesh=mesh,
        in_specs=(
            P(None, "row", "col"),
            P(),
            P(),
            P(),
            P(),
            P(None, "chan"),
            P("chan"),
            P("chan", None),
            P(),
            P(),
            P(None, "row", "col"),
        ),
        out_specs=(
            P(None, "row", "col"),
            P(None, "row", "col"),
            P(),
            P(),
            P(),
            P(),
            P(None, "chan"),
            P("chan"),
            P("chan", None),
            P(),
            P(),
        ),
        check_vma=False,
    )
```

```python
import jax
import jax.numpy as jnp
from jax import lax
from jax.experimental import pallas as pl
from jax.sharding import PartitionSpec as P


def extended(x, sides, width):
    for axis, dim in sides:
        devices, length = (lax.axis_size(axis), x.shape[dim])
        up = [(i, (i + 1) % devices) for i in range(devices - 1)]
        down = [(j, i) for i, j in up]
        last = lax.slice_in_dim(x, length - width, length, axis=dim)
        leading = lax.slice_in_dim(x, 0, width, axis=dim)
        if devices == 2:
            first = lax.axis_index(axis) == 0
            got = lax.ppermute(jnp.where(first, last, leading), axis, [(0, 1), (1, 0)])
            nothing = jnp.zeros_like(got)
            before = jnp.where(first, nothing, got)
            after = jnp.where(first, got, nothing)
        else:
            before = lax.ppermute(last, axis, up)
            after = lax.ppermute(leading, axis, down)
        x = jnp.concatenate([before, x, after], axis=dim)
    return x


def shortened(x):
    return jax.tree.map(lambda a: a.astype(jnp.bfloat16) if a.dtype == jnp.float32 else a, x)


def depthwise(padded, kernel):
    channel_count = padded.shape[0]
    return lax.conv_general_dilated(
        padded[None],
        kernel[:, :, None, :],
        (1, 1),
        "VALID",
        dimension_numbers=("NCHW", "HWIO", "NCHW"),
        feature_group_count=channel_count,
        precision=lax.Precision.HIGHEST,
    )[0]


def gelu_parts(pre_act):
    cdf_val = 0.5 * (1.0 + lax.erf(pre_act * 0.7071067811865476))
    density = jnp.exp(-0.5 * pre_act * pre_act) * 0.3989422804014327
    return (pre_act * cdf_val, cdf_val + pre_act * density)


def contract(left, right, dim_left, dim_right):
    return lax.dot_general(
        left, right, (((dim_left,), (dim_right,)), ((), ())), preferred_element_type=jnp.float32
    )


def layer_norm_forward(conv_flat, norm_gain, norm_bias):
    mean_val = jnp.mean(conv_flat, axis=0)
    centered_values = conv_flat - mean_val
    variance = jnp.mean(centered_values * centered_values, axis=0)
    inverse_deviation = lax.rsqrt(variance + 1e-06)
    standardized_input = centered_values * inverse_deviation
    normalized_output = (standardized_input * norm_gain[:, None] + norm_bias[:, None]).astype(
        jnp.bfloat16
    )
    return (standardized_input, inverse_deviation, normalized_output)


def layer_norm_backward(normalized_gradient, standardized_input, inverse_deviation, norm_gain):
    standardized_gradient = normalized_gradient * norm_gain[:, None]
    initial_mean = jnp.mean(standardized_gradient, axis=0)
    product_mean = jnp.mean(standardized_gradient * standardized_input, axis=0)
    convolved_gradient = inverse_deviation * (
        standardized_gradient - initial_mean - standardized_input * product_mean
    )
    return (
        convolved_gradient,
        jnp.sum(normalized_gradient * standardized_input, axis=1),
        jnp.sum(normalized_gradient, axis=1),
    )


def kernel_grad_body(d_ref, p_ref, o_ref):
    rows, cols, _ = d_ref.shape
    taps = o_ref.shape[0]
    side = int(round(taps ** 0.5))
    o_ref[...] = jnp.zeros(o_ref.shape, o_ref.dtype)

    def row_step(h, carry):
        d_row = d_ref[h]
        for i in range(side):
            for j in range(side):
                prod = d_row * p_ref[h + i, j : j + cols, :]
                part = jnp.sum(prod.reshape(cols // 8, 8, prod.shape[-1]), axis=0)
                o_ref[i * side + j] += part
        return carry

    lax.fori_loop(0, rows, row_step, 0)


def kernel_grad_minor(d_t, p_t):
    side = p_t.shape[0] - d_t.shape[0] + 1
    channel_count = d_t.shape[-1]
    partial = pl.pallas_call(
        kernel_grad_body,
        out_shape=jax.ShapeDtypeStruct((side * side, 8, channel_count), jnp.float32),
    )(d_t, p_t)
    return jnp.sum(partial, axis=1).reshape(side, side, channel_count)


def butterfly_sum(values, axes):
    shapes = [v.shape for v in values]
    flat = jnp.concatenate([v.reshape(-1) for v in values])
    for axis in axes:
        devices = lax.axis_size(axis)
        if devices & (devices - 1):
            flat = lax.psum(flat, axis)
            continue
        step = 1
        while step < devices:
            flat = flat + lax.ppermute(flat, axis, [(i, i ^ step) for i in range(devices)])
            step *= 2
    out = []
    offset = 0
    for shape in shapes:
        size = 1
        for s in shape:
            size *= s
        out.append(flat[offset : offset + size].reshape(shape))
        offset += size
    return out


def gathered_weights(w_in, b_in, w_out):
    channel_count = w_in.shape[0]
    pieces = []
    rest = b_in
    for _ in range(3):
        piece = rest.astype(jnp.bfloat16)
        rest = rest - piece.astype(jnp.float32)
        pieces.append(piece[:, None])
    packed = jnp.concatenate([w_in.T, w_out] + pieces, axis=1)
    full = lax.all_gather(packed, "chan", axis=0, tiled=True)
    w_in_all = full[:, :channel_count].T
    w_out_all = full[:, channel_count : 2 * channel_count]
    parts = full[:, 2 * channel_count :].astype(jnp.float32)
    b_in_all = (parts[:, 0] + parts[:, 1]) + parts[:, 2]
    return w_in_all, b_in_all, w_out_all


def depthwise_minor(padded_t, kernel):
    channel_count = padded_t.shape[-1]
    return lax.conv_general_dilated(
        padded_t[None],
        kernel[:, :, None, :],
        (1, 1),
        "VALID",
        dimension_numbers=("NHWC", "HWIO", "NHWC"),
        feature_group_count=channel_count,
        precision=lax.Precision.HIGHEST,
    )[0]


def shards(
    feature,
    kernel,
    conv_bias,
    norm_gain,
    norm_bias,
    w_in,
    b_in,
    w_out,
    b_out,
    layer_scale,
    cotangent,
):
    channel_count, tile_rows, tile_cols = feature.shape
    pixel_count = tile_rows * tile_cols
    blocks = lax.axis_size("chan")
    share = w_in.shape[1]
    own = lax.axis_index("chan")
    w_in_all, b_in_all, w_out_all = gathered_weights(w_in, b_in, w_out)
    padded_bf = extended(feature, (("row", 1), ("col", 2)), 3)
    padded_t = jnp.transpose(padded_bf, (1, 2, 0)).astype(jnp.float32)
    total_pixels = pixel_count * lax.axis_size("row") * lax.axis_size("col")
    norm_factor = 1.0 / jnp.sqrt(jnp.float32(total_pixels))
    conv_flat = (depthwise_minor(padded_t, kernel) + conv_bias).reshape(pixel_count, channel_count)
    mean_val = jnp.mean(conv_flat, axis=1, keepdims=True)
    centered_values = conv_flat - mean_val
    variance = jnp.mean(centered_values * centered_values, axis=1, keepdims=True)
    inverse_deviation = lax.rsqrt(variance + 1e-06)
    standardized_input = centered_values * inverse_deviation
    normalized_output = (standardized_input * norm_gain + norm_bias).astype(jnp.bfloat16)
    pre_act = contract(normalized_output, w_in_all, 1, 0) + b_in_all
    gelu_val, gelu_slope = gelu_parts(pre_act)
    hidden = gelu_val.astype(jnp.bfloat16)
    out_partials = lax.dot_general(
        hidden.reshape(pixel_count, blocks, share),
        w_out_all.reshape(blocks, share, channel_count),
        (((2,), (1,)), ((1,), (0,))),
        preferred_element_type=jnp.float32,
    )
    mixed_sum = jnp.sum(out_partials.astype(jnp.bfloat16).astype(jnp.float32), axis=0)
    branch = mixed_sum + b_out
    feature_t = jnp.transpose(feature, (1, 2, 0)).reshape(pixel_count, channel_count)
    result_t = (feature_t.astype(jnp.float32) + layer_scale * branch).astype(jnp.bfloat16)
    result = jnp.transpose(result_t.reshape(tile_rows, tile_cols, channel_count), (2, 0, 1))
    cotangent_t = jnp.transpose(cotangent, (1, 2, 0))
    grad_out = cotangent_t.reshape(pixel_count, channel_count).astype(jnp.float32)
    g_branch = grad_out * layer_scale
    grad_layer_scale = jnp.sum(grad_out * branch, axis=0)
    grad_b_out = jnp.sum(g_branch, axis=0)
    g_out = g_branch.astype(jnp.bfloat16)
    d_pre = contract(g_out, w_out_all, 1, 1) * gelu_slope
    g_pre = d_pre.astype(jnp.bfloat16)
    hidden_own = lax.dynamic_slice_in_dim(hidden, own * share, share, axis=1)
    g_pre_own = lax.dynamic_slice_in_dim(g_pre, own * share, share, axis=1)
    d_pre_own = lax.dynamic_slice_in_dim(d_pre, own * share, share, axis=1)
    grad_w_out = contract(hidden_own, g_out, 0, 0)
    grad_b_in = jnp.sum(d_pre_own, axis=0)
    grad_w_in = contract(normalized_output, g_pre_own, 0, 0)
    dn_partials = lax.dot_general(
        g_pre.reshape(pixel_count, blocks, share),
        w_in_all.reshape(channel_count, blocks, share),
        (((2,), (2,)), ((1,), (1,))),
        preferred_element_type=jnp.float32,
    )
    normalized_gradient = jnp.sum(dn_partials.astype(jnp.bfloat16).astype(jnp.float32), axis=0)
    standardized_gradient = normalized_gradient * norm_gain
    initial_mean = jnp.mean(standardized_gradient, axis=1, keepdims=True)
    product_mean = jnp.mean(standardized_gradient * standardized_input, axis=1, keepdims=True)
    convolved_gradient = inverse_deviation * (
        standardized_gradient - initial_mean - standardized_input * product_mean
    )
    gain_portion = jnp.sum(normalized_gradient * standardized_input, axis=0)
    bias_portion = jnp.sum(normalized_gradient, axis=0)
    grad_conv_bias = jnp.sum(convolved_gradient, axis=0)
    d_t = convolved_gradient.reshape(tile_rows, tile_cols, channel_count)
    grad_kernel = kernel_grad_minor(d_t, padded_t)
    (
        grad_kernel,
        grad_conv_bias,
        gain_portion,
        bias_portion,
        grad_w_in,
        grad_b_in,
        grad_w_out,
        grad_b_out,
        grad_layer_scale,
    ) = butterfly_sum(
        (
            grad_kernel,
            grad_conv_bias,
            gain_portion,
            bias_portion,
            grad_w_in,
            grad_b_in,
            grad_w_out,
            grad_b_out,
            grad_layer_scale,
        ),
        ("row", "col"),
    )
    d_padded = extended(d_t.astype(jnp.bfloat16), (("row", 0), ("col", 1)), 3).astype(jnp.float32)
    grad_feature_t = (
        cotangent_t.astype(jnp.float32) + depthwise_minor(d_padded, kernel[::-1, ::-1])
    ).astype(jnp.bfloat16)
    grad_feature = jnp.transpose(grad_feature_t, (2, 0, 1))
    return (
        result,
        grad_feature,
        grad_kernel * norm_factor,
        grad_conv_bias * norm_factor,
        gain_portion * norm_factor,
        bias_portion * norm_factor,
        grad_w_in * norm_factor,
        grad_b_in * norm_factor,
        grad_w_out * norm_factor,
        grad_b_out * norm_factor,
        grad_layer_scale * norm_factor,
    )


def solution(mesh):
    return jax.shard_map(
        shards,
        mesh=mesh,
        in_specs=(
            P(None, "row", "col"),
            P(),
            P(),
            P(),
            P(),
            P(None, "chan"),
            P("chan"),
            P("chan", None),
            P(),
            P(),
            P(None, "row", "col"),
        ),
        out_specs=(
            P(None, "row", "col"),
            P(None, "row", "col"),
            P(),
            P(),
            P(),
            P(),
            P(None, "chan"),
            P("chan"),
            P("chan", None),
            P(),
            P(),
        ),
        check_vma=False,
    )
```

```python
import jax
import jax.numpy as jnp
from jax import lax
from jax.experimental import pallas as pl
from jax.sharding import PartitionSpec as P


def extended(x, sides, width):
    for axis, dim in sides:
        devices, length = (lax.axis_size(axis), x.shape[dim])
        up = [(i, (i + 1) % devices) for i in range(devices - 1)]
        down = [(j, i) for i, j in up]
        last = lax.slice_in_dim(x, length - width, length, axis=dim)
        leading = lax.slice_in_dim(x, 0, width, axis=dim)
        if devices == 2:
            first = lax.axis_index(axis) == 0
            got = lax.ppermute(jnp.where(first, last, leading), axis, [(0, 1), (1, 0)])
            nothing = jnp.zeros_like(got)
            before = jnp.where(first, nothing, got)
            after = jnp.where(first, got, nothing)
        else:
            before = lax.ppermute(last, axis, up)
            after = lax.ppermute(leading, axis, down)
        x = jnp.concatenate([before, x, after], axis=dim)
    return x


def shortened(x):
    return jax.tree.map(lambda a: a.astype(jnp.bfloat16) if a.dtype == jnp.float32 else a, x)


def depthwise(padded, kernel):
    channel_count = padded.shape[0]
    return lax.conv_general_dilated(
        padded[None],
        kernel[:, :, None, :],
        (1, 1),
        "VALID",
        dimension_numbers=("NCHW", "HWIO", "NCHW"),
        feature_group_count=channel_count,
        precision=lax.Precision.HIGHEST,
    )[0]


def gelu_parts(pre_act):
    cdf_val = 0.5 * (1.0 + lax.erf(pre_act * 0.7071067811865476))
    density = jnp.exp(-0.5 * pre_act * pre_act) * 0.3989422804014327
    return (pre_act * cdf_val, cdf_val + pre_act * density)


def contract(left, right, dim_left, dim_right):
    return lax.dot_general(
        left, right, (((dim_left,), (dim_right,)), ((), ())), preferred_element_type=jnp.float32
    )


def layer_norm_forward(conv_flat, norm_gain, norm_bias):
    mean_val = jnp.mean(conv_flat, axis=0)
    centered_values = conv_flat - mean_val
    variance = jnp.mean(centered_values * centered_values, axis=0)
    inverse_deviation = lax.rsqrt(variance + 1e-06)
    standardized_input = centered_values * inverse_deviation
    normalized_output = (standardized_input * norm_gain[:, None] + norm_bias[:, None]).astype(
        jnp.bfloat16
    )
    return (standardized_input, inverse_deviation, normalized_output)


def layer_norm_backward(normalized_gradient, standardized_input, inverse_deviation, norm_gain):
    standardized_gradient = normalized_gradient * norm_gain[:, None]
    initial_mean = jnp.mean(standardized_gradient, axis=0)
    product_mean = jnp.mean(standardized_gradient * standardized_input, axis=0)
    convolved_gradient = inverse_deviation * (
        standardized_gradient - initial_mean - standardized_input * product_mean
    )
    return (
        convolved_gradient,
        jnp.sum(normalized_gradient * standardized_input, axis=1),
        jnp.sum(normalized_gradient, axis=1),
    )


def kernel_grad_body(d_ref, p_ref, o_ref):
    rows, cols, _ = d_ref.shape
    taps = o_ref.shape[0]
    side = int(round(taps ** 0.5))
    o_ref[...] = jnp.zeros(o_ref.shape, o_ref.dtype)

    def row_step(h, carry):
        d_row = d_ref[h]
        for i in range(side):
            for j in range(side):
                prod = d_row * p_ref[h + i, j : j + cols, :]
                part = jnp.sum(prod.reshape(cols // 8, 8, prod.shape[-1]), axis=0)
                o_ref[i * side + j] += part
        return carry

    lax.fori_loop(0, rows, row_step, 0)


def kernel_grad_minor(d_t, p_t):
    side = p_t.shape[0] - d_t.shape[0] + 1
    channel_count = d_t.shape[-1]
    partial = pl.pallas_call(
        kernel_grad_body,
        out_shape=jax.ShapeDtypeStruct((side * side, 8, channel_count), jnp.float32),
    )(d_t, p_t)
    return jnp.sum(partial, axis=1).reshape(side, side, channel_count)


def flat_pack(values):
    return jnp.concatenate([v.reshape(-1) for v in values])


def flat_unpack(flat, values):
    out = []
    offset = 0
    for v in values:
        out.append(flat[offset : offset + v.size].reshape(v.shape))
        offset += v.size
    return out


def butterfly_steps(axes):
    steps = []
    for axis in axes:
        devices = lax.axis_size(axis)
        if devices & (devices - 1):
            steps.append((axis, 0))
            continue
        step = 1
        while step < devices:
            steps.append((axis, step))
            step *= 2
    return steps


def butterfly_step(flat, axis, step):
    if step == 0:
        return lax.psum(flat, axis)
    devices = lax.axis_size(axis)
    return flat + lax.ppermute(flat, axis, [(i, i ^ step) for i in range(devices)])


def butterfly_sum(values, axes):
    flat = flat_pack(values)
    first = butterfly_steps(axes[:1])
    order_a = first + butterfly_steps(axes[1:])[::-1]
    order_b = order_a[len(first) :] + order_a[: len(first)]
    half = flat.shape[0] // 2
    part_a, part_b = flat[:half], flat[half:]
    for step_a, step_b in zip(order_a, order_b):
        part_a, part_b = butterfly_step(part_a, *step_a), butterfly_step(part_b, *step_b)
    return flat_unpack(jnp.concatenate([part_a, part_b]), values)


def gathered_weights(w_in, b_in, w_out):
    channel_count = w_in.shape[0]
    pieces = []
    rest = b_in
    for _ in range(3):
        piece = rest.astype(jnp.bfloat16)
        rest = rest - piece.astype(jnp.float32)
        pieces.append(piece[:, None])
    packed = jnp.concatenate([w_in.T, w_out] + pieces, axis=1)
    full = lax.all_gather(packed, "chan", axis=0, tiled=True)
    w_in_all = full[:, :channel_count].T
    w_out_all = full[:, channel_count : 2 * channel_count]
    parts = full[:, 2 * channel_count :].astype(jnp.float32)
    b_in_all = (parts[:, 0] + parts[:, 1]) + parts[:, 2]
    return w_in_all, b_in_all, w_out_all


def depthwise_minor(padded_t, kernel):
    channel_count = padded_t.shape[-1]
    return lax.conv_general_dilated(
        padded_t[None],
        kernel[:, :, None, :],
        (1, 1),
        "VALID",
        dimension_numbers=("NHWC", "HWIO", "NHWC"),
        feature_group_count=channel_count,
        precision=lax.Precision.HIGHEST,
    )[0]


def shards(
    feature,
    kernel,
    conv_bias,
    norm_gain,
    norm_bias,
    w_in,
    b_in,
    w_out,
    b_out,
    layer_scale,
    cotangent,
):
    channel_count, tile_rows, tile_cols = feature.shape
    pixel_count = tile_rows * tile_cols
    blocks = lax.axis_size("chan")
    share = w_in.shape[1]
    own = lax.axis_index("chan")
    w_in_all, b_in_all, w_out_all = gathered_weights(w_in, b_in, w_out)
    padded_bf = extended(feature, (("row", 1), ("col", 2)), 3)
    padded_t = jnp.transpose(padded_bf, (1, 2, 0)).astype(jnp.float32)
    total_pixels = pixel_count * lax.axis_size("row") * lax.axis_size("col")
    norm_factor = 1.0 / jnp.sqrt(jnp.float32(total_pixels))
    conv_flat = (depthwise_minor(padded_t, kernel) + conv_bias).reshape(pixel_count, channel_count)
    mean_val = jnp.mean(conv_flat, axis=1, keepdims=True)
    centered_values = conv_flat - mean_val
    variance = jnp.mean(centered_values * centered_values, axis=1, keepdims=True)
    inverse_deviation = lax.rsqrt(variance + 1e-06)
    standardized_input = centered_values * inverse_deviation
    normalized_output = (standardized_input * norm_gain + norm_bias).astype(jnp.bfloat16)
    pre_act = contract(normalized_output, w_in_all, 1, 0) + b_in_all
    gelu_val, gelu_slope = gelu_parts(pre_act)
    hidden = gelu_val.astype(jnp.bfloat16)
    out_partials = lax.dot_general(
        hidden.reshape(pixel_count, blocks, share),
        w_out_all.reshape(blocks, share, channel_count),
        (((2,), (1,)), ((1,), (0,))),
        preferred_element_type=jnp.float32,
    )
    mixed_sum = jnp.sum(out_partials.astype(jnp.bfloat16).astype(jnp.float32), axis=0)
    branch = mixed_sum + b_out
    feature_t = jnp.transpose(feature, (1, 2, 0)).reshape(pixel_count, channel_count)
    result_t = (feature_t.astype(jnp.float32) + layer_scale * branch).astype(jnp.bfloat16)
    result = jnp.transpose(result_t.reshape(tile_rows, tile_cols, channel_count), (2, 0, 1))
    cotangent_t = jnp.transpose(cotangent, (1, 2, 0))
    grad_out = cotangent_t.reshape(pixel_count, channel_count).astype(jnp.float32)
    g_branch = grad_out * layer_scale
    grad_layer_scale = jnp.sum(grad_out * branch, axis=0)
    grad_b_out = jnp.sum(g_branch, axis=0)
    g_out = g_branch.astype(jnp.bfloat16)
    d_pre = contract(g_out, w_out_all, 1, 1) * gelu_slope
    g_pre = d_pre.astype(jnp.bfloat16)
    hidden_own = lax.dynamic_slice_in_dim(hidden, own * share, share, axis=1)
    g_pre_own = lax.dynamic_slice_in_dim(g_pre, own * share, share, axis=1)
    d_pre_own = lax.dynamic_slice_in_dim(d_pre, own * share, share, axis=1)
    grad_w_out = contract(hidden_own, g_out, 0, 0)
    grad_b_in = jnp.sum(d_pre_own, axis=0)
    grad_w_in = contract(normalized_output, g_pre_own, 0, 0)
    dn_partials = lax.dot_general(
        g_pre.reshape(pixel_count, blocks, share),
        w_in_all.reshape(channel_count, blocks, share),
        (((2,), (2,)), ((1,), (1,))),
        preferred_element_type=jnp.float32,
    )
    normalized_gradient = jnp.sum(dn_partials.astype(jnp.bfloat16).astype(jnp.float32), axis=0)
    standardized_gradient = normalized_gradient * norm_gain
    initial_mean = jnp.mean(standardized_gradient, axis=1, keepdims=True)
    product_mean = jnp.mean(standardized_gradient * standardized_input, axis=1, keepdims=True)
    convolved_gradient = inverse_deviation * (
        standardized_gradient - initial_mean - standardized_input * product_mean
    )
    gain_portion = jnp.sum(normalized_gradient * standardized_input, axis=0)
    bias_portion = jnp.sum(normalized_gradient, axis=0)
    grad_conv_bias = jnp.sum(convolved_gradient, axis=0)
    d_t = convolved_gradient.reshape(tile_rows, tile_cols, channel_count)
    grad_kernel = kernel_grad_minor(d_t, padded_t)
    (
        grad_kernel,
        grad_conv_bias,
        gain_portion,
        bias_portion,
        grad_w_in,
        grad_b_in,
        grad_w_out,
        grad_b_out,
        grad_layer_scale,
    ) = butterfly_sum(
        (
            grad_kernel,
            grad_conv_bias,
            gain_portion,
            bias_portion,
            grad_w_in,
            grad_b_in,
            grad_w_out,
            grad_b_out,
            grad_layer_scale,
        ),
        ("row", "col"),
    )
    d_padded = extended(d_t.astype(jnp.bfloat16), (("row", 0), ("col", 1)), 3).astype(jnp.float32)
    grad_feature_t = (
        cotangent_t.astype(jnp.float32) + depthwise_minor(d_padded, kernel[::-1, ::-1])
    ).astype(jnp.bfloat16)
    grad_feature = jnp.transpose(grad_feature_t, (2, 0, 1))
    return (
        result,
        grad_feature,
        grad_kernel * norm_factor,
        grad_conv_bias * norm_factor,
        gain_portion * norm_factor,
        bias_portion * norm_factor,
        grad_w_in * norm_factor,
        grad_b_in * norm_factor,
        grad_w_out * norm_factor,
        grad_b_out * norm_factor,
        grad_layer_scale * norm_factor,
    )


def solution(mesh):
    return jax.shard_map(
        shards,
        mesh=mesh,
        in_specs=(
            P(None, "row", "col"),
            P(),
            P(),
            P(),
            P(),
            P(None, "chan"),
            P("chan"),
            P("chan", None),
            P(),
            P(),
            P(None, "row", "col"),
        ),
        out_specs=(
            P(None, "row", "col"),
            P(None, "row", "col"),
            P(),
            P(),
            P(),
            P(),
            P(None, "chan"),
            P("chan"),
            P("chan", None),
            P(),
            P(),
        ),
        check_vma=False,
    )
```

```python
import jax
import jax.numpy as jnp
from jax import lax
from jax.experimental import pallas as pl
from jax.sharding import PartitionSpec as P


def extended(x, sides, width):
    for axis, dim in sides:
        devices, length = (lax.axis_size(axis), x.shape[dim])
        up = [(i, (i + 1) % devices) for i in range(devices - 1)]
        down = [(j, i) for i, j in up]
        last = lax.slice_in_dim(x, length - width, length, axis=dim)
        leading = lax.slice_in_dim(x, 0, width, axis=dim)
        if devices == 2:
            first = lax.axis_index(axis) == 0
            got = lax.ppermute(jnp.where(first, last, leading), axis, [(0, 1), (1, 0)])
            nothing = jnp.zeros_like(got)
            before = jnp.where(first, nothing, got)
            after = jnp.where(first, got, nothing)
        else:
            before = lax.ppermute(last, axis, up)
            after = lax.ppermute(leading, axis, down)
        x = jnp.concatenate([before, x, after], axis=dim)
    return x


def shortened(x):
    return jax.tree.map(lambda a: a.astype(jnp.bfloat16) if a.dtype == jnp.float32 else a, x)


def depthwise(padded, kernel):
    channel_count = padded.shape[0]
    return lax.conv_general_dilated(
        padded[None],
        kernel[:, :, None, :],
        (1, 1),
        "VALID",
        dimension_numbers=("NCHW", "HWIO", "NCHW"),
        feature_group_count=channel_count,
        precision=lax.Precision.HIGHEST,
    )[0]


def gelu_parts(pre_act):
    cdf_val = 0.5 * (1.0 + lax.erf(pre_act * 0.7071067811865476))
    density = jnp.exp(-0.5 * pre_act * pre_act) * 0.3989422804014327
    return (pre_act * cdf_val, cdf_val + pre_act * density)


def contract(left, right, dim_left, dim_right):
    return lax.dot_general(
        left, right, (((dim_left,), (dim_right,)), ((), ())), preferred_element_type=jnp.float32
    )


def layer_norm_forward(conv_flat, norm_gain, norm_bias):
    mean_val = jnp.mean(conv_flat, axis=0)
    centered_values = conv_flat - mean_val
    variance = jnp.mean(centered_values * centered_values, axis=0)
    inverse_deviation = lax.rsqrt(variance + 1e-06)
    standardized_input = centered_values * inverse_deviation
    normalized_output = (standardized_input * norm_gain[:, None] + norm_bias[:, None]).astype(
        jnp.bfloat16
    )
    return (standardized_input, inverse_deviation, normalized_output)


def layer_norm_backward(normalized_gradient, standardized_input, inverse_deviation, norm_gain):
    standardized_gradient = normalized_gradient * norm_gain[:, None]
    initial_mean = jnp.mean(standardized_gradient, axis=0)
    product_mean = jnp.mean(standardized_gradient * standardized_input, axis=0)
    convolved_gradient = inverse_deviation * (
        standardized_gradient - initial_mean - standardized_input * product_mean
    )
    return (
        convolved_gradient,
        jnp.sum(normalized_gradient * standardized_input, axis=1),
        jnp.sum(normalized_gradient, axis=1),
    )


def kernel_grad_body(d_ref, p_ref, o_ref):
    rows, cols, _ = d_ref.shape
    taps = o_ref.shape[0]
    side = int(round(taps ** 0.5))
    o_ref[...] = jnp.zeros(o_ref.shape, o_ref.dtype)

    def row_step(h, carry):
        d_row = d_ref[h]
        for i in range(side):
            for j in range(side):
                prod = d_row * p_ref[h + i, j : j + cols, :]
                part = jnp.sum(prod.reshape(cols // 8, 8, prod.shape[-1]), axis=0)
                o_ref[i * side + j] += part
        return carry

    lax.fori_loop(0, rows, row_step, 0)


def kernel_grad_minor(d_t, p_t):
    side = p_t.shape[0] - d_t.shape[0] + 1
    channel_count = d_t.shape[-1]
    partial = pl.pallas_call(
        kernel_grad_body,
        out_shape=jax.ShapeDtypeStruct((side * side, 8, channel_count), jnp.float32),
    )(d_t, p_t)
    return jnp.sum(partial, axis=1).reshape(side, side, channel_count)


def flat_pack(values):
    return jnp.concatenate([v.reshape(-1) for v in values])


def flat_unpack(flat, values):
    out = []
    offset = 0
    for v in values:
        out.append(flat[offset : offset + v.size].reshape(v.shape))
        offset += v.size
    return out


def butterfly_steps(axes):
    steps = []
    for axis in axes:
        devices = lax.axis_size(axis)
        if devices & (devices - 1):
            steps.append((axis, 0))
            continue
        step = 1
        while step < devices:
            steps.append((axis, step))
            step *= 2
    return steps


def butterfly_step(flat, axis, step):
    if step == 0:
        return lax.psum(flat, axis)
    devices = lax.axis_size(axis)
    return flat + lax.ppermute(flat, axis, [(i, i ^ step) for i in range(devices)])


def butterfly_sum(values, axes):
    flat = flat_pack(values)
    first = butterfly_steps(axes[:1])
    order_a = first + butterfly_steps(axes[1:])[::-1]
    order_b = order_a[len(first) :] + order_a[: len(first)]
    half = flat.shape[0] // 2
    part_a, part_b = flat[:half], flat[half:]
    for step_a, step_b in zip(order_a, order_b):
        part_a, part_b = butterfly_step(part_a, *step_a), butterfly_step(part_b, *step_b)
    return flat_unpack(jnp.concatenate([part_a, part_b]), values)


def gathered_weights(w_in, b_in, w_out):
    channel_count = w_in.shape[0]
    pieces = []
    rest = b_in
    for _ in range(3):
        piece = rest.astype(jnp.bfloat16)
        rest = rest - piece.astype(jnp.float32)
        pieces.append(piece[:, None])
    packed = jnp.concatenate([w_in.T, w_out] + pieces, axis=1)
    devices = lax.axis_size("chan")
    own = lax.axis_index("chan")
    received = [packed] + [
        lax.ppermute(packed, "chan", [(i, (i + shift) % devices) for i in range(devices)])
        for shift in range(1, devices)
    ]
    order = (own - jnp.arange(devices)) % devices
    full = jnp.stack(received)[order].reshape(devices * packed.shape[0], packed.shape[1])
    w_in_all = full[:, :channel_count].T
    w_out_all = full[:, channel_count : 2 * channel_count]
    parts = full[:, 2 * channel_count :].astype(jnp.float32)
    b_in_all = (parts[:, 0] + parts[:, 1]) + parts[:, 2]
    return w_in_all, b_in_all, w_out_all


def depthwise_minor(padded_t, kernel):
    channel_count = padded_t.shape[-1]
    return lax.conv_general_dilated(
        padded_t[None],
        kernel[:, :, None, :],
        (1, 1),
        "VALID",
        dimension_numbers=("NHWC", "HWIO", "NHWC"),
        feature_group_count=channel_count,
        precision=lax.Precision.HIGHEST,
    )[0]


def shards(
    feature,
    kernel,
    conv_bias,
    norm_gain,
    norm_bias,
    w_in,
    b_in,
    w_out,
    b_out,
    layer_scale,
    cotangent,
):
    channel_count, tile_rows, tile_cols = feature.shape
    pixel_count = tile_rows * tile_cols
    blocks = lax.axis_size("chan")
    share = w_in.shape[1]
    own = lax.axis_index("chan")
    w_in_all, b_in_all, w_out_all = gathered_weights(w_in, b_in, w_out)
    padded_bf = extended(feature, (("row", 1), ("col", 2)), 3)
    padded_t = jnp.transpose(padded_bf, (1, 2, 0)).astype(jnp.float32)
    total_pixels = pixel_count * lax.axis_size("row") * lax.axis_size("col")
    norm_factor = 1.0 / jnp.sqrt(jnp.float32(total_pixels))
    conv_flat = (depthwise_minor(padded_t, kernel) + conv_bias).reshape(pixel_count, channel_count)
    mean_val = jnp.mean(conv_flat, axis=1, keepdims=True)
    centered_values = conv_flat - mean_val
    variance = jnp.mean(centered_values * centered_values, axis=1, keepdims=True)
    inverse_deviation = lax.rsqrt(variance + 1e-06)
    standardized_input = centered_values * inverse_deviation
    normalized_output = (standardized_input * norm_gain + norm_bias).astype(jnp.bfloat16)
    pre_act = contract(normalized_output, w_in_all, 1, 0) + b_in_all
    gelu_val, gelu_slope = gelu_parts(pre_act)
    hidden = gelu_val.astype(jnp.bfloat16)
    out_partials = lax.dot_general(
        hidden.reshape(pixel_count, blocks, share),
        w_out_all.reshape(blocks, share, channel_count),
        (((2,), (1,)), ((1,), (0,))),
        preferred_element_type=jnp.float32,
    )
    mixed_sum = jnp.sum(out_partials.astype(jnp.bfloat16).astype(jnp.float32), axis=0)
    branch = mixed_sum + b_out
    feature_t = jnp.transpose(feature, (1, 2, 0)).reshape(pixel_count, channel_count)
    result_t = (feature_t.astype(jnp.float32) + layer_scale * branch).astype(jnp.bfloat16)
    result = jnp.transpose(result_t.reshape(tile_rows, tile_cols, channel_count), (2, 0, 1))
    cotangent_t = jnp.transpose(cotangent, (1, 2, 0))
    grad_out = cotangent_t.reshape(pixel_count, channel_count).astype(jnp.float32)
    g_branch = grad_out * layer_scale
    grad_layer_scale = jnp.sum(grad_out * branch, axis=0)
    grad_b_out = jnp.sum(g_branch, axis=0)
    g_out = g_branch.astype(jnp.bfloat16)
    d_pre = contract(g_out, w_out_all, 1, 1) * gelu_slope
    g_pre = d_pre.astype(jnp.bfloat16)
    hidden_own = lax.dynamic_slice_in_dim(hidden, own * share, share, axis=1)
    g_pre_own = lax.dynamic_slice_in_dim(g_pre, own * share, share, axis=1)
    d_pre_own = lax.dynamic_slice_in_dim(d_pre, own * share, share, axis=1)
    grad_w_out = contract(hidden_own, g_out, 0, 0)
    grad_b_in = jnp.sum(d_pre_own, axis=0)
    grad_w_in = contract(normalized_output, g_pre_own, 0, 0)
    dn_partials = lax.dot_general(
        g_pre.reshape(pixel_count, blocks, share),
        w_in_all.reshape(channel_count, blocks, share),
        (((2,), (2,)), ((1,), (1,))),
        preferred_element_type=jnp.float32,
    )
    normalized_gradient = jnp.sum(dn_partials.astype(jnp.bfloat16).astype(jnp.float32), axis=0)
    standardized_gradient = normalized_gradient * norm_gain
    initial_mean = jnp.mean(standardized_gradient, axis=1, keepdims=True)
    product_mean = jnp.mean(standardized_gradient * standardized_input, axis=1, keepdims=True)
    convolved_gradient = inverse_deviation * (
        standardized_gradient - initial_mean - standardized_input * product_mean
    )
    gain_portion = jnp.sum(normalized_gradient * standardized_input, axis=0)
    bias_portion = jnp.sum(normalized_gradient, axis=0)
    grad_conv_bias = jnp.sum(convolved_gradient, axis=0)
    d_t = convolved_gradient.reshape(tile_rows, tile_cols, channel_count)
    grad_kernel = kernel_grad_minor(d_t, padded_t)
    (
        grad_kernel,
        grad_conv_bias,
        gain_portion,
        bias_portion,
        grad_w_in,
        grad_b_in,
        grad_w_out,
        grad_b_out,
        grad_layer_scale,
    ) = butterfly_sum(
        (
            grad_kernel,
            grad_conv_bias,
            gain_portion,
            bias_portion,
            grad_w_in,
            grad_b_in,
            grad_w_out,
            grad_b_out,
            grad_layer_scale,
        ),
        ("row", "col"),
    )
    d_padded = extended(d_t.astype(jnp.bfloat16), (("row", 0), ("col", 1)), 3).astype(jnp.float32)
    grad_feature_t = (
        cotangent_t.astype(jnp.float32) + depthwise_minor(d_padded, kernel[::-1, ::-1])
    ).astype(jnp.bfloat16)
    grad_feature = jnp.transpose(grad_feature_t, (2, 0, 1))
    return (
        result,
        grad_feature,
        grad_kernel * norm_factor,
        grad_conv_bias * norm_factor,
        gain_portion * norm_factor,
        bias_portion * norm_factor,
        grad_w_in * norm_factor,
        grad_b_in * norm_factor,
        grad_w_out * norm_factor,
        grad_b_out * norm_factor,
        grad_layer_scale * norm_factor,
    )


def solution(mesh):
    return jax.shard_map(
        shards,
        mesh=mesh,
        in_specs=(
            P(None, "row", "col"),
            P(),
            P(),
            P(),
            P(),
            P(None, "chan"),
            P("chan"),
            P("chan", None),
            P(),
            P(),
            P(None, "row", "col"),
        ),
        out_specs=(
            P(None, "row", "col"),
            P(None, "row", "col"),
            P(),
            P(),
            P(),
            P(),
            P(None, "chan"),
            P("chan"),
            P("chan", None),
            P(),
            P(),
        ),
        check_vma=False,
    )
```

```python
import jax
import jax.numpy as jnp
from jax import lax
from jax.experimental import pallas as pl
from jax.experimental.pallas import tpu as pltpu
from jax.sharding import PartitionSpec as P


def extended(x, sides, width):
    for axis, dim in sides:
        devices, length = (lax.axis_size(axis), x.shape[dim])
        up = [(i, (i + 1) % devices) for i in range(devices - 1)]
        down = [(j, i) for i, j in up]
        last = lax.slice_in_dim(x, length - width, length, axis=dim)
        leading = lax.slice_in_dim(x, 0, width, axis=dim)
        if devices == 2:
            first = lax.axis_index(axis) == 0
            got = lax.ppermute(jnp.where(first, last, leading), axis, [(0, 1), (1, 0)])
            nothing = jnp.zeros_like(got)
            before = jnp.where(first, nothing, got)
            after = jnp.where(first, got, nothing)
        else:
            before = lax.ppermute(last, axis, up)
            after = lax.ppermute(leading, axis, down)
        x = jnp.concatenate([before, x, after], axis=dim)
    return x


def shortened(x):
    return jax.tree.map(lambda a: a.astype(jnp.bfloat16) if a.dtype == jnp.float32 else a, x)


def depthwise(padded, kernel):
    channel_count = padded.shape[0]
    return lax.conv_general_dilated(
        padded[None],
        kernel[:, :, None, :],
        (1, 1),
        "VALID",
        dimension_numbers=("NCHW", "HWIO", "NCHW"),
        feature_group_count=channel_count,
        precision=lax.Precision.HIGHEST,
    )[0]


def gelu_parts(pre_act):
    cdf_val = 0.5 * (1.0 + lax.erf(pre_act * 0.7071067811865476))
    density = jnp.exp(-0.5 * pre_act * pre_act) * 0.3989422804014327
    return (pre_act * cdf_val, cdf_val + pre_act * density)


def contract(left, right, dim_left, dim_right):
    return lax.dot_general(
        left, right, (((dim_left,), (dim_right,)), ((), ())), preferred_element_type=jnp.float32
    )


def layer_norm_forward(conv_flat, norm_gain, norm_bias):
    mean_val = jnp.mean(conv_flat, axis=0)
    centered_values = conv_flat - mean_val
    variance = jnp.mean(centered_values * centered_values, axis=0)
    inverse_deviation = lax.rsqrt(variance + 1e-06)
    standardized_input = centered_values * inverse_deviation
    normalized_output = (standardized_input * norm_gain[:, None] + norm_bias[:, None]).astype(
        jnp.bfloat16
    )
    return (standardized_input, inverse_deviation, normalized_output)


def layer_norm_backward(normalized_gradient, standardized_input, inverse_deviation, norm_gain):
    standardized_gradient = normalized_gradient * norm_gain[:, None]
    initial_mean = jnp.mean(standardized_gradient, axis=0)
    product_mean = jnp.mean(standardized_gradient * standardized_input, axis=0)
    convolved_gradient = inverse_deviation * (
        standardized_gradient - initial_mean - standardized_input * product_mean
    )
    return (
        convolved_gradient,
        jnp.sum(normalized_gradient * standardized_input, axis=1),
        jnp.sum(normalized_gradient, axis=1),
    )


def kernel_grad_body(d_ref, p_ref, o_ref, shifted_ref):
    rows, cols, _ = d_ref.shape
    taps = o_ref.shape[0]
    side = int(round(taps ** 0.5))
    o_ref[...] = jnp.zeros(o_ref.shape, o_ref.dtype)
    for j in range(side):
        shifted_ref[j] = p_ref[:, j : j + cols, :]

    def row_step(h, carry):
        d_row = d_ref[h]
        for i in range(side):
            for j in range(side):
                prod = d_row * shifted_ref[j, h + i]
                part = jnp.sum(prod.reshape(cols // 8, 8, prod.shape[-1]), axis=0)
                o_ref[i * side + j] += part
        return carry

    lax.fori_loop(0, rows, row_step, 0)


def kernel_grad_minor(d_t, p_t):
    side = p_t.shape[0] - d_t.shape[0] + 1
    channel_count = d_t.shape[-1]
    partial = pl.pallas_call(
        kernel_grad_body,
        out_shape=jax.ShapeDtypeStruct((side * side, 8, channel_count), jnp.float32),
        scratch_shapes=[pltpu.VMEM((side,) + p_t.shape[:1] + d_t.shape[1:], jnp.float32)],
    )(d_t, p_t)
    return jnp.sum(partial, axis=1).reshape(side, side, channel_count)


def flat_pack(values):
    return jnp.concatenate([v.reshape(-1) for v in values])


def flat_unpack(flat, values):
    out = []
    offset = 0
    for v in values:
        out.append(flat[offset : offset + v.size].reshape(v.shape))
        offset += v.size
    return out


def butterfly_steps(axes):
    steps = []
    for axis in axes:
        devices = lax.axis_size(axis)
        if devices & (devices - 1):
            steps.append((axis, 0))
            continue
        step = 1
        while step < devices:
            steps.append((axis, step))
            step *= 2
    return steps


def butterfly_step(flat, axis, step):
    if step == 0:
        return lax.psum(flat, axis)
    devices = lax.axis_size(axis)
    return flat + lax.ppermute(flat, axis, [(i, i ^ step) for i in range(devices)])


def butterfly_sum(values, axes):
    flat = flat_pack(values)
    first = butterfly_steps(axes[:1])
    order_a = first + butterfly_steps(axes[1:])[::-1]
    order_b = order_a[len(first) :] + order_a[: len(first)]
    half = flat.shape[0] // 2
    part_a, part_b = flat[:half], flat[half:]
    for step_a, step_b in zip(order_a, order_b):
        part_a, part_b = butterfly_step(part_a, *step_a), butterfly_step(part_b, *step_b)
    return flat_unpack(jnp.concatenate([part_a, part_b]), values)


def gathered_weights(w_in, b_in, w_out):
    channel_count = w_in.shape[0]
    pieces = []
    rest = b_in
    for _ in range(3):
        piece = rest.astype(jnp.bfloat16)
        rest = rest - piece.astype(jnp.float32)
        pieces.append(piece[:, None])
    packed = jnp.concatenate([w_in.T, w_out] + pieces, axis=1)
    full = lax.all_gather(packed, "chan", axis=0, tiled=True)
    w_in_all = full[:, :channel_count].T
    w_out_all = full[:, channel_count : 2 * channel_count]
    parts = full[:, 2 * channel_count :].astype(jnp.float32)
    b_in_all = (parts[:, 0] + parts[:, 1]) + parts[:, 2]
    return w_in_all, b_in_all, w_out_all


def depthwise_minor(padded_t, kernel):
    channel_count = padded_t.shape[-1]
    return lax.conv_general_dilated(
        padded_t[None],
        kernel[:, :, None, :],
        (1, 1),
        "VALID",
        dimension_numbers=("NHWC", "HWIO", "NHWC"),
        feature_group_count=channel_count,
        precision=lax.Precision.HIGHEST,
    )[0]


def shards(
    feature,
    kernel,
    conv_bias,
    norm_gain,
    norm_bias,
    w_in,
    b_in,
    w_out,
    b_out,
    layer_scale,
    cotangent,
):
    channel_count, tile_rows, tile_cols = feature.shape
    pixel_count = tile_rows * tile_cols
    blocks = lax.axis_size("chan")
    share = w_in.shape[1]
    own = lax.axis_index("chan")
    w_in_all, b_in_all, w_out_all = gathered_weights(w_in, b_in, w_out)
    padded_bf = extended(feature, (("row", 1), ("col", 2)), 3)
    padded_t = jnp.transpose(padded_bf, (1, 2, 0)).astype(jnp.float32)
    total_pixels = pixel_count * lax.axis_size("row") * lax.axis_size("col")
    norm_factor = 1.0 / jnp.sqrt(jnp.float32(total_pixels))
    conv_flat = (depthwise_minor(padded_t, kernel) + conv_bias).reshape(pixel_count, channel_count)
    mean_val = jnp.mean(conv_flat, axis=1, keepdims=True)
    centered_values = conv_flat - mean_val
    variance = jnp.mean(centered_values * centered_values, axis=1, keepdims=True)
    inverse_deviation = lax.rsqrt(variance + 1e-06)
    standardized_input = centered_values * inverse_deviation
    normalized_output = (standardized_input * norm_gain + norm_bias).astype(jnp.bfloat16)
    pre_act = contract(normalized_output, w_in_all, 1, 0) + b_in_all
    gelu_val, gelu_slope = gelu_parts(pre_act)
    hidden = gelu_val.astype(jnp.bfloat16)
    out_partials = lax.dot_general(
        hidden.reshape(pixel_count, blocks, share),
        w_out_all.reshape(blocks, share, channel_count),
        (((2,), (1,)), ((1,), (0,))),
        preferred_element_type=jnp.float32,
    )
    mixed_sum = jnp.sum(out_partials.astype(jnp.bfloat16).astype(jnp.float32), axis=0)
    branch = mixed_sum + b_out
    feature_t = jnp.transpose(feature, (1, 2, 0)).reshape(pixel_count, channel_count)
    result_t = (feature_t.astype(jnp.float32) + layer_scale * branch).astype(jnp.bfloat16)
    result = jnp.transpose(result_t.reshape(tile_rows, tile_cols, channel_count), (2, 0, 1))
    cotangent_t = jnp.transpose(cotangent, (1, 2, 0))
    grad_out = cotangent_t.reshape(pixel_count, channel_count).astype(jnp.float32)
    g_branch = grad_out * layer_scale
    grad_layer_scale = jnp.sum(grad_out * branch, axis=0)
    grad_b_out = jnp.sum(g_branch, axis=0)
    g_out = g_branch.astype(jnp.bfloat16)
    d_pre = contract(g_out, w_out_all, 1, 1) * gelu_slope
    g_pre = d_pre.astype(jnp.bfloat16)
    hidden_own = lax.dynamic_slice_in_dim(hidden, own * share, share, axis=1)
    g_pre_own = lax.dynamic_slice_in_dim(g_pre, own * share, share, axis=1)
    d_pre_own = lax.dynamic_slice_in_dim(d_pre, own * share, share, axis=1)
    grad_w_out = contract(hidden_own, g_out, 0, 0)
    grad_b_in = jnp.sum(d_pre_own, axis=0)
    grad_w_in = contract(normalized_output, g_pre_own, 0, 0)
    dn_partials = lax.dot_general(
        g_pre.reshape(pixel_count, blocks, share),
        w_in_all.reshape(channel_count, blocks, share),
        (((2,), (2,)), ((1,), (1,))),
        preferred_element_type=jnp.float32,
    )
    normalized_gradient = jnp.sum(dn_partials.astype(jnp.bfloat16).astype(jnp.float32), axis=0)
    standardized_gradient = normalized_gradient * norm_gain
    initial_mean = jnp.mean(standardized_gradient, axis=1, keepdims=True)
    product_mean = jnp.mean(standardized_gradient * standardized_input, axis=1, keepdims=True)
    convolved_gradient = inverse_deviation * (
        standardized_gradient - initial_mean - standardized_input * product_mean
    )
    gain_portion = jnp.sum(normalized_gradient * standardized_input, axis=0)
    bias_portion = jnp.sum(normalized_gradient, axis=0)
    grad_conv_bias = jnp.sum(convolved_gradient, axis=0)
    d_t = convolved_gradient.reshape(tile_rows, tile_cols, channel_count)
    grad_kernel = kernel_grad_minor(d_t, padded_t)
    (
        grad_kernel,
        grad_conv_bias,
        gain_portion,
        bias_portion,
        grad_w_in,
        grad_b_in,
        grad_w_out,
        grad_b_out,
        grad_layer_scale,
    ) = butterfly_sum(
        (
            grad_kernel,
            grad_conv_bias,
            gain_portion,
            bias_portion,
            grad_w_in,
            grad_b_in,
            grad_w_out,
            grad_b_out,
            grad_layer_scale,
        ),
        ("row", "col"),
    )
    d_padded = extended(d_t.astype(jnp.bfloat16), (("row", 0), ("col", 1)), 3).astype(jnp.float32)
    grad_feature_t = (
        cotangent_t.astype(jnp.float32) + depthwise_minor(d_padded, kernel[::-1, ::-1])
    ).astype(jnp.bfloat16)
    grad_feature = jnp.transpose(grad_feature_t, (2, 0, 1))
    return (
        result,
        grad_feature,
        grad_kernel * norm_factor,
        grad_conv_bias * norm_factor,
        gain_portion * norm_factor,
        bias_portion * norm_factor,
        grad_w_in * norm_factor,
        grad_b_in * norm_factor,
        grad_w_out * norm_factor,
        grad_b_out * norm_factor,
        grad_layer_scale * norm_factor,
    )


def solution(mesh):
    return jax.shard_map(
        shards,
        mesh=mesh,
        in_specs=(
            P(None, "row", "col"),
            P(),
            P(),
            P(),
            P(),
            P(None, "chan"),
            P("chan"),
            P("chan", None),
            P(),
            P(),
            P(None, "row", "col"),
        ),
        out_specs=(
            P(None, "row", "col"),
            P(None, "row", "col"),
            P(),
            P(),
            P(),
            P(),
            P(None, "chan"),
            P("chan"),
            P("chan", None),
            P(),
            P(),
        ),
        check_vma=False,
    )
```

```python
import jax
import jax.numpy as jnp
from jax import lax
from jax.experimental import pallas as pl
from jax.experimental.pallas import tpu as pltpu
from jax.sharding import PartitionSpec as P


def extended(x, sides, width):
    for axis, dim in sides:
        devices, length = (lax.axis_size(axis), x.shape[dim])
        up = [(i, (i + 1) % devices) for i in range(devices - 1)]
        down = [(j, i) for i, j in up]
        last = lax.slice_in_dim(x, length - width, length, axis=dim)
        leading = lax.slice_in_dim(x, 0, width, axis=dim)
        if devices == 2:
            first = lax.axis_index(axis) == 0
            got = lax.ppermute(jnp.where(first, last, leading), axis, [(0, 1), (1, 0)])
            nothing = jnp.zeros_like(got)
            before = jnp.where(first, nothing, got)
            after = jnp.where(first, got, nothing)
        else:
            before = lax.ppermute(last, axis, up)
            after = lax.ppermute(leading, axis, down)
        x = jnp.concatenate([before, x, after], axis=dim)
    return x


def shortened(x):
    return jax.tree.map(lambda a: a.astype(jnp.bfloat16) if a.dtype == jnp.float32 else a, x)


def depthwise(padded, kernel):
    channel_count = padded.shape[0]
    return lax.conv_general_dilated(
        padded[None],
        kernel[:, :, None, :],
        (1, 1),
        "VALID",
        dimension_numbers=("NCHW", "HWIO", "NCHW"),
        feature_group_count=channel_count,
        precision=lax.Precision.HIGHEST,
    )[0]


def gelu_parts(pre_act):
    cdf_val = 0.5 * (1.0 + lax.erf(pre_act * 0.7071067811865476))
    density = jnp.exp(-0.5 * pre_act * pre_act) * 0.3989422804014327
    return (pre_act * cdf_val, cdf_val + pre_act * density)


def contract(left, right, dim_left, dim_right):
    return lax.dot_general(
        left, right, (((dim_left,), (dim_right,)), ((), ())), preferred_element_type=jnp.float32
    )


def layer_norm_forward(conv_flat, norm_gain, norm_bias):
    mean_val = jnp.mean(conv_flat, axis=0)
    centered_values = conv_flat - mean_val
    variance = jnp.mean(centered_values * centered_values, axis=0)
    inverse_deviation = lax.rsqrt(variance + 1e-06)
    standardized_input = centered_values * inverse_deviation
    normalized_output = (standardized_input * norm_gain[:, None] + norm_bias[:, None]).astype(
        jnp.bfloat16
    )
    return (standardized_input, inverse_deviation, normalized_output)


def layer_norm_backward(normalized_gradient, standardized_input, inverse_deviation, norm_gain):
    standardized_gradient = normalized_gradient * norm_gain[:, None]
    initial_mean = jnp.mean(standardized_gradient, axis=0)
    product_mean = jnp.mean(standardized_gradient * standardized_input, axis=0)
    convolved_gradient = inverse_deviation * (
        standardized_gradient - initial_mean - standardized_input * product_mean
    )
    return (
        convolved_gradient,
        jnp.sum(normalized_gradient * standardized_input, axis=1),
        jnp.sum(normalized_gradient, axis=1),
    )


def kernel_grad_body(d_ref, p_ref, o_ref, shifted_ref):
    rows, cols, _ = d_ref.shape
    taps = o_ref.shape[0]
    side = int(round(taps ** 0.5))
    o_ref[...] = jnp.zeros(o_ref.shape, o_ref.dtype)
    for j in range(side):
        shifted_ref[j] = p_ref[:, j : j + cols, :]

    def row_step(h, carry):
        d_row = d_ref[h]
        for i in range(side):
            for j in range(side):
                prod = d_row * shifted_ref[j, h + i]
                part = jnp.sum(prod.reshape(cols // 8, 8, prod.shape[-1]), axis=0)
                o_ref[i * side + j] += part
        return carry

    lax.fori_loop(0, rows, row_step, 0)


def kernel_grad_minor(d_t, p_t):
    side = p_t.shape[0] - d_t.shape[0] + 1
    channel_count = d_t.shape[-1]
    partial = pl.pallas_call(
        kernel_grad_body,
        out_shape=jax.ShapeDtypeStruct((side * side, 8, channel_count), jnp.float32),
        scratch_shapes=[pltpu.VMEM((side,) + p_t.shape[:1] + d_t.shape[1:], jnp.float32)],
    )(d_t, p_t)
    return jnp.sum(partial, axis=1).reshape(side, side, channel_count)


def flat_pack(values):
    return jnp.concatenate([v.reshape(-1) for v in values])


def flat_unpack(flat, values):
    out = []
    offset = 0
    for v in values:
        out.append(flat[offset : offset + v.size].reshape(v.shape))
        offset += v.size
    return out


def butterfly_steps(axes):
    steps = []
    for axis in axes:
        devices = lax.axis_size(axis)
        if devices & (devices - 1):
            steps.append((axis, 0))
            continue
        step = 1
        while step < devices:
            steps.append((axis, step))
            step *= 2
    return steps


def butterfly_step(flat, axis, step):
    if step == 0:
        return lax.psum(flat, axis)
    devices = lax.axis_size(axis)
    return flat + lax.ppermute(flat, axis, [(i, i ^ step) for i in range(devices)])


def butterfly_sum(values, axes):
    flat = flat_pack(values)
    steps = butterfly_steps(axes[:1]) + butterfly_steps(axes[1:])[::-1]
    count = min(3, len(steps))
    size = -(-flat.shape[0] // count)
    parts = [flat[p * size : (p + 1) * size] for p in range(count)]
    orders = [steps[p * len(steps) // count :] + steps[: p * len(steps) // count] for p in range(count)]
    for stage in range(len(steps)):
        parts = [butterfly_step(part, *order[stage]) for part, order in zip(parts, orders)]
    return flat_unpack(jnp.concatenate(parts), values)


def gathered_weights(w_in, b_in, w_out):
    channel_count = w_in.shape[0]
    pieces = []
    rest = b_in
    for _ in range(3):
        piece = rest.astype(jnp.bfloat16)
        rest = rest - piece.astype(jnp.float32)
        pieces.append(piece[:, None])
    packed = jnp.concatenate([w_in.T, w_out] + pieces, axis=1)
    full = lax.all_gather(packed, "chan", axis=0, tiled=True)
    w_in_all = full[:, :channel_count].T
    w_out_all = full[:, channel_count : 2 * channel_count]
    parts = full[:, 2 * channel_count :].astype(jnp.float32)
    b_in_all = (parts[:, 0] + parts[:, 1]) + parts[:, 2]
    return w_in_all, b_in_all, w_out_all


def depthwise_minor(padded_t, kernel):
    channel_count = padded_t.shape[-1]
    return lax.conv_general_dilated(
        padded_t[None],
        kernel[:, :, None, :],
        (1, 1),
        "VALID",
        dimension_numbers=("NHWC", "HWIO", "NHWC"),
        feature_group_count=channel_count,
        precision=lax.Precision.HIGHEST,
    )[0]


def shards(
    feature,
    kernel,
    conv_bias,
    norm_gain,
    norm_bias,
    w_in,
    b_in,
    w_out,
    b_out,
    layer_scale,
    cotangent,
):
    channel_count, tile_rows, tile_cols = feature.shape
    pixel_count = tile_rows * tile_cols
    blocks = lax.axis_size("chan")
    share = w_in.shape[1]
    own = lax.axis_index("chan")
    w_in_all, b_in_all, w_out_all = gathered_weights(w_in, b_in, w_out)
    padded_bf = extended(feature, (("row", 1), ("col", 2)), 3)
    padded_t = jnp.transpose(padded_bf, (1, 2, 0)).astype(jnp.float32)
    total_pixels = pixel_count * lax.axis_size("row") * lax.axis_size("col")
    norm_factor = 1.0 / jnp.sqrt(jnp.float32(total_pixels))
    conv_flat = (depthwise_minor(padded_t, kernel) + conv_bias).reshape(pixel_count, channel_count)
    mean_val = jnp.mean(conv_flat, axis=1, keepdims=True)
    centered_values = conv_flat - mean_val
    variance = jnp.mean(centered_values * centered_values, axis=1, keepdims=True)
    inverse_deviation = lax.rsqrt(variance + 1e-06)
    standardized_input = centered_values * inverse_deviation
    normalized_output = (standardized_input * norm_gain + norm_bias).astype(jnp.bfloat16)
    pre_act = contract(normalized_output, w_in_all, 1, 0) + b_in_all
    gelu_val, gelu_slope = gelu_parts(pre_act)
    hidden = gelu_val.astype(jnp.bfloat16)
    out_partials = lax.dot_general(
        hidden.reshape(pixel_count, blocks, share),
        w_out_all.reshape(blocks, share, channel_count),
        (((2,), (1,)), ((1,), (0,))),
        preferred_element_type=jnp.float32,
    )
    mixed_sum = jnp.sum(out_partials.astype(jnp.bfloat16).astype(jnp.float32), axis=0)
    branch = mixed_sum + b_out
    feature_t = jnp.transpose(feature, (1, 2, 0)).reshape(pixel_count, channel_count)
    result_t = (feature_t.astype(jnp.float32) + layer_scale * branch).astype(jnp.bfloat16)
    result = jnp.transpose(result_t.reshape(tile_rows, tile_cols, channel_count), (2, 0, 1))
    cotangent_t = jnp.transpose(cotangent, (1, 2, 0))
    grad_out = cotangent_t.reshape(pixel_count, channel_count).astype(jnp.float32)
    g_branch = grad_out * layer_scale
    grad_layer_scale = jnp.sum(grad_out * branch, axis=0)
    grad_b_out = jnp.sum(g_branch, axis=0)
    g_out = g_branch.astype(jnp.bfloat16)
    d_pre = contract(g_out, w_out_all, 1, 1) * gelu_slope
    g_pre = d_pre.astype(jnp.bfloat16)
    hidden_own = lax.dynamic_slice_in_dim(hidden, own * share, share, axis=1)
    g_pre_own = lax.dynamic_slice_in_dim(g_pre, own * share, share, axis=1)
    d_pre_own = lax.dynamic_slice_in_dim(d_pre, own * share, share, axis=1)
    grad_w_out = contract(hidden_own, g_out, 0, 0)
    grad_b_in = jnp.sum(d_pre_own, axis=0)
    grad_w_in = contract(normalized_output, g_pre_own, 0, 0)
    dn_partials = lax.dot_general(
        g_pre.reshape(pixel_count, blocks, share),
        w_in_all.reshape(channel_count, blocks, share),
        (((2,), (2,)), ((1,), (1,))),
        preferred_element_type=jnp.float32,
    )
    normalized_gradient = jnp.sum(dn_partials.astype(jnp.bfloat16).astype(jnp.float32), axis=0)
    standardized_gradient = normalized_gradient * norm_gain
    initial_mean = jnp.mean(standardized_gradient, axis=1, keepdims=True)
    product_mean = jnp.mean(standardized_gradient * standardized_input, axis=1, keepdims=True)
    convolved_gradient = inverse_deviation * (
        standardized_gradient - initial_mean - standardized_input * product_mean
    )
    gain_portion = jnp.sum(normalized_gradient * standardized_input, axis=0)
    bias_portion = jnp.sum(normalized_gradient, axis=0)
    grad_conv_bias = jnp.sum(convolved_gradient, axis=0)
    d_t = convolved_gradient.reshape(tile_rows, tile_cols, channel_count)
    grad_kernel = kernel_grad_minor(d_t, padded_t)
    (
        grad_kernel,
        grad_conv_bias,
        gain_portion,
        bias_portion,
        grad_w_in,
        grad_b_in,
        grad_w_out,
        grad_b_out,
        grad_layer_scale,
    ) = butterfly_sum(
        (
            grad_kernel,
            grad_conv_bias,
            gain_portion,
            bias_portion,
            grad_w_in,
            grad_b_in,
            grad_w_out,
            grad_b_out,
            grad_layer_scale,
        ),
        ("row", "col"),
    )
    d_padded = extended(d_t.astype(jnp.bfloat16), (("row", 0), ("col", 1)), 3).astype(jnp.float32)
    grad_feature_t = (
        cotangent_t.astype(jnp.float32) + depthwise_minor(d_padded, kernel[::-1, ::-1])
    ).astype(jnp.bfloat16)
    grad_feature = jnp.transpose(grad_feature_t, (2, 0, 1))
    return (
        result,
        grad_feature,
        grad_kernel * norm_factor,
        grad_conv_bias * norm_factor,
        gain_portion * norm_factor,
        bias_portion * norm_factor,
        grad_w_in * norm_factor,
        grad_b_in * norm_factor,
        grad_w_out * norm_factor,
        grad_b_out * norm_factor,
        grad_layer_scale * norm_factor,
    )


def solution(mesh):
    return jax.shard_map(
        shards,
        mesh=mesh,
        in_specs=(
            P(None, "row", "col"),
            P(),
            P(),
            P(),
            P(),
            P(None, "chan"),
            P("chan"),
            P("chan", None),
            P(),
            P(),
            P(None, "row", "col"),
        ),
        out_specs=(
            P(None, "row", "col"),
            P(None, "row", "col"),
            P(),
            P(),
            P(),
            P(),
            P(None, "chan"),
            P("chan"),
            P("chan", None),
            P(),
            P(),
        ),
        check_vma=False,
    )
```

```python
import jax
import jax.numpy as jnp
from jax import lax
from jax.experimental import pallas as pl
from jax.experimental.pallas import tpu as pltpu
from jax.sharding import PartitionSpec as P


def extended(x, sides, width):
    for axis, dim in sides:
        devices, length = (lax.axis_size(axis), x.shape[dim])
        up = [(i, (i + 1) % devices) for i in range(devices - 1)]
        down = [(j, i) for i, j in up]
        last = lax.slice_in_dim(x, length - width, length, axis=dim)
        leading = lax.slice_in_dim(x, 0, width, axis=dim)
        if devices == 2:
            first = lax.axis_index(axis) == 0
            got = lax.ppermute(jnp.where(first, last, leading), axis, [(0, 1), (1, 0)])
            nothing = jnp.zeros_like(got)
            before = jnp.where(first, nothing, got)
            after = jnp.where(first, got, nothing)
        else:
            before = lax.ppermute(last, axis, up)
            after = lax.ppermute(leading, axis, down)
        x = jnp.concatenate([before, x, after], axis=dim)
    return x


def shortened(x):
    return jax.tree.map(lambda a: a.astype(jnp.bfloat16) if a.dtype == jnp.float32 else a, x)


def depthwise(padded, kernel):
    channel_count = padded.shape[0]
    return lax.conv_general_dilated(
        padded[None],
        kernel[:, :, None, :],
        (1, 1),
        "VALID",
        dimension_numbers=("NCHW", "HWIO", "NCHW"),
        feature_group_count=channel_count,
        precision=lax.Precision.HIGHEST,
    )[0]


def gelu_parts(pre_act):
    cdf_val = 0.5 * (1.0 + lax.erf(pre_act * 0.7071067811865476))
    density = jnp.exp(-0.5 * pre_act * pre_act) * 0.3989422804014327
    return (pre_act * cdf_val, cdf_val + pre_act * density)


def contract(left, right, dim_left, dim_right):
    return lax.dot_general(
        left, right, (((dim_left,), (dim_right,)), ((), ())), preferred_element_type=jnp.float32
    )


def layer_norm_forward(conv_flat, norm_gain, norm_bias):
    mean_val = jnp.mean(conv_flat, axis=0)
    centered_values = conv_flat - mean_val
    variance = jnp.mean(centered_values * centered_values, axis=0)
    inverse_deviation = lax.rsqrt(variance + 1e-06)
    standardized_input = centered_values * inverse_deviation
    normalized_output = (standardized_input * norm_gain[:, None] + norm_bias[:, None]).astype(
        jnp.bfloat16
    )
    return (standardized_input, inverse_deviation, normalized_output)


def layer_norm_backward(normalized_gradient, standardized_input, inverse_deviation, norm_gain):
    standardized_gradient = normalized_gradient * norm_gain[:, None]
    initial_mean = jnp.mean(standardized_gradient, axis=0)
    product_mean = jnp.mean(standardized_gradient * standardized_input, axis=0)
    convolved_gradient = inverse_deviation * (
        standardized_gradient - initial_mean - standardized_input * product_mean
    )
    return (
        convolved_gradient,
        jnp.sum(normalized_gradient * standardized_input, axis=1),
        jnp.sum(normalized_gradient, axis=1),
    )


def kernel_grad_body(d_ref, p_ref, o_ref, shifted_ref):
    rows, cols, _ = d_ref.shape
    taps = o_ref.shape[0]
    side = int(round(taps ** 0.5))
    o_ref[...] = jnp.zeros(o_ref.shape, o_ref.dtype)
    for j in range(side):
        shifted_ref[j] = p_ref[:, j : j + cols, :]

    def row_step(h, carry):
        d_row = d_ref[h]
        for i in range(side):
            for j in range(side):
                prod = d_row * shifted_ref[j, h + i]
                part = jnp.sum(prod.reshape(cols // 8, 8, prod.shape[-1]), axis=0)
                o_ref[i * side + j] += part
        return carry

    lax.fori_loop(0, rows, row_step, 0)


def kernel_grad_minor(d_t, p_t):
    side = p_t.shape[0] - d_t.shape[0] + 1
    channel_count = d_t.shape[-1]
    partial = pl.pallas_call(
        kernel_grad_body,
        out_shape=jax.ShapeDtypeStruct((side * side, 8, channel_count), jnp.float32),
        scratch_shapes=[pltpu.VMEM((side,) + p_t.shape[:1] + d_t.shape[1:], jnp.float32)],
    )(d_t, p_t)
    return jnp.sum(partial, axis=1).reshape(side, side, channel_count)


def flat_pack(values):
    return jnp.concatenate([v.reshape(-1) for v in values])


def flat_unpack(flat, values):
    out = []
    offset = 0
    for v in values:
        out.append(flat[offset : offset + v.size].reshape(v.shape))
        offset += v.size
    return out


def butterfly_steps(axes):
    steps = []
    for axis in axes:
        devices = lax.axis_size(axis)
        if devices & (devices - 1):
            steps.append((axis, 0))
            continue
        step = 1
        while step < devices:
            steps.append((axis, step))
            step *= 2
    return steps


def butterfly_step(flat, axis, step):
    if step == 0:
        return lax.psum(flat, axis)
    devices = lax.axis_size(axis)
    return flat + lax.ppermute(flat, axis, [(i, i ^ step) for i in range(devices)])


def butterfly_sum(values, axes):
    flat = flat_pack(values)
    first = butterfly_steps(axes[:1])
    order_a = first + butterfly_steps(axes[1:])[::-1]
    order_b = order_a[len(first) :] + order_a[: len(first)]
    half = flat.shape[0] // 2
    part_a, part_b = flat[:half], flat[half:]
    for step_a, step_b in zip(order_a, order_b):
        part_a, part_b = butterfly_step(part_a, *step_a), butterfly_step(part_b, *step_b)
    return flat_unpack(jnp.concatenate([part_a, part_b]), values)


def gathered_weights(w_in, b_in, w_out):
    channel_count = w_in.shape[0]
    pieces = []
    rest = b_in
    for _ in range(3):
        piece = rest.astype(jnp.bfloat16)
        rest = rest - piece.astype(jnp.float32)
        pieces.append(piece[:, None])
    packed = jnp.concatenate([w_in.T, w_out] + pieces, axis=1)
    full = lax.all_gather(packed, "chan", axis=0, tiled=True)
    w_in_all = full[:, :channel_count].T
    w_out_all = full[:, channel_count : 2 * channel_count]
    parts = full[:, 2 * channel_count :].astype(jnp.float32)
    b_in_all = (parts[:, 0] + parts[:, 1]) + parts[:, 2]
    return w_in_all, b_in_all, w_out_all


def depthwise_minor(padded_t, kernel):
    channel_count = padded_t.shape[-1]
    return lax.conv_general_dilated(
        padded_t[None],
        kernel[:, :, None, :],
        (1, 1),
        "VALID",
        dimension_numbers=("NHWC", "HWIO", "NHWC"),
        feature_group_count=channel_count,
        precision=lax.Precision.HIGHEST,
    )[0]


def shards(
    feature,
    kernel,
    conv_bias,
    norm_gain,
    norm_bias,
    w_in,
    b_in,
    w_out,
    b_out,
    layer_scale,
    cotangent,
):
    channel_count, tile_rows, tile_cols = feature.shape
    pixel_count = tile_rows * tile_cols
    blocks = lax.axis_size("chan")
    share = w_in.shape[1]
    own = lax.axis_index("chan")
    w_in_all, b_in_all, w_out_all = gathered_weights(w_in, b_in, w_out)
    padded_bf = extended(feature, (("row", 1), ("col", 2)), 3)
    padded_t = jnp.transpose(padded_bf, (1, 2, 0)).astype(jnp.float32)
    total_pixels = pixel_count * lax.axis_size("row") * lax.axis_size("col")
    norm_factor = 1.0 / jnp.sqrt(jnp.float32(total_pixels))
    conv_flat = (depthwise_minor(padded_t, kernel) + conv_bias).reshape(pixel_count, channel_count)
    mean_val = jnp.mean(conv_flat, axis=1, keepdims=True)
    centered_values = conv_flat - mean_val
    variance = jnp.mean(centered_values * centered_values, axis=1, keepdims=True)
    inverse_deviation = lax.rsqrt(variance + 1e-06)
    standardized_input = centered_values * inverse_deviation
    normalized_output = (standardized_input * norm_gain + norm_bias).astype(jnp.bfloat16)
    pre_act = contract(normalized_output, w_in_all, 1, 0) + b_in_all
    gelu_val, gelu_slope = gelu_parts(pre_act)
    hidden = gelu_val.astype(jnp.bfloat16)
    out_partials = lax.dot_general(
        hidden.reshape(pixel_count, blocks, share),
        w_out_all.reshape(blocks, share, channel_count),
        (((2,), (1,)), ((1,), (0,))),
        preferred_element_type=jnp.float32,
    )
    mixed_sum = jnp.sum(out_partials.astype(jnp.bfloat16).astype(jnp.float32), axis=0)
    branch = mixed_sum + b_out
    feature_t = jnp.transpose(feature, (1, 2, 0)).reshape(pixel_count, channel_count)
    result_t = (feature_t.astype(jnp.float32) + layer_scale * branch).astype(jnp.bfloat16)
    result = jnp.transpose(result_t.reshape(tile_rows, tile_cols, channel_count), (2, 0, 1))
    cotangent_t = jnp.transpose(cotangent, (1, 2, 0))
    grad_out = cotangent_t.reshape(pixel_count, channel_count).astype(jnp.float32)
    g_branch = grad_out * layer_scale
    grad_layer_scale = jnp.sum(grad_out * branch, axis=0)
    grad_b_out = jnp.sum(g_branch, axis=0)
    g_out = g_branch.astype(jnp.bfloat16)
    d_pre = contract(g_out, w_out_all, 1, 1) * gelu_slope
    g_pre = d_pre.astype(jnp.bfloat16)
    hidden_own = lax.dynamic_slice_in_dim(hidden, own * share, share, axis=1)
    g_pre_own = lax.dynamic_slice_in_dim(g_pre, own * share, share, axis=1)
    d_pre_own = lax.dynamic_slice_in_dim(d_pre, own * share, share, axis=1)
    grad_w_out = contract(hidden_own, g_out, 0, 0)
    grad_b_in = jnp.sum(d_pre_own, axis=0)
    grad_w_in = contract(normalized_output, g_pre_own, 0, 0)
    dn_partials = lax.dot_general(
        g_pre.reshape(pixel_count, blocks, share),
        w_in_all.reshape(channel_count, blocks, share),
        (((2,), (2,)), ((1,), (1,))),
        preferred_element_type=jnp.float32,
    )
    normalized_gradient = jnp.sum(dn_partials.astype(jnp.bfloat16).astype(jnp.float32), axis=0)
    standardized_gradient = normalized_gradient * norm_gain
    initial_mean = jnp.mean(standardized_gradient, axis=1, keepdims=True)
    product_mean = jnp.mean(standardized_gradient * standardized_input, axis=1, keepdims=True)
    convolved_gradient = inverse_deviation * (
        standardized_gradient - initial_mean - standardized_input * product_mean
    )
    gain_portion = jnp.sum(normalized_gradient * standardized_input, axis=0)
    bias_portion = jnp.sum(normalized_gradient, axis=0)
    grad_conv_bias = jnp.sum(convolved_gradient, axis=0)
    d_t = convolved_gradient.reshape(tile_rows, tile_cols, channel_count)
    grad_kernel = kernel_grad_minor(d_t, padded_t)
    d_rows = extended(d_t.astype(jnp.bfloat16), (("row", 0),), 3)
    grad_kernel, d_rows = lax.optimization_barrier((grad_kernel, d_rows))
    d_padded = extended(d_rows, (("col", 1),), 3).astype(jnp.float32)
    (
        grad_kernel,
        grad_conv_bias,
        gain_portion,
        bias_portion,
        grad_w_in,
        grad_b_in,
        grad_w_out,
        grad_b_out,
        grad_layer_scale,
    ) = butterfly_sum(
        (
            grad_kernel,
            grad_conv_bias,
            gain_portion,
            bias_portion,
            grad_w_in,
            grad_b_in,
            grad_w_out,
            grad_b_out,
            grad_layer_scale,
        ),
        ("row", "col"),
    )
    grad_feature_t = (
        cotangent_t.astype(jnp.float32) + depthwise_minor(d_padded, kernel[::-1, ::-1])
    ).astype(jnp.bfloat16)
    grad_feature = jnp.transpose(grad_feature_t, (2, 0, 1))
    return (
        result,
        grad_feature,
        grad_kernel * norm_factor,
        grad_conv_bias * norm_factor,
        gain_portion * norm_factor,
        bias_portion * norm_factor,
        grad_w_in * norm_factor,
        grad_b_in * norm_factor,
        grad_w_out * norm_factor,
        grad_b_out * norm_factor,
        grad_layer_scale * norm_factor,
    )


def solution(mesh):
    return jax.shard_map(
        shards,
        mesh=mesh,
        in_specs=(
            P(None, "row", "col"),
            P(),
            P(),
            P(),
            P(),
            P(None, "chan"),
            P("chan"),
            P("chan", None),
            P(),
            P(),
            P(None, "row", "col"),
        ),
        out_specs=(
            P(None, "row", "col"),
            P(None, "row", "col"),
            P(),
            P(),
            P(),
            P(),
            P(None, "chan"),
            P("chan"),
            P("chan", None),
            P(),
            P(),
        ),
        check_vma=False,
    )
```

```python
import jax
import jax.numpy as jnp
from jax import lax
from jax.experimental import pallas as pl
from jax.experimental.pallas import tpu as pltpu
from jax.sharding import PartitionSpec as P


def extended(x, sides, width):
    for axis, dim in sides:
        devices, length = (lax.axis_size(axis), x.shape[dim])
        up = [(i, (i + 1) % devices) for i in range(devices - 1)]
        down = [(j, i) for i, j in up]
        last = lax.slice_in_dim(x, length - width, length, axis=dim)
        leading = lax.slice_in_dim(x, 0, width, axis=dim)
        if devices == 2:
            first = lax.axis_index(axis) == 0
            got = lax.ppermute(jnp.where(first, last, leading), axis, [(0, 1), (1, 0)])
            nothing = jnp.zeros_like(got)
            before = jnp.where(first, nothing, got)
            after = jnp.where(first, got, nothing)
        else:
            before = lax.ppermute(last, axis, up)
            after = lax.ppermute(leading, axis, down)
        x = jnp.concatenate([before, x, after], axis=dim)
    return x


def shortened(x):
    return jax.tree.map(lambda a: a.astype(jnp.bfloat16) if a.dtype == jnp.float32 else a, x)


def depthwise(padded, kernel):
    channel_count = padded.shape[0]
    return lax.conv_general_dilated(
        padded[None],
        kernel[:, :, None, :],
        (1, 1),
        "VALID",
        dimension_numbers=("NCHW", "HWIO", "NCHW"),
        feature_group_count=channel_count,
        precision=lax.Precision.HIGHEST,
    )[0]


def gelu_parts(pre_act):
    cdf_val = 0.5 * (1.0 + lax.erf(pre_act * 0.7071067811865476))
    density = jnp.exp(-0.5 * pre_act * pre_act) * 0.3989422804014327
    return (pre_act * cdf_val, cdf_val + pre_act * density)


def contract(left, right, dim_left, dim_right):
    return lax.dot_general(
        left, right, (((dim_left,), (dim_right,)), ((), ())), preferred_element_type=jnp.float32
    )


def layer_norm_forward(conv_flat, norm_gain, norm_bias):
    mean_val = jnp.mean(conv_flat, axis=0)
    centered_values = conv_flat - mean_val
    variance = jnp.mean(centered_values * centered_values, axis=0)
    inverse_deviation = lax.rsqrt(variance + 1e-06)
    standardized_input = centered_values * inverse_deviation
    normalized_output = (standardized_input * norm_gain[:, None] + norm_bias[:, None]).astype(
        jnp.bfloat16
    )
    return (standardized_input, inverse_deviation, normalized_output)


def layer_norm_backward(normalized_gradient, standardized_input, inverse_deviation, norm_gain):
    standardized_gradient = normalized_gradient * norm_gain[:, None]
    initial_mean = jnp.mean(standardized_gradient, axis=0)
    product_mean = jnp.mean(standardized_gradient * standardized_input, axis=0)
    convolved_gradient = inverse_deviation * (
        standardized_gradient - initial_mean - standardized_input * product_mean
    )
    return (
        convolved_gradient,
        jnp.sum(normalized_gradient * standardized_input, axis=1),
        jnp.sum(normalized_gradient, axis=1),
    )


def kernel_grad_body(d_ref, p_ref, o_ref, shifted_ref):
    rows, cols, _ = d_ref.shape
    taps = o_ref.shape[0]
    side = int(round(taps ** 0.5))
    o_ref[...] = jnp.zeros(o_ref.shape, o_ref.dtype)
    for j in range(side):
        shifted_ref[j] = p_ref[:, j : j + cols, :]

    def row_step(h, carry):
        d_row = d_ref[h]
        for i in range(side):
            for j in range(side):
                prod = d_row * shifted_ref[j, h + i]
                part = jnp.sum(prod.reshape(cols // 8, 8, prod.shape[-1]), axis=0)
                o_ref[i * side + j] += part
        return carry

    lax.fori_loop(0, rows, row_step, 0)


def kernel_grad_minor(d_t, p_t):
    side = p_t.shape[0] - d_t.shape[0] + 1
    channel_count = d_t.shape[-1]
    partial = pl.pallas_call(
        kernel_grad_body,
        out_shape=jax.ShapeDtypeStruct((side * side, 8, channel_count), jnp.float32),
        scratch_shapes=[pltpu.VMEM((side,) + p_t.shape[:1] + d_t.shape[1:], jnp.float32)],
    )(d_t, p_t)
    return jnp.sum(partial, axis=1).reshape(side, side, channel_count)


def flat_pack(values):
    return jnp.concatenate([v.reshape(-1) for v in values])


def flat_unpack(flat, values):
    out = []
    offset = 0
    for v in values:
        out.append(flat[offset : offset + v.size].reshape(v.shape))
        offset += v.size
    return out


def butterfly_steps(axes):
    steps = []
    for axis in axes:
        devices = lax.axis_size(axis)
        if devices & (devices - 1):
            steps.append((axis, 0))
            continue
        step = 1
        while step < devices:
            steps.append((axis, step))
            step *= 2
    return steps


def butterfly_step(flat, axis, step):
    if step == 0:
        return lax.psum(flat, axis)
    devices = lax.axis_size(axis)
    return flat + lax.ppermute(flat, axis, [(i, i ^ step) for i in range(devices)])


def butterfly_sum(values, axes):
    flat = flat_pack(values)
    first = butterfly_steps(axes[:1])
    order_a = first + butterfly_steps(axes[1:])[::-1]
    order_b = order_a[len(first) :] + order_a[: len(first)]
    half = flat.shape[0] // 2
    part_a, part_b = flat[:half], flat[half:]
    for step_a, step_b in zip(order_a, order_b):
        part_a, part_b = butterfly_step(part_a, *step_a), butterfly_step(part_b, *step_b)
    return flat_unpack(jnp.concatenate([part_a, part_b]), values)


def gathered_weights(w_in, b_in, w_out):
    channel_count = w_in.shape[0]
    pieces = []
    rest = b_in
    for _ in range(3):
        piece = rest.astype(jnp.bfloat16)
        rest = rest - piece.astype(jnp.float32)
        pieces.append(piece[:, None])
    packed = jnp.concatenate([w_in.T, w_out] + pieces, axis=1)
    full = lax.all_gather(packed, "chan", axis=0, tiled=True)
    w_in_all = full[:, :channel_count].T
    w_out_all = full[:, channel_count : 2 * channel_count]
    parts = full[:, 2 * channel_count :].astype(jnp.float32)
    b_in_all = (parts[:, 0] + parts[:, 1]) + parts[:, 2]
    return w_in_all, b_in_all, w_out_all


def depthwise_minor(padded_t, kernel):
    channel_count = padded_t.shape[-1]
    return lax.conv_general_dilated(
        padded_t[None],
        kernel[:, :, None, :],
        (1, 1),
        "VALID",
        dimension_numbers=("NHWC", "HWIO", "NHWC"),
        feature_group_count=channel_count,
        precision=lax.Precision.HIGHEST,
    )[0]


def shards(
    feature,
    kernel,
    conv_bias,
    norm_gain,
    norm_bias,
    w_in,
    b_in,
    w_out,
    b_out,
    layer_scale,
    cotangent,
):
    channel_count, tile_rows, tile_cols = feature.shape
    pixel_count = tile_rows * tile_cols
    blocks = lax.axis_size("chan")
    share = w_in.shape[1]
    own = lax.axis_index("chan")
    w_in_all, b_in_all, w_out_all = gathered_weights(w_in, b_in, w_out)
    padded_bf = extended(feature, (("row", 1), ("col", 2)), 3)
    padded_t = jnp.transpose(padded_bf, (1, 2, 0)).astype(jnp.float32)
    total_pixels = pixel_count * lax.axis_size("row") * lax.axis_size("col")
    norm_factor = 1.0 / jnp.sqrt(jnp.float32(total_pixels))
    conv_flat = (depthwise_minor(padded_t, kernel) + conv_bias).reshape(pixel_count, channel_count)
    mean_val = jnp.mean(conv_flat, axis=1, keepdims=True)
    centered_values = conv_flat - mean_val
    variance = jnp.mean(centered_values * centered_values, axis=1, keepdims=True)
    inverse_deviation = lax.rsqrt(variance + 1e-06)
    standardized_input = centered_values * inverse_deviation
    normalized_output = (standardized_input * norm_gain + norm_bias).astype(jnp.bfloat16)
    pre_act = contract(normalized_output, w_in_all, 1, 0) + b_in_all
    gelu_val, gelu_slope = gelu_parts(pre_act)
    hidden = gelu_val.astype(jnp.bfloat16)
    out_partials = lax.dot_general(
        hidden.reshape(pixel_count, blocks, share),
        w_out_all.reshape(blocks, share, channel_count),
        (((2,), (1,)), ((1,), (0,))),
        preferred_element_type=jnp.float32,
    )
    mixed_sum = jnp.sum(out_partials.astype(jnp.bfloat16).astype(jnp.float32), axis=0)
    branch = mixed_sum + b_out
    feature_t = jnp.transpose(feature, (1, 2, 0)).reshape(pixel_count, channel_count)
    result_t = (feature_t.astype(jnp.float32) + layer_scale * branch).astype(jnp.bfloat16)
    result = jnp.transpose(result_t.reshape(tile_rows, tile_cols, channel_count), (2, 0, 1))
    cotangent_t = jnp.transpose(cotangent, (1, 2, 0))
    grad_out = cotangent_t.reshape(pixel_count, channel_count).astype(jnp.float32)
    g_branch = grad_out * layer_scale
    grad_layer_scale = jnp.sum(grad_out * branch, axis=0)
    grad_b_out = jnp.sum(g_branch, axis=0)
    g_out = g_branch.astype(jnp.bfloat16)
    grad_layer_scale, grad_b_out, g_out = lax.optimization_barrier((grad_layer_scale, grad_b_out, g_out))
    d_pre = contract(g_out, w_out_all, 1, 1) * gelu_slope
    g_pre = d_pre.astype(jnp.bfloat16)
    hidden_own = lax.dynamic_slice_in_dim(hidden, own * share, share, axis=1)
    g_pre_own = lax.dynamic_slice_in_dim(g_pre, own * share, share, axis=1)
    d_pre_own = lax.dynamic_slice_in_dim(d_pre, own * share, share, axis=1)
    grad_w_out = contract(hidden_own, g_out, 0, 0)
    grad_b_in = jnp.sum(d_pre_own, axis=0)
    grad_w_in = contract(normalized_output, g_pre_own, 0, 0)
    dn_partials = lax.dot_general(
        g_pre.reshape(pixel_count, blocks, share),
        w_in_all.reshape(channel_count, blocks, share),
        (((2,), (2,)), ((1,), (1,))),
        preferred_element_type=jnp.float32,
    )
    normalized_gradient = jnp.sum(dn_partials.astype(jnp.bfloat16).astype(jnp.float32), axis=0)
    standardized_gradient = normalized_gradient * norm_gain
    initial_mean = jnp.mean(standardized_gradient, axis=1, keepdims=True)
    product_mean = jnp.mean(standardized_gradient * standardized_input, axis=1, keepdims=True)
    convolved_gradient = inverse_deviation * (
        standardized_gradient - initial_mean - standardized_input * product_mean
    )
    gain_portion = jnp.sum(normalized_gradient * standardized_input, axis=0)
    bias_portion = jnp.sum(normalized_gradient, axis=0)
    grad_conv_bias = jnp.sum(convolved_gradient, axis=0)
    d_t = convolved_gradient.reshape(tile_rows, tile_cols, channel_count)
    grad_kernel = kernel_grad_minor(d_t, padded_t)
    (
        grad_kernel,
        grad_conv_bias,
        gain_portion,
        bias_portion,
        grad_w_in,
        grad_b_in,
        grad_w_out,
        grad_b_out,
        grad_layer_scale,
    ) = butterfly_sum(
        (
            grad_kernel,
            grad_conv_bias,
            gain_portion,
            bias_portion,
            grad_w_in,
            grad_b_in,
            grad_w_out,
            grad_b_out,
            grad_layer_scale,
        ),
        ("row", "col"),
    )
    d_padded = extended(d_t.astype(jnp.bfloat16), (("row", 0), ("col", 1)), 3).astype(jnp.float32)
    grad_feature_t = (
        cotangent_t.astype(jnp.float32) + depthwise_minor(d_padded, kernel[::-1, ::-1])
    ).astype(jnp.bfloat16)
    grad_feature = jnp.transpose(grad_feature_t, (2, 0, 1))
    return (
        result,
        grad_feature,
        grad_kernel * norm_factor,
        grad_conv_bias * norm_factor,
        gain_portion * norm_factor,
        bias_portion * norm_factor,
        grad_w_in * norm_factor,
        grad_b_in * norm_factor,
        grad_w_out * norm_factor,
        grad_b_out * norm_factor,
        grad_layer_scale * norm_factor,
    )


def solution(mesh):
    return jax.shard_map(
        shards,
        mesh=mesh,
        in_specs=(
            P(None, "row", "col"),
            P(),
            P(),
            P(),
            P(),
            P(None, "chan"),
            P("chan"),
            P("chan", None),
            P(),
            P(),
            P(None, "row", "col"),
        ),
        out_specs=(
            P(None, "row", "col"),
            P(None, "row", "col"),
            P(),
            P(),
            P(),
            P(),
            P(None, "chan"),
            P("chan"),
            P("chan", None),
            P(),
            P(),
        ),
        check_vma=False,
    )
```

```python
import jax
import jax.numpy as jnp
from jax import lax
from jax.experimental import pallas as pl
from jax.experimental.pallas import tpu as pltpu
from jax.sharding import PartitionSpec as P


def extended(x, sides, width):
    for axis, dim in sides:
        devices, length = (lax.axis_size(axis), x.shape[dim])
        up = [(i, (i + 1) % devices) for i in range(devices - 1)]
        down = [(j, i) for i, j in up]
        last = lax.slice_in_dim(x, length - width, length, axis=dim)
        leading = lax.slice_in_dim(x, 0, width, axis=dim)
        if devices == 2:
            first = lax.axis_index(axis) == 0
            got = lax.ppermute(jnp.where(first, last, leading), axis, [(0, 1), (1, 0)])
            nothing = jnp.zeros_like(got)
            before = jnp.where(first, nothing, got)
            after = jnp.where(first, got, nothing)
        else:
            before = lax.ppermute(last, axis, up)
            after = lax.ppermute(leading, axis, down)
        x = jnp.concatenate([before, x, after], axis=dim)
    return x


def shortened(x):
    return jax.tree.map(lambda a: a.astype(jnp.bfloat16) if a.dtype == jnp.float32 else a, x)


def depthwise(padded, kernel):
    channel_count = padded.shape[0]
    return lax.conv_general_dilated(
        padded[None],
        kernel[:, :, None, :],
        (1, 1),
        "VALID",
        dimension_numbers=("NCHW", "HWIO", "NCHW"),
        feature_group_count=channel_count,
        precision=lax.Precision.HIGHEST,
    )[0]


def gelu_parts(pre_act):
    cdf_val = 0.5 * (1.0 + lax.erf(pre_act * 0.7071067811865476))
    density = jnp.exp(-0.5 * pre_act * pre_act) * 0.3989422804014327
    return (pre_act * cdf_val, cdf_val + pre_act * density)


def contract(left, right, dim_left, dim_right):
    return lax.dot_general(
        left, right, (((dim_left,), (dim_right,)), ((), ())), preferred_element_type=jnp.float32
    )


def layer_norm_forward(conv_flat, norm_gain, norm_bias):
    mean_val = jnp.mean(conv_flat, axis=0)
    centered_values = conv_flat - mean_val
    variance = jnp.mean(centered_values * centered_values, axis=0)
    inverse_deviation = lax.rsqrt(variance + 1e-06)
    standardized_input = centered_values * inverse_deviation
    normalized_output = (standardized_input * norm_gain[:, None] + norm_bias[:, None]).astype(
        jnp.bfloat16
    )
    return (standardized_input, inverse_deviation, normalized_output)


def layer_norm_backward(normalized_gradient, standardized_input, inverse_deviation, norm_gain):
    standardized_gradient = normalized_gradient * norm_gain[:, None]
    initial_mean = jnp.mean(standardized_gradient, axis=0)
    product_mean = jnp.mean(standardized_gradient * standardized_input, axis=0)
    convolved_gradient = inverse_deviation * (
        standardized_gradient - initial_mean - standardized_input * product_mean
    )
    return (
        convolved_gradient,
        jnp.sum(normalized_gradient * standardized_input, axis=1),
        jnp.sum(normalized_gradient, axis=1),
    )


def kernel_grad_body(d_ref, p_ref, o_ref, shifted_ref):
    rows, cols, _ = d_ref.shape
    taps = o_ref.shape[0]
    side = int(round(taps ** 0.5))
    o_ref[...] = jnp.zeros(o_ref.shape, o_ref.dtype)
    for j in range(side):
        shifted_ref[j] = p_ref[:, j : j + cols, :]

    def row_step(h, carry):
        d_row = d_ref[h]
        for i in range(side):
            for j in range(side):
                prod = d_row * shifted_ref[j, h + i]
                part = jnp.sum(prod.reshape(cols // 8, 8, prod.shape[-1]), axis=0)
                o_ref[i * side + j] += part
        return carry

    lax.fori_loop(0, rows, row_step, 0)


def kernel_grad_minor(d_t, p_t):
    side = p_t.shape[0] - d_t.shape[0] + 1
    channel_count = d_t.shape[-1]
    partial = pl.pallas_call(
        kernel_grad_body,
        out_shape=jax.ShapeDtypeStruct((side * side, 8, channel_count), jnp.float32),
        scratch_shapes=[pltpu.VMEM((side,) + p_t.shape[:1] + d_t.shape[1:], jnp.float32)],
    )(d_t, p_t)
    return jnp.sum(partial, axis=1).reshape(side, side, channel_count)


def flat_pack(values):
    return jnp.concatenate([v.reshape(-1) for v in values])


def flat_unpack(flat, values):
    out = []
    offset = 0
    for v in values:
        out.append(flat[offset : offset + v.size].reshape(v.shape))
        offset += v.size
    return out


def butterfly_steps(axes):
    steps = []
    for axis in axes:
        devices = lax.axis_size(axis)
        if devices & (devices - 1):
            steps.append((axis, 0))
            continue
        step = 1
        while step < devices:
            steps.append((axis, step))
            step *= 2
    return steps


def butterfly_step(flat, axis, step):
    if step == 0:
        return lax.psum(flat, axis)
    devices = lax.axis_size(axis)
    return flat + lax.ppermute(flat, axis, [(i, i ^ step) for i in range(devices)])


def butterfly_sum(values, axes):
    flat = flat_pack(values)
    first = butterfly_steps(axes[:1])
    order_a = first + butterfly_steps(axes[1:])[::-1]
    order_b = order_a[len(first) :] + order_a[: len(first)]
    half = flat.shape[0] // 2
    part_a, part_b = flat[:half], flat[half:]
    for step_a, step_b in zip(order_a, order_b):
        part_a, part_b = butterfly_step(part_a, *step_a), butterfly_step(part_b, *step_b)
    return flat_unpack(jnp.concatenate([part_a, part_b]), values)


def gathered_weights(w_in, b_in, w_out):
    channel_count = w_in.shape[0]
    pieces = []
    rest = b_in
    for _ in range(3):
        piece = rest.astype(jnp.bfloat16)
        rest = rest - piece.astype(jnp.float32)
        pieces.append(piece[:, None])
    packed = jnp.concatenate([w_in.T, w_out] + pieces, axis=1)
    full = lax.all_gather(packed, "chan", axis=0, tiled=True)
    w_in_all = full[:, :channel_count].T
    w_out_all = full[:, channel_count : 2 * channel_count]
    parts = full[:, 2 * channel_count :].astype(jnp.float32)
    b_in_all = (parts[:, 0] + parts[:, 1]) + parts[:, 2]
    return w_in_all, b_in_all, w_out_all


def depthwise_minor(padded_t, kernel):
    channel_count = padded_t.shape[-1]
    return lax.conv_general_dilated(
        padded_t[None],
        kernel[:, :, None, :],
        (1, 1),
        "VALID",
        dimension_numbers=("NHWC", "HWIO", "NHWC"),
        feature_group_count=channel_count,
        precision=lax.Precision.HIGHEST,
    )[0]


def shards(
    feature,
    kernel,
    conv_bias,
    norm_gain,
    norm_bias,
    w_in,
    b_in,
    w_out,
    b_out,
    layer_scale,
    cotangent,
):
    channel_count, tile_rows, tile_cols = feature.shape
    pixel_count = tile_rows * tile_cols
    blocks = lax.axis_size("chan")
    share = w_in.shape[1]
    own = lax.axis_index("chan")
    w_in_all, b_in_all, w_out_all = gathered_weights(w_in, b_in, w_out)
    padded_bf = extended(feature, (("row", 1), ("col", 2)), 3)
    padded_t = jnp.transpose(padded_bf, (1, 2, 0)).astype(jnp.float32)
    total_pixels = pixel_count * lax.axis_size("row") * lax.axis_size("col")
    norm_factor = 1.0 / jnp.sqrt(jnp.float32(total_pixels))
    conv_flat = (depthwise_minor(padded_t, kernel) + conv_bias).reshape(pixel_count, channel_count)
    mean_val = jnp.mean(conv_flat, axis=1, keepdims=True)
    centered_values = conv_flat - mean_val
    variance = jnp.mean(centered_values * centered_values, axis=1, keepdims=True)
    inverse_deviation = lax.rsqrt(variance + 1e-06)
    standardized_input = centered_values * inverse_deviation
    normalized_output = (standardized_input * norm_gain + norm_bias).astype(jnp.bfloat16)
    pre_act = contract(normalized_output, w_in_all, 1, 0) + b_in_all
    gelu_val, gelu_slope = gelu_parts(pre_act)
    hidden = gelu_val.astype(jnp.bfloat16)
    out_partials = lax.dot_general(
        hidden.reshape(pixel_count, blocks, share),
        w_out_all.reshape(blocks, share, channel_count),
        (((2,), (1,)), ((1,), (0,))),
        preferred_element_type=jnp.float32,
    )
    mixed_sum = jnp.sum(out_partials.astype(jnp.bfloat16).astype(jnp.float32), axis=0)
    branch = mixed_sum + b_out
    feature_t = jnp.transpose(feature, (1, 2, 0)).reshape(pixel_count, channel_count)
    result_t = (feature_t.astype(jnp.float32) + layer_scale * branch).astype(jnp.bfloat16)
    result = jnp.transpose(result_t.reshape(tile_rows, tile_cols, channel_count), (2, 0, 1))
    cotangent_t = jnp.transpose(cotangent, (1, 2, 0))
    grad_out = cotangent_t.reshape(pixel_count, channel_count).astype(jnp.float32)
    g_branch = grad_out * layer_scale
    grad_layer_scale = jnp.sum(grad_out * branch, axis=0)
    grad_b_out = jnp.sum(g_branch, axis=0)
    g_out = g_branch.astype(jnp.bfloat16)
    grad_layer_scale, grad_b_out, g_out = lax.optimization_barrier((grad_layer_scale, grad_b_out, g_out))
    d_pre = contract(g_out, w_out_all, 1, 1) * gelu_slope
    g_pre = d_pre.astype(jnp.bfloat16)
    hidden_own = lax.dynamic_slice_in_dim(hidden, own * share, share, axis=1)
    g_pre_own = lax.dynamic_slice_in_dim(g_pre, own * share, share, axis=1)
    d_pre_own = lax.dynamic_slice_in_dim(d_pre, own * share, share, axis=1)
    grad_w_out = contract(hidden_own, g_out, 0, 0)
    grad_b_in = jnp.sum(d_pre_own, axis=0)
    grad_w_in = contract(normalized_output, g_pre_own, 0, 0)
    dn_partials = lax.dot_general(
        g_pre.reshape(pixel_count, blocks, share),
        w_in_all.reshape(channel_count, blocks, share),
        (((2,), (2,)), ((1,), (1,))),
        preferred_element_type=jnp.float32,
    )
    normalized_gradient = jnp.sum(dn_partials.astype(jnp.bfloat16).astype(jnp.float32), axis=0)
    standardized_gradient = normalized_gradient * norm_gain
    initial_mean = jnp.mean(standardized_gradient, axis=1, keepdims=True)
    product_mean = jnp.mean(standardized_gradient * standardized_input, axis=1, keepdims=True)
    convolved_gradient = inverse_deviation * (
        standardized_gradient - initial_mean - standardized_input * product_mean
    )
    gain_portion = jnp.sum(normalized_gradient * standardized_input, axis=0)
    bias_portion = jnp.sum(normalized_gradient, axis=0)
    grad_conv_bias = jnp.sum(convolved_gradient, axis=0)
    d_t = convolved_gradient.reshape(tile_rows, tile_cols, channel_count)
    grad_kernel = kernel_grad_minor(d_t, padded_t)
    (
        grad_w_in,
        grad_w_out,
        grad_b_in,
        grad_b_out,
        grad_layer_scale,
        grad_kernel,
        grad_conv_bias,
        gain_portion,
        bias_portion,
    ) = butterfly_sum(
        (
            grad_w_in,
            grad_w_out,
            grad_b_in,
            grad_b_out,
            grad_layer_scale,
            grad_kernel,
            grad_conv_bias,
            gain_portion,
            bias_portion,
        ),
        ("row", "col"),
    )
    d_padded = extended(d_t.astype(jnp.bfloat16), (("row", 0), ("col", 1)), 3).astype(jnp.float32)
    grad_feature_t = (
        cotangent_t.astype(jnp.float32) + depthwise_minor(d_padded, kernel[::-1, ::-1])
    ).astype(jnp.bfloat16)
    grad_feature = jnp.transpose(grad_feature_t, (2, 0, 1))
    return (
        result,
        grad_feature,
        grad_kernel * norm_factor,
        grad_conv_bias * norm_factor,
        gain_portion * norm_factor,
        bias_portion * norm_factor,
        grad_w_in * norm_factor,
        grad_b_in * norm_factor,
        grad_w_out * norm_factor,
        grad_b_out * norm_factor,
        grad_layer_scale * norm_factor,
    )


def solution(mesh):
    return jax.shard_map(
        shards,
        mesh=mesh,
        in_specs=(
            P(None, "row", "col"),
            P(),
            P(),
            P(),
            P(),
            P(None, "chan"),
            P("chan"),
            P("chan", None),
            P(),
            P(),
            P(None, "row", "col"),
        ),
        out_specs=(
            P(None, "row", "col"),
            P(None, "row", "col"),
            P(),
            P(),
            P(),
            P(),
            P(None, "chan"),
            P("chan"),
            P("chan", None),
            P(),
            P(),
        ),
        check_vma=False,
    )
```

```python
import jax
import jax.numpy as jnp
from jax import lax
from jax.experimental import pallas as pl
from jax.experimental.pallas import tpu as pltpu
from jax.sharding import PartitionSpec as P


def extended(x, sides, width):
    for axis, dim in sides:
        devices, length = (lax.axis_size(axis), x.shape[dim])
        up = [(i, (i + 1) % devices) for i in range(devices - 1)]
        down = [(j, i) for i, j in up]
        last = lax.slice_in_dim(x, length - width, length, axis=dim)
        leading = lax.slice_in_dim(x, 0, width, axis=dim)
        if devices == 2:
            first = lax.axis_index(axis) == 0
            got = lax.ppermute(jnp.where(first, last, leading), axis, [(0, 1), (1, 0)])
            nothing = jnp.zeros_like(got)
            before = jnp.where(first, nothing, got)
            after = jnp.where(first, got, nothing)
        else:
            before = lax.ppermute(last, axis, up)
            after = lax.ppermute(leading, axis, down)
        x = jnp.concatenate([before, x, after], axis=dim)
    return x


def shortened(x):
    return jax.tree.map(lambda a: a.astype(jnp.bfloat16) if a.dtype == jnp.float32 else a, x)


def depthwise(padded, kernel):
    channel_count = padded.shape[0]
    return lax.conv_general_dilated(
        padded[None],
        kernel[:, :, None, :],
        (1, 1),
        "VALID",
        dimension_numbers=("NCHW", "HWIO", "NCHW"),
        feature_group_count=channel_count,
        precision=lax.Precision.HIGHEST,
    )[0]


def gelu_parts(pre_act):
    cdf_val = 0.5 * (1.0 + lax.erf(pre_act * 0.7071067811865476))
    density = jnp.exp(-0.5 * pre_act * pre_act) * 0.3989422804014327
    return (pre_act * cdf_val, cdf_val + pre_act * density)


def contract(left, right, dim_left, dim_right):
    return lax.dot_general(
        left, right, (((dim_left,), (dim_right,)), ((), ())), preferred_element_type=jnp.float32
    )


def layer_norm_forward(conv_flat, norm_gain, norm_bias):
    mean_val = jnp.mean(conv_flat, axis=0)
    centered_values = conv_flat - mean_val
    variance = jnp.mean(centered_values * centered_values, axis=0)
    inverse_deviation = lax.rsqrt(variance + 1e-06)
    standardized_input = centered_values * inverse_deviation
    normalized_output = (standardized_input * norm_gain[:, None] + norm_bias[:, None]).astype(
        jnp.bfloat16
    )
    return (standardized_input, inverse_deviation, normalized_output)


def layer_norm_backward(normalized_gradient, standardized_input, inverse_deviation, norm_gain):
    standardized_gradient = normalized_gradient * norm_gain[:, None]
    initial_mean = jnp.mean(standardized_gradient, axis=0)
    product_mean = jnp.mean(standardized_gradient * standardized_input, axis=0)
    convolved_gradient = inverse_deviation * (
        standardized_gradient - initial_mean - standardized_input * product_mean
    )
    return (
        convolved_gradient,
        jnp.sum(normalized_gradient * standardized_input, axis=1),
        jnp.sum(normalized_gradient, axis=1),
    )


def kernel_grad_body(d_ref, p_ref, o_ref, shifted_ref, acc_ref):
    rows, cols, _ = d_ref.shape
    taps = o_ref.shape[0]
    side = int(round(taps ** 0.5))
    acc_ref[...] = jnp.zeros(acc_ref.shape, acc_ref.dtype)
    for j in range(side):
        shifted_ref[j] = p_ref[:, j : j + cols, :]

    def row_step(h, carry):
        d_row = d_ref[h]
        for i in range(side):
            for j in range(side):
                prod = d_row * shifted_ref[j, h + i]
                part = jnp.sum(prod.reshape(cols // 8, 8, prod.shape[-1]), axis=0)
                acc_ref[i * side + j] += part
        return carry

    lax.fori_loop(0, rows, row_step, 0)
    o_ref[...] = jnp.sum(acc_ref[...], axis=1)


def kernel_grad_minor(d_t, p_t):
    side = p_t.shape[0] - d_t.shape[0] + 1
    channel_count = d_t.shape[-1]
    summed = pl.pallas_call(
        kernel_grad_body,
        out_shape=jax.ShapeDtypeStruct((side * side, channel_count), jnp.float32),
        scratch_shapes=[
            pltpu.VMEM((side,) + p_t.shape[:1] + d_t.shape[1:], jnp.float32),
            pltpu.VMEM((side * side, 8, channel_count), jnp.float32),
        ],
    )(d_t, p_t)
    return summed.reshape(side, side, channel_count)


def flat_pack(values):
    return jnp.concatenate([v.reshape(-1) for v in values])


def flat_unpack(flat, values):
    out = []
    offset = 0
    for v in values:
        out.append(flat[offset : offset + v.size].reshape(v.shape))
        offset += v.size
    return out


def butterfly_steps(axes):
    steps = []
    for axis in axes:
        devices = lax.axis_size(axis)
        if devices & (devices - 1):
            steps.append((axis, 0))
            continue
        step = 1
        while step < devices:
            steps.append((axis, step))
            step *= 2
    return steps


def butterfly_step(flat, axis, step):
    if step == 0:
        return lax.psum(flat, axis)
    devices = lax.axis_size(axis)
    return flat + lax.ppermute(flat, axis, [(i, i ^ step) for i in range(devices)])


def butterfly_sum(values, axes):
    flat = flat_pack(values)
    first = butterfly_steps(axes[:1])
    order_a = first + butterfly_steps(axes[1:])[::-1]
    order_b = order_a[len(first) :] + order_a[: len(first)]
    half = flat.shape[0] // 2
    part_a, part_b = flat[:half], flat[half:]
    for step_a, step_b in zip(order_a, order_b):
        part_a, part_b = butterfly_step(part_a, *step_a), butterfly_step(part_b, *step_b)
    return flat_unpack(jnp.concatenate([part_a, part_b]), values)


def gathered_weights(w_in, b_in, w_out):
    channel_count = w_in.shape[0]
    pieces = []
    rest = b_in
    for _ in range(3):
        piece = rest.astype(jnp.bfloat16)
        rest = rest - piece.astype(jnp.float32)
        pieces.append(piece[:, None])
    packed = jnp.concatenate([w_in.T, w_out] + pieces, axis=1)
    full = lax.all_gather(packed, "chan", axis=0, tiled=True)
    w_in_all = full[:, :channel_count].T
    w_out_all = full[:, channel_count : 2 * channel_count]
    parts = full[:, 2 * channel_count :].astype(jnp.float32)
    b_in_all = (parts[:, 0] + parts[:, 1]) + parts[:, 2]
    return w_in_all, b_in_all, w_out_all


def depthwise_minor(padded_t, kernel):
    channel_count = padded_t.shape[-1]
    return lax.conv_general_dilated(
        padded_t[None],
        kernel[:, :, None, :],
        (1, 1),
        "VALID",
        dimension_numbers=("NHWC", "HWIO", "NHWC"),
        feature_group_count=channel_count,
        precision=lax.Precision.HIGHEST,
    )[0]


def shards(
    feature,
    kernel,
    conv_bias,
    norm_gain,
    norm_bias,
    w_in,
    b_in,
    w_out,
    b_out,
    layer_scale,
    cotangent,
):
    channel_count, tile_rows, tile_cols = feature.shape
    pixel_count = tile_rows * tile_cols
    blocks = lax.axis_size("chan")
    share = w_in.shape[1]
    own = lax.axis_index("chan")
    w_in_all, b_in_all, w_out_all = gathered_weights(w_in, b_in, w_out)
    padded_bf = extended(feature, (("row", 1), ("col", 2)), 3)
    padded_t = jnp.transpose(padded_bf, (1, 2, 0)).astype(jnp.float32)
    total_pixels = pixel_count * lax.axis_size("row") * lax.axis_size("col")
    norm_factor = 1.0 / jnp.sqrt(jnp.float32(total_pixels))
    conv_flat = (depthwise_minor(padded_t, kernel) + conv_bias).reshape(pixel_count, channel_count)
    mean_val = jnp.mean(conv_flat, axis=1, keepdims=True)
    centered_values = conv_flat - mean_val
    variance = jnp.mean(centered_values * centered_values, axis=1, keepdims=True)
    inverse_deviation = lax.rsqrt(variance + 1e-06)
    standardized_input = centered_values * inverse_deviation
    normalized_output = (standardized_input * norm_gain + norm_bias).astype(jnp.bfloat16)
    pre_act = contract(normalized_output, w_in_all, 1, 0) + b_in_all
    gelu_val, gelu_slope = gelu_parts(pre_act)
    hidden = gelu_val.astype(jnp.bfloat16)
    out_partials = lax.dot_general(
        hidden.reshape(pixel_count, blocks, share),
        w_out_all.reshape(blocks, share, channel_count),
        (((2,), (1,)), ((1,), (0,))),
        preferred_element_type=jnp.float32,
    )
    mixed_sum = jnp.sum(out_partials.astype(jnp.bfloat16).astype(jnp.float32), axis=0)
    branch = mixed_sum + b_out
    feature_t = jnp.transpose(feature, (1, 2, 0)).reshape(pixel_count, channel_count)
    result_t = (feature_t.astype(jnp.float32) + layer_scale * branch).astype(jnp.bfloat16)
    result = jnp.transpose(result_t.reshape(tile_rows, tile_cols, channel_count), (2, 0, 1))
    cotangent_t = jnp.transpose(cotangent, (1, 2, 0))
    grad_out = cotangent_t.reshape(pixel_count, channel_count).astype(jnp.float32)
    g_branch = grad_out * layer_scale
    grad_layer_scale = jnp.sum(grad_out * branch, axis=0)
    grad_b_out = jnp.sum(g_branch, axis=0)
    g_out = g_branch.astype(jnp.bfloat16)
    grad_layer_scale, grad_b_out, g_out = lax.optimization_barrier((grad_layer_scale, grad_b_out, g_out))
    d_pre = contract(g_out, w_out_all, 1, 1) * gelu_slope
    g_pre = d_pre.astype(jnp.bfloat16)
    hidden_own = lax.dynamic_slice_in_dim(hidden, own * share, share, axis=1)
    g_pre_own = lax.dynamic_slice_in_dim(g_pre, own * share, share, axis=1)
    d_pre_own = lax.dynamic_slice_in_dim(d_pre, own * share, share, axis=1)
    grad_w_out = contract(hidden_own, g_out, 0, 0)
    grad_b_in = jnp.sum(d_pre_own, axis=0)
    grad_w_in = contract(normalized_output, g_pre_own, 0, 0)
    dn_partials = lax.dot_general(
        g_pre.reshape(pixel_count, blocks, share),
        w_in_all.reshape(channel_count, blocks, share),
        (((2,), (2,)), ((1,), (1,))),
        preferred_element_type=jnp.float32,
    )
    normalized_gradient = jnp.sum(dn_partials.astype(jnp.bfloat16).astype(jnp.float32), axis=0)
    standardized_gradient = normalized_gradient * norm_gain
    initial_mean = jnp.mean(standardized_gradient, axis=1, keepdims=True)
    product_mean = jnp.mean(standardized_gradient * standardized_input, axis=1, keepdims=True)
    convolved_gradient = inverse_deviation * (
        standardized_gradient - initial_mean - standardized_input * product_mean
    )
    gain_portion = jnp.sum(normalized_gradient * standardized_input, axis=0)
    bias_portion = jnp.sum(normalized_gradient, axis=0)
    grad_conv_bias = jnp.sum(convolved_gradient, axis=0)
    d_t = convolved_gradient.reshape(tile_rows, tile_cols, channel_count)
    grad_kernel = kernel_grad_minor(d_t, padded_t)
    (
        grad_kernel,
        grad_conv_bias,
        gain_portion,
        bias_portion,
        grad_w_in,
        grad_b_in,
        grad_w_out,
        grad_b_out,
        grad_layer_scale,
    ) = butterfly_sum(
        (
            grad_kernel,
            grad_conv_bias,
            gain_portion,
            bias_portion,
            grad_w_in,
            grad_b_in,
            grad_w_out,
            grad_b_out,
            grad_layer_scale,
        ),
        ("row", "col"),
    )
    d_padded = extended(d_t.astype(jnp.bfloat16), (("row", 0), ("col", 1)), 3).astype(jnp.float32)
    grad_feature_t = (
        cotangent_t.astype(jnp.float32) + depthwise_minor(d_padded, kernel[::-1, ::-1])
    ).astype(jnp.bfloat16)
    grad_feature = jnp.transpose(grad_feature_t, (2, 0, 1))
    return (
        result,
        grad_feature,
        grad_kernel * norm_factor,
        grad_conv_bias * norm_factor,
        gain_portion * norm_factor,
        bias_portion * norm_factor,
        grad_w_in * norm_factor,
        grad_b_in * norm_factor,
        grad_w_out * norm_factor,
        grad_b_out * norm_factor,
        grad_layer_scale * norm_factor,
    )


def solution(mesh):
    return jax.shard_map(
        shards,
        mesh=mesh,
        in_specs=(
            P(None, "row", "col"),
            P(),
            P(),
            P(),
            P(),
            P(None, "chan"),
            P("chan"),
            P("chan", None),
            P(),
            P(),
            P(None, "row", "col"),
        ),
        out_specs=(
            P(None, "row", "col"),
            P(None, "row", "col"),
            P(),
            P(),
            P(),
            P(),
            P(None, "chan"),
            P("chan"),
            P("chan", None),
            P(),
            P(),
        ),
        check_vma=False,
    )
```

```python
import jax
import jax.numpy as jnp
from jax import lax
from jax.experimental import pallas as pl
from jax.experimental.pallas import tpu as pltpu
from jax.sharding import PartitionSpec as P


def extended(x, sides, width):
    for axis, dim in sides:
        devices, length = (lax.axis_size(axis), x.shape[dim])
        up = [(i, (i + 1) % devices) for i in range(devices - 1)]
        down = [(j, i) for i, j in up]
        last = lax.slice_in_dim(x, length - width, length, axis=dim)
        leading = lax.slice_in_dim(x, 0, width, axis=dim)
        if devices == 2:
            first = lax.axis_index(axis) == 0
            got = lax.ppermute(jnp.where(first, last, leading), axis, [(0, 1), (1, 0)])
            nothing = jnp.zeros_like(got)
            before = jnp.where(first, nothing, got)
            after = jnp.where(first, got, nothing)
        else:
            before = lax.ppermute(last, axis, up)
            after = lax.ppermute(leading, axis, down)
        x = jnp.concatenate([before, x, after], axis=dim)
    return x


def shortened(x):
    return jax.tree.map(lambda a: a.astype(jnp.bfloat16) if a.dtype == jnp.float32 else a, x)


def depthwise(padded, kernel):
    channel_count = padded.shape[0]
    return lax.conv_general_dilated(
        padded[None],
        kernel[:, :, None, :],
        (1, 1),
        "VALID",
        dimension_numbers=("NCHW", "HWIO", "NCHW"),
        feature_group_count=channel_count,
        precision=lax.Precision.HIGHEST,
    )[0]


def gelu_parts(pre_act):
    cdf_val = 0.5 * (1.0 + lax.erf(pre_act * 0.7071067811865476))
    density = jnp.exp(-0.5 * pre_act * pre_act) * 0.3989422804014327
    return (pre_act * cdf_val, cdf_val + pre_act * density)


def contract(left, right, dim_left, dim_right):
    return lax.dot_general(
        left, right, (((dim_left,), (dim_right,)), ((), ())), preferred_element_type=jnp.float32
    )


def layer_norm_forward(conv_flat, norm_gain, norm_bias):
    mean_val = jnp.mean(conv_flat, axis=0)
    centered_values = conv_flat - mean_val
    variance = jnp.mean(centered_values * centered_values, axis=0)
    inverse_deviation = lax.rsqrt(variance + 1e-06)
    standardized_input = centered_values * inverse_deviation
    normalized_output = (standardized_input * norm_gain[:, None] + norm_bias[:, None]).astype(
        jnp.bfloat16
    )
    return (standardized_input, inverse_deviation, normalized_output)


def layer_norm_backward(normalized_gradient, standardized_input, inverse_deviation, norm_gain):
    standardized_gradient = normalized_gradient * norm_gain[:, None]
    initial_mean = jnp.mean(standardized_gradient, axis=0)
    product_mean = jnp.mean(standardized_gradient * standardized_input, axis=0)
    convolved_gradient = inverse_deviation * (
        standardized_gradient - initial_mean - standardized_input * product_mean
    )
    return (
        convolved_gradient,
        jnp.sum(normalized_gradient * standardized_input, axis=1),
        jnp.sum(normalized_gradient, axis=1),
    )


def kernel_grad_body(d_ref, p_ref, o_ref, shifted_ref):
    rows, cols, _ = d_ref.shape
    taps = o_ref.shape[0]
    side = int(round(taps ** 0.5))
    o_ref[...] = jnp.zeros(o_ref.shape, o_ref.dtype)
    for j in range(side):
        shifted_ref[j] = p_ref[:, j : j + cols, :]

    def row_step(h, carry):
        d_row = d_ref[h]
        for i in range(side):
            for j in range(side):
                prod = d_row * shifted_ref[j, h + i]
                part = jnp.sum(prod.reshape(cols // 8, 8, prod.shape[-1]), axis=0)
                o_ref[i * side + j] += part
        return carry

    lax.fori_loop(0, rows, row_step, 0)


def kernel_grad_minor(d_t, p_t):
    side = p_t.shape[0] - d_t.shape[0] + 1
    channel_count = d_t.shape[-1]
    partial = pl.pallas_call(
        kernel_grad_body,
        out_shape=jax.ShapeDtypeStruct((side * side, 8, channel_count), jnp.float32),
        scratch_shapes=[pltpu.VMEM((side,) + p_t.shape[:1] + d_t.shape[1:], jnp.float32)],
    )(d_t, p_t)
    return jnp.sum(partial, axis=1).reshape(side, side, channel_count)


def flat_pack(values):
    return jnp.concatenate([v.reshape(-1) for v in values])


def flat_unpack(flat, values):
    out = []
    offset = 0
    for v in values:
        out.append(flat[offset : offset + v.size].reshape(v.shape))
        offset += v.size
    return out


def butterfly_steps(axes):
    steps = []
    for axis in axes:
        devices = lax.axis_size(axis)
        if devices & (devices - 1):
            steps.append((axis, 0))
            continue
        step = 1
        while step < devices:
            steps.append((axis, step))
            step *= 2
    return steps


def butterfly_step(flat, axis, step):
    if step == 0:
        return lax.psum(flat, axis)
    devices = lax.axis_size(axis)
    return flat + lax.ppermute(flat, axis, [(i, i ^ step) for i in range(devices)])


def butterfly_sum(values, axes):
    flat = flat_pack(values)
    first = butterfly_steps(axes[:1])
    order_a = first + butterfly_steps(axes[1:])
    order_b = order_a[len(first) :] + order_a[: len(first)]
    half = flat.shape[0] // 2
    part_a, part_b = flat[:half], flat[half:]
    for step_a, step_b in zip(order_a, order_b):
        part_a, part_b = butterfly_step(part_a, *step_a), butterfly_step(part_b, *step_b)
    return flat_unpack(jnp.concatenate([part_a, part_b]), values)


def gathered_weights(w_in, b_in, w_out):
    channel_count = w_in.shape[0]
    pieces = []
    rest = b_in
    for _ in range(3):
        piece = rest.astype(jnp.bfloat16)
        rest = rest - piece.astype(jnp.float32)
        pieces.append(piece[:, None])
    packed = jnp.concatenate([w_in.T, w_out] + pieces, axis=1)
    full = lax.all_gather(packed, "chan", axis=0, tiled=True)
    w_in_all = full[:, :channel_count].T
    w_out_all = full[:, channel_count : 2 * channel_count]
    parts = full[:, 2 * channel_count :].astype(jnp.float32)
    b_in_all = (parts[:, 0] + parts[:, 1]) + parts[:, 2]
    return w_in_all, b_in_all, w_out_all


def depthwise_minor(padded_t, kernel):
    channel_count = padded_t.shape[-1]
    return lax.conv_general_dilated(
        padded_t[None],
        kernel[:, :, None, :],
        (1, 1),
        "VALID",
        dimension_numbers=("NHWC", "HWIO", "NHWC"),
        feature_group_count=channel_count,
        precision=lax.Precision.HIGHEST,
    )[0]


def shards(
    feature,
    kernel,
    conv_bias,
    norm_gain,
    norm_bias,
    w_in,
    b_in,
    w_out,
    b_out,
    layer_scale,
    cotangent,
):
    channel_count, tile_rows, tile_cols = feature.shape
    pixel_count = tile_rows * tile_cols
    blocks = lax.axis_size("chan")
    share = w_in.shape[1]
    own = lax.axis_index("chan")
    w_in_all, b_in_all, w_out_all = gathered_weights(w_in, b_in, w_out)
    padded_bf = extended(feature, (("row", 1), ("col", 2)), 3)
    padded_t = jnp.transpose(padded_bf, (1, 2, 0)).astype(jnp.float32)
    total_pixels = pixel_count * lax.axis_size("row") * lax.axis_size("col")
    norm_factor = 1.0 / jnp.sqrt(jnp.float32(total_pixels))
    conv_flat = (depthwise_minor(padded_t, kernel) + conv_bias).reshape(pixel_count, channel_count)
    mean_val = jnp.mean(conv_flat, axis=1, keepdims=True)
    centered_values = conv_flat - mean_val
    variance = jnp.mean(centered_values * centered_values, axis=1, keepdims=True)
    inverse_deviation = lax.rsqrt(variance + 1e-06)
    standardized_input = centered_values * inverse_deviation
    normalized_output = (standardized_input * norm_gain + norm_bias).astype(jnp.bfloat16)
    pre_act = contract(normalized_output, w_in_all, 1, 0) + b_in_all
    gelu_val, gelu_slope = gelu_parts(pre_act)
    hidden = gelu_val.astype(jnp.bfloat16)
    out_partials = lax.dot_general(
        hidden.reshape(pixel_count, blocks, share),
        w_out_all.reshape(blocks, share, channel_count),
        (((2,), (1,)), ((1,), (0,))),
        preferred_element_type=jnp.float32,
    )
    mixed_sum = jnp.sum(out_partials.astype(jnp.bfloat16).astype(jnp.float32), axis=0)
    branch = mixed_sum + b_out
    feature_t = jnp.transpose(feature, (1, 2, 0)).reshape(pixel_count, channel_count)
    result_t = (feature_t.astype(jnp.float32) + layer_scale * branch).astype(jnp.bfloat16)
    result = jnp.transpose(result_t.reshape(tile_rows, tile_cols, channel_count), (2, 0, 1))
    cotangent_t = jnp.transpose(cotangent, (1, 2, 0))
    grad_out = cotangent_t.reshape(pixel_count, channel_count).astype(jnp.float32)
    g_branch = grad_out * layer_scale
    grad_layer_scale = jnp.sum(grad_out * branch, axis=0)
    grad_b_out = jnp.sum(g_branch, axis=0)
    g_out = g_branch.astype(jnp.bfloat16)
    grad_layer_scale, grad_b_out, g_out = lax.optimization_barrier((grad_layer_scale, grad_b_out, g_out))
    d_pre = contract(g_out, w_out_all, 1, 1) * gelu_slope
    g_pre = d_pre.astype(jnp.bfloat16)
    hidden_own = lax.dynamic_slice_in_dim(hidden, own * share, share, axis=1)
    g_pre_own = lax.dynamic_slice_in_dim(g_pre, own * share, share, axis=1)
    d_pre_own = lax.dynamic_slice_in_dim(d_pre, own * share, share, axis=1)
    grad_w_out = contract(hidden_own, g_out, 0, 0)
    grad_b_in = jnp.sum(d_pre_own, axis=0)
    grad_w_in = contract(normalized_output, g_pre_own, 0, 0)
    dn_partials = lax.dot_general(
        g_pre.reshape(pixel_count, blocks, share),
        w_in_all.reshape(channel_count, blocks, share),
        (((2,), (2,)), ((1,), (1,))),
        preferred_element_type=jnp.float32,
    )
    normalized_gradient = jnp.sum(dn_partials.astype(jnp.bfloat16).astype(jnp.float32), axis=0)
    standardized_gradient = normalized_gradient * norm_gain
    initial_mean = jnp.mean(standardized_gradient, axis=1, keepdims=True)
    product_mean = jnp.mean(standardized_gradient * standardized_input, axis=1, keepdims=True)
    convolved_gradient = inverse_deviation * (
        standardized_gradient - initial_mean - standardized_input * product_mean
    )
    gain_portion = jnp.sum(normalized_gradient * standardized_input, axis=0)
    bias_portion = jnp.sum(normalized_gradient, axis=0)
    grad_conv_bias = jnp.sum(convolved_gradient, axis=0)
    d_t = convolved_gradient.reshape(tile_rows, tile_cols, channel_count)
    grad_kernel = kernel_grad_minor(d_t, padded_t)
    (
        grad_kernel,
        grad_conv_bias,
        gain_portion,
        bias_portion,
        grad_w_in,
        grad_b_in,
        grad_w_out,
        grad_b_out,
        grad_layer_scale,
    ) = butterfly_sum(
        (
            grad_kernel,
            grad_conv_bias,
            gain_portion,
            bias_portion,
            grad_w_in,
            grad_b_in,
            grad_w_out,
            grad_b_out,
            grad_layer_scale,
        ),
        ("row", "col"),
    )
    d_padded = extended(d_t.astype(jnp.bfloat16), (("row", 0), ("col", 1)), 3).astype(jnp.float32)
    grad_feature_t = (
        cotangent_t.astype(jnp.float32) + depthwise_minor(d_padded, kernel[::-1, ::-1])
    ).astype(jnp.bfloat16)
    grad_feature = jnp.transpose(grad_feature_t, (2, 0, 1))
    return (
        result,
        grad_feature,
        grad_kernel * norm_factor,
        grad_conv_bias * norm_factor,
        gain_portion * norm_factor,
        bias_portion * norm_factor,
        grad_w_in * norm_factor,
        grad_b_in * norm_factor,
        grad_w_out * norm_factor,
        grad_b_out * norm_factor,
        grad_layer_scale * norm_factor,
    )


def solution(mesh):
    return jax.shard_map(
        shards,
        mesh=mesh,
        in_specs=(
            P(None, "row", "col"),
            P(),
            P(),
            P(),
            P(),
            P(None, "chan"),
            P("chan"),
            P("chan", None),
            P(),
            P(),
            P(None, "row", "col"),
        ),
        out_specs=(
            P(None, "row", "col"),
            P(None, "row", "col"),
            P(),
            P(),
            P(),
            P(),
            P(None, "chan"),
            P("chan"),
            P("chan", None),
            P(),
            P(),
        ),
        check_vma=False,
    )
```

```python
import jax
import jax.numpy as jnp
from jax import lax
from jax.experimental import pallas as pl
from jax.experimental.pallas import tpu as pltpu
from jax.sharding import PartitionSpec as P


def extended(x, sides, width):
    for axis, dim in sides:
        devices, length = (lax.axis_size(axis), x.shape[dim])
        up = [(i, (i + 1) % devices) for i in range(devices - 1)]
        down = [(j, i) for i, j in up]
        last = lax.slice_in_dim(x, length - width, length, axis=dim)
        leading = lax.slice_in_dim(x, 0, width, axis=dim)
        if devices == 2:
            first = lax.axis_index(axis) == 0
            got = lax.ppermute(jnp.where(first, last, leading), axis, [(0, 1), (1, 0)])
            nothing = jnp.zeros_like(got)
            before = jnp.where(first, nothing, got)
            after = jnp.where(first, got, nothing)
        else:
            before = lax.ppermute(last, axis, up)
            after = lax.ppermute(leading, axis, down)
        x = jnp.concatenate([before, x, after], axis=dim)
    return x


def shortened(x):
    return jax.tree.map(lambda a: a.astype(jnp.bfloat16) if a.dtype == jnp.float32 else a, x)


def depthwise(padded, kernel):
    channel_count = padded.shape[0]
    return lax.conv_general_dilated(
        padded[None],
        kernel[:, :, None, :],
        (1, 1),
        "VALID",
        dimension_numbers=("NCHW", "HWIO", "NCHW"),
        feature_group_count=channel_count,
        precision=lax.Precision.HIGHEST,
    )[0]


def gelu_parts(pre_act):
    cdf_val = 0.5 * (1.0 + lax.erf(pre_act * 0.7071067811865476))
    density = jnp.exp(-0.5 * pre_act * pre_act) * 0.3989422804014327
    return (pre_act * cdf_val, cdf_val + pre_act * density)


def contract(left, right, dim_left, dim_right):
    return lax.dot_general(
        left, right, (((dim_left,), (dim_right,)), ((), ())), preferred_element_type=jnp.float32
    )


def layer_norm_forward(conv_flat, norm_gain, norm_bias):
    mean_val = jnp.mean(conv_flat, axis=0)
    centered_values = conv_flat - mean_val
    variance = jnp.mean(centered_values * centered_values, axis=0)
    inverse_deviation = lax.rsqrt(variance + 1e-06)
    standardized_input = centered_values * inverse_deviation
    normalized_output = (standardized_input * norm_gain[:, None] + norm_bias[:, None]).astype(
        jnp.bfloat16
    )
    return (standardized_input, inverse_deviation, normalized_output)


def layer_norm_backward(normalized_gradient, standardized_input, inverse_deviation, norm_gain):
    standardized_gradient = normalized_gradient * norm_gain[:, None]
    initial_mean = jnp.mean(standardized_gradient, axis=0)
    product_mean = jnp.mean(standardized_gradient * standardized_input, axis=0)
    convolved_gradient = inverse_deviation * (
        standardized_gradient - initial_mean - standardized_input * product_mean
    )
    return (
        convolved_gradient,
        jnp.sum(normalized_gradient * standardized_input, axis=1),
        jnp.sum(normalized_gradient, axis=1),
    )


def kernel_grad_body(d_ref, p_ref, o_ref, shifted_ref):
    rows, cols, _ = d_ref.shape
    taps = o_ref.shape[0]
    side = int(round(taps ** 0.5))
    o_ref[...] = jnp.zeros(o_ref.shape, o_ref.dtype)
    for j in range(side):
        shifted_ref[j] = p_ref[:, j : j + cols, :]

    def row_step(h, carry):
        d_row = d_ref[h]
        for i in range(side):
            for j in range(side):
                prod = d_row * shifted_ref[j, h + i]
                part = jnp.sum(prod.reshape(cols // 8, 8, prod.shape[-1]), axis=0)
                o_ref[i * side + j] += part
        return carry

    lax.fori_loop(0, rows, row_step, 0)


def kernel_grad_minor(d_t, p_t):
    side = p_t.shape[0] - d_t.shape[0] + 1
    channel_count = d_t.shape[-1]
    partial = pl.pallas_call(
        kernel_grad_body,
        out_shape=jax.ShapeDtypeStruct((side * side, 8, channel_count), jnp.float32),
        scratch_shapes=[pltpu.VMEM((side,) + p_t.shape[:1] + d_t.shape[1:], jnp.float32)],
    )(d_t, p_t)
    return jnp.sum(partial, axis=1).reshape(side, side, channel_count)


def flat_pack(values):
    return jnp.concatenate([v.reshape(-1) for v in values])


def flat_unpack(flat, values):
    out = []
    offset = 0
    for v in values:
        out.append(flat[offset : offset + v.size].reshape(v.shape))
        offset += v.size
    return out


def butterfly_steps(axes):
    steps = []
    for axis in axes:
        devices = lax.axis_size(axis)
        if devices & (devices - 1):
            steps.append((axis, 0))
            continue
        step = 1
        while step < devices:
            steps.append((axis, step))
            step *= 2
    return steps


def butterfly_step(flat, axis, step):
    if step == 0:
        return lax.psum(flat, axis)
    devices = lax.axis_size(axis)
    return flat + lax.ppermute(flat, axis, [(i, i ^ step) for i in range(devices)])


def butterfly_sum(values, axes):
    flat = flat_pack(values)
    first = butterfly_steps(axes[:1])
    order_a = first + butterfly_steps(axes[1:])[::-1]
    order_b = order_a[len(first) :] + order_a[: len(first)]
    half = flat.shape[0] // 2
    part_a, part_b = flat[:half], flat[half:]
    for step_a, step_b in zip(order_a, order_b):
        part_a, part_b = butterfly_step(part_a, *step_a), butterfly_step(part_b, *step_b)
    return flat_unpack(jnp.concatenate([part_a, part_b]), values)


def gathered_weights(w_in, b_in, w_out):
    channel_count = w_in.shape[0]
    pieces = []
    rest = b_in
    for _ in range(3):
        piece = rest.astype(jnp.bfloat16)
        rest = rest - piece.astype(jnp.float32)
        pieces.append(piece[:, None])
    packed = jnp.concatenate([w_in.T, w_out] + pieces, axis=1)
    full = lax.all_gather(packed, "chan", axis=0, tiled=True)
    w_in_all = full[:, :channel_count].T
    w_out_all = full[:, channel_count : 2 * channel_count]
    parts = full[:, 2 * channel_count :].astype(jnp.float32)
    b_in_all = (parts[:, 0] + parts[:, 1]) + parts[:, 2]
    return w_in_all, b_in_all, w_out_all


def depthwise_minor(padded_t, kernel):
    channel_count = padded_t.shape[-1]
    return lax.conv_general_dilated(
        padded_t[None],
        kernel[:, :, None, :],
        (1, 1),
        "VALID",
        dimension_numbers=("NHWC", "HWIO", "NHWC"),
        feature_group_count=channel_count,
        precision=lax.Precision.HIGHEST,
    )[0]


def shards(
    feature,
    kernel,
    conv_bias,
    norm_gain,
    norm_bias,
    w_in,
    b_in,
    w_out,
    b_out,
    layer_scale,
    cotangent,
):
    channel_count, tile_rows, tile_cols = feature.shape
    pixel_count = tile_rows * tile_cols
    blocks = lax.axis_size("chan")
    share = w_in.shape[1]
    own = lax.axis_index("chan")
    w_in_all, b_in_all, w_out_all = gathered_weights(w_in, b_in, w_out)
    padded_bf = extended(feature, (("row", 1), ("col", 2)), 3)
    padded_t = jnp.transpose(padded_bf, (1, 2, 0)).astype(jnp.float32)
    total_pixels = pixel_count * lax.axis_size("row") * lax.axis_size("col")
    norm_factor = 1.0 / jnp.sqrt(jnp.float32(total_pixels))
    conv_flat = (depthwise_minor(padded_t, kernel) + conv_bias).reshape(pixel_count, channel_count)
    mean_val = jnp.mean(conv_flat, axis=1, keepdims=True)
    centered_values = conv_flat - mean_val
    variance = jnp.mean(centered_values * centered_values, axis=1, keepdims=True)
    inverse_deviation = lax.rsqrt(variance + 1e-06)
    standardized_input = centered_values * inverse_deviation
    normalized_output = (standardized_input * norm_gain + norm_bias).astype(jnp.bfloat16)
    pre_act = contract(normalized_output, w_in_all, 1, 0) + b_in_all
    gelu_val, gelu_slope = gelu_parts(pre_act)
    hidden = gelu_val.astype(jnp.bfloat16)
    out_partials = lax.dot_general(
        hidden.reshape(pixel_count, blocks, share),
        w_out_all.reshape(blocks, share, channel_count),
        (((2,), (1,)), ((1,), (0,))),
        preferred_element_type=jnp.float32,
    )
    mixed_sum = jnp.sum(out_partials.astype(jnp.bfloat16).astype(jnp.float32), axis=0)
    branch = mixed_sum + b_out
    feature_t = jnp.transpose(feature, (1, 2, 0)).reshape(pixel_count, channel_count)
    result_t = (feature_t.astype(jnp.float32) + layer_scale * branch).astype(jnp.bfloat16)
    result = jnp.transpose(result_t.reshape(tile_rows, tile_cols, channel_count), (2, 0, 1))
    cotangent_t = jnp.transpose(cotangent, (1, 2, 0))
    grad_out = cotangent_t.reshape(pixel_count, channel_count).astype(jnp.float32)
    g_branch = grad_out * layer_scale
    grad_layer_scale = jnp.sum(grad_out * branch, axis=0)
    grad_b_out = jnp.sum(g_branch, axis=0)
    g_out = g_branch.astype(jnp.bfloat16)
    grad_layer_scale, grad_b_out, g_out = lax.optimization_barrier((grad_layer_scale, grad_b_out, g_out))
    d_pre = contract(g_out, w_out_all, 1, 1) * gelu_slope
    g_pre = d_pre.astype(jnp.bfloat16)
    hidden_own = lax.dynamic_slice_in_dim(hidden, own * share, share, axis=1)
    g_pre_own = lax.dynamic_slice_in_dim(g_pre, own * share, share, axis=1)
    d_pre_own = lax.dynamic_slice_in_dim(d_pre, own * share, share, axis=1)
    grad_w_out = contract(hidden_own, g_out, 0, 0)
    grad_b_in = jnp.sum(d_pre_own, axis=0)
    grad_b_in, g_pre = lax.optimization_barrier((grad_b_in, g_pre))
    grad_w_in = contract(normalized_output, g_pre_own, 0, 0)
    dn_partials = lax.dot_general(
        g_pre.reshape(pixel_count, blocks, share),
        w_in_all.reshape(channel_count, blocks, share),
        (((2,), (2,)), ((1,), (1,))),
        preferred_element_type=jnp.float32,
    )
    normalized_gradient = jnp.sum(dn_partials.astype(jnp.bfloat16).astype(jnp.float32), axis=0)
    standardized_gradient = normalized_gradient * norm_gain
    initial_mean = jnp.mean(standardized_gradient, axis=1, keepdims=True)
    product_mean = jnp.mean(standardized_gradient * standardized_input, axis=1, keepdims=True)
    convolved_gradient = inverse_deviation * (
        standardized_gradient - initial_mean - standardized_input * product_mean
    )
    gain_portion = jnp.sum(normalized_gradient * standardized_input, axis=0)
    bias_portion = jnp.sum(normalized_gradient, axis=0)
    grad_conv_bias = jnp.sum(convolved_gradient, axis=0)
    d_t = convolved_gradient.reshape(tile_rows, tile_cols, channel_count)
    grad_kernel = kernel_grad_minor(d_t, padded_t)
    (
        grad_kernel,
        grad_conv_bias,
        gain_portion,
        bias_portion,
        grad_w_in,
        grad_b_in,
        grad_w_out,
        grad_b_out,
        grad_layer_scale,
    ) = butterfly_sum(
        (
            grad_kernel,
            grad_conv_bias,
            gain_portion,
            bias_portion,
            grad_w_in,
            grad_b_in,
            grad_w_out,
            grad_b_out,
            grad_layer_scale,
        ),
        ("row", "col"),
    )
    d_padded = extended(d_t.astype(jnp.bfloat16), (("row", 0), ("col", 1)), 3).astype(jnp.float32)
    grad_feature_t = (
        cotangent_t.astype(jnp.float32) + depthwise_minor(d_padded, kernel[::-1, ::-1])
    ).astype(jnp.bfloat16)
    grad_feature = jnp.transpose(grad_feature_t, (2, 0, 1))
    return (
        result,
        grad_feature,
        grad_kernel * norm_factor,
        grad_conv_bias * norm_factor,
        gain_portion * norm_factor,
        bias_portion * norm_factor,
        grad_w_in * norm_factor,
        grad_b_in * norm_factor,
        grad_w_out * norm_factor,
        grad_b_out * norm_factor,
        grad_layer_scale * norm_factor,
    )


def solution(mesh):
    return jax.shard_map(
        shards,
        mesh=mesh,
        in_specs=(
            P(None, "row", "col"),
            P(),
            P(),
            P(),
            P(),
            P(None, "chan"),
            P("chan"),
            P("chan", None),
            P(),
            P(),
            P(None, "row", "col"),
        ),
        out_specs=(
            P(None, "row", "col"),
            P(None, "row", "col"),
            P(),
            P(),
            P(),
            P(),
            P(None, "chan"),
            P("chan"),
            P("chan", None),
            P(),
            P(),
        ),
        check_vma=False,
    )
```

```python
import jax
import jax.numpy as jnp
from jax import lax
from jax.experimental import pallas as pl
from jax.experimental.pallas import tpu as pltpu
from jax.sharding import PartitionSpec as P


def extended(x, sides, width):
    for axis, dim in sides:
        devices, length = (lax.axis_size(axis), x.shape[dim])
        up = [(i, (i + 1) % devices) for i in range(devices - 1)]
        down = [(j, i) for i, j in up]
        last = lax.slice_in_dim(x, length - width, length, axis=dim)
        leading = lax.slice_in_dim(x, 0, width, axis=dim)
        if devices == 2:
            first = lax.axis_index(axis) == 0
            got = lax.ppermute(jnp.where(first, last, leading), axis, [(0, 1), (1, 0)])
            nothing = jnp.zeros_like(got)
            before = jnp.where(first, nothing, got)
            after = jnp.where(first, got, nothing)
        else:
            before = lax.ppermute(last, axis, up)
            after = lax.ppermute(leading, axis, down)
        x = jnp.concatenate([before, x, after], axis=dim)
    return x


def shortened(x):
    return jax.tree.map(lambda a: a.astype(jnp.bfloat16) if a.dtype == jnp.float32 else a, x)


def depthwise(padded, kernel):
    channel_count = padded.shape[0]
    return lax.conv_general_dilated(
        padded[None],
        kernel[:, :, None, :],
        (1, 1),
        "VALID",
        dimension_numbers=("NCHW", "HWIO", "NCHW"),
        feature_group_count=channel_count,
        precision=lax.Precision.HIGHEST,
    )[0]


def gelu_parts(pre_act):
    cdf_val = 0.5 * (1.0 + lax.erf(pre_act * 0.7071067811865476))
    density = jnp.exp(-0.5 * pre_act * pre_act) * 0.3989422804014327
    return (pre_act * cdf_val, cdf_val + pre_act * density)


def contract(left, right, dim_left, dim_right):
    return lax.dot_general(
        left, right, (((dim_left,), (dim_right,)), ((), ())), preferred_element_type=jnp.float32
    )


def layer_norm_forward(conv_flat, norm_gain, norm_bias):
    mean_val = jnp.mean(conv_flat, axis=0)
    centered_values = conv_flat - mean_val
    variance = jnp.mean(centered_values * centered_values, axis=0)
    inverse_deviation = lax.rsqrt(variance + 1e-06)
    standardized_input = centered_values * inverse_deviation
    normalized_output = (standardized_input * norm_gain[:, None] + norm_bias[:, None]).astype(
        jnp.bfloat16
    )
    return (standardized_input, inverse_deviation, normalized_output)


def layer_norm_backward(normalized_gradient, standardized_input, inverse_deviation, norm_gain):
    standardized_gradient = normalized_gradient * norm_gain[:, None]
    initial_mean = jnp.mean(standardized_gradient, axis=0)
    product_mean = jnp.mean(standardized_gradient * standardized_input, axis=0)
    convolved_gradient = inverse_deviation * (
        standardized_gradient - initial_mean - standardized_input * product_mean
    )
    return (
        convolved_gradient,
        jnp.sum(normalized_gradient * standardized_input, axis=1),
        jnp.sum(normalized_gradient, axis=1),
    )


def kernel_grad_body(d_ref, p_ref, o_ref, shifted_ref):
    rows, cols, _ = d_ref.shape
    taps = o_ref.shape[0]
    side = int(round(taps ** 0.5))
    o_ref[...] = jnp.zeros(o_ref.shape, o_ref.dtype)
    for j in range(side):
        shifted_ref[j] = p_ref[:, j : j + cols, :]

    def row_step(h, carry):
        d_row = d_ref[h]
        for i in range(side):
            for j in range(side):
                prod = d_row * shifted_ref[j, h + i]
                part = jnp.sum(prod.reshape(cols // 8, 8, prod.shape[-1]), axis=0)
                o_ref[i * side + j] += part
        return carry

    lax.fori_loop(0, rows, row_step, 0)


def kernel_grad_minor(d_t, p_t):
    side = p_t.shape[0] - d_t.shape[0] + 1
    channel_count = d_t.shape[-1]
    partial = pl.pallas_call(
        kernel_grad_body,
        out_shape=jax.ShapeDtypeStruct((side * side, 8, channel_count), jnp.float32),
        scratch_shapes=[pltpu.VMEM((side,) + p_t.shape[:1] + d_t.shape[1:], jnp.float32)],
    )(d_t, p_t)
    return jnp.sum(partial, axis=1).reshape(side, side, channel_count)


def flat_pack(values):
    return jnp.concatenate([v.reshape(-1) for v in values])


def flat_unpack(flat, values):
    out = []
    offset = 0
    for v in values:
        out.append(flat[offset : offset + v.size].reshape(v.shape))
        offset += v.size
    return out


def butterfly_steps(axes):
    steps = []
    for axis in axes:
        devices = lax.axis_size(axis)
        if devices & (devices - 1):
            steps.append((axis, 0))
            continue
        step = 1
        while step < devices:
            steps.append((axis, step))
            step *= 2
    return steps


def butterfly_step(flat, axis, step):
    if step == 0:
        return lax.psum(flat, axis)
    devices = lax.axis_size(axis)
    return flat + lax.ppermute(flat, axis, [(i, i ^ step) for i in range(devices)])


def butterfly_sum(values, axes, late_count):
    flat = flat_pack(values)
    first = butterfly_steps(axes[:1])
    order_a = first + butterfly_steps(axes[1:])[::-1]
    order_b = order_a[len(first) :] + order_a[: len(first)]
    half = sum(v.size for v in values[:late_count])
    part_a, part_b = flat[:half], flat[half:]
    for step_a, step_b in zip(order_a, order_b):
        part_a, part_b = butterfly_step(part_a, *step_a), butterfly_step(part_b, *step_b)
    return flat_unpack(jnp.concatenate([part_a, part_b]), values)


def gathered_weights(w_in, b_in, w_out):
    channel_count = w_in.shape[0]
    pieces = []
    rest = b_in
    for _ in range(3):
        piece = rest.astype(jnp.bfloat16)
        rest = rest - piece.astype(jnp.float32)
        pieces.append(piece[:, None])
    packed = jnp.concatenate([w_in.T, w_out] + pieces, axis=1)
    full = lax.all_gather(packed, "chan", axis=0, tiled=True)
    w_in_all = full[:, :channel_count].T
    w_out_all = full[:, channel_count : 2 * channel_count]
    parts = full[:, 2 * channel_count :].astype(jnp.float32)
    b_in_all = (parts[:, 0] + parts[:, 1]) + parts[:, 2]
    return w_in_all, b_in_all, w_out_all


def depthwise_minor(padded_t, kernel):
    channel_count = padded_t.shape[-1]
    return lax.conv_general_dilated(
        padded_t[None],
        kernel[:, :, None, :],
        (1, 1),
        "VALID",
        dimension_numbers=("NHWC", "HWIO", "NHWC"),
        feature_group_count=channel_count,
        precision=lax.Precision.HIGHEST,
    )[0]


def shards(
    feature,
    kernel,
    conv_bias,
    norm_gain,
    norm_bias,
    w_in,
    b_in,
    w_out,
    b_out,
    layer_scale,
    cotangent,
):
    channel_count, tile_rows, tile_cols = feature.shape
    pixel_count = tile_rows * tile_cols
    blocks = lax.axis_size("chan")
    share = w_in.shape[1]
    own = lax.axis_index("chan")
    w_in_all, b_in_all, w_out_all = gathered_weights(w_in, b_in, w_out)
    padded_bf = extended(feature, (("row", 1), ("col", 2)), 3)
    padded_t = jnp.transpose(padded_bf, (1, 2, 0)).astype(jnp.float32)
    total_pixels = pixel_count * lax.axis_size("row") * lax.axis_size("col")
    norm_factor = 1.0 / jnp.sqrt(jnp.float32(total_pixels))
    conv_flat = (depthwise_minor(padded_t, kernel) + conv_bias).reshape(pixel_count, channel_count)
    mean_val = jnp.mean(conv_flat, axis=1, keepdims=True)
    centered_values = conv_flat - mean_val
    variance = jnp.mean(centered_values * centered_values, axis=1, keepdims=True)
    inverse_deviation = lax.rsqrt(variance + 1e-06)
    standardized_input = centered_values * inverse_deviation
    normalized_output = (standardized_input * norm_gain + norm_bias).astype(jnp.bfloat16)
    pre_act = contract(normalized_output, w_in_all, 1, 0) + b_in_all
    gelu_val, gelu_slope = gelu_parts(pre_act)
    hidden = gelu_val.astype(jnp.bfloat16)
    out_partials = lax.dot_general(
        hidden.reshape(pixel_count, blocks, share),
        w_out_all.reshape(blocks, share, channel_count),
        (((2,), (1,)), ((1,), (0,))),
        preferred_element_type=jnp.float32,
    )
    mixed_sum = jnp.sum(out_partials.astype(jnp.bfloat16).astype(jnp.float32), axis=0)
    branch = mixed_sum + b_out
    feature_t = jnp.transpose(feature, (1, 2, 0)).reshape(pixel_count, channel_count)
    result_t = (feature_t.astype(jnp.float32) + layer_scale * branch).astype(jnp.bfloat16)
    result = jnp.transpose(result_t.reshape(tile_rows, tile_cols, channel_count), (2, 0, 1))
    cotangent_t = jnp.transpose(cotangent, (1, 2, 0))
    grad_out = cotangent_t.reshape(pixel_count, channel_count).astype(jnp.float32)
    g_branch = grad_out * layer_scale
    grad_layer_scale = jnp.sum(grad_out * branch, axis=0)
    grad_b_out = jnp.sum(g_branch, axis=0)
    g_out = g_branch.astype(jnp.bfloat16)
    grad_layer_scale, grad_b_out, g_out = lax.optimization_barrier((grad_layer_scale, grad_b_out, g_out))
    d_pre = contract(g_out, w_out_all, 1, 1) * gelu_slope
    g_pre = d_pre.astype(jnp.bfloat16)
    hidden_own = lax.dynamic_slice_in_dim(hidden, own * share, share, axis=1)
    g_pre_own = lax.dynamic_slice_in_dim(g_pre, own * share, share, axis=1)
    d_pre_own = lax.dynamic_slice_in_dim(d_pre, own * share, share, axis=1)
    grad_w_out = contract(hidden_own, g_out, 0, 0)
    grad_b_in = jnp.sum(d_pre_own, axis=0)
    grad_b_in, g_pre = lax.optimization_barrier((grad_b_in, g_pre))
    grad_w_in = contract(normalized_output, g_pre_own, 0, 0)
    dn_partials = lax.dot_general(
        g_pre.reshape(pixel_count, blocks, share),
        w_in_all.reshape(channel_count, blocks, share),
        (((2,), (2,)), ((1,), (1,))),
        preferred_element_type=jnp.float32,
    )
    normalized_gradient = jnp.sum(dn_partials.astype(jnp.bfloat16).astype(jnp.float32), axis=0)
    standardized_gradient = normalized_gradient * norm_gain
    initial_mean = jnp.mean(standardized_gradient, axis=1, keepdims=True)
    product_mean = jnp.mean(standardized_gradient * standardized_input, axis=1, keepdims=True)
    convolved_gradient = inverse_deviation * (
        standardized_gradient - initial_mean - standardized_input * product_mean
    )
    gain_portion = jnp.sum(normalized_gradient * standardized_input, axis=0)
    bias_portion = jnp.sum(normalized_gradient, axis=0)
    grad_conv_bias = jnp.sum(convolved_gradient, axis=0)
    d_t = convolved_gradient.reshape(tile_rows, tile_cols, channel_count)
    grad_kernel = kernel_grad_minor(d_t, padded_t)
    (
        grad_kernel,
        grad_conv_bias,
        gain_portion,
        bias_portion,
        grad_w_in,
        grad_b_in,
        grad_w_out,
        grad_b_out,
        grad_layer_scale,
    ) = butterfly_sum(
        (
            grad_kernel,
            grad_conv_bias,
            gain_portion,
            bias_portion,
            grad_w_in,
            grad_b_in,
            grad_w_out,
            grad_b_out,
            grad_layer_scale,
        ),
        ("row", "col"),
        4,
    )
    d_padded = extended(d_t.astype(jnp.bfloat16), (("row", 0), ("col", 1)), 3).astype(jnp.float32)
    grad_feature_t = (
        cotangent_t.astype(jnp.float32) + depthwise_minor(d_padded, kernel[::-1, ::-1])
    ).astype(jnp.bfloat16)
    grad_feature = jnp.transpose(grad_feature_t, (2, 0, 1))
    return (
        result,
        grad_feature,
        grad_kernel * norm_factor,
        grad_conv_bias * norm_factor,
        gain_portion * norm_factor,
        bias_portion * norm_factor,
        grad_w_in * norm_factor,
        grad_b_in * norm_factor,
        grad_w_out * norm_factor,
        grad_b_out * norm_factor,
        grad_layer_scale * norm_factor,
    )


def solution(mesh):
    return jax.shard_map(
        shards,
        mesh=mesh,
        in_specs=(
            P(None, "row", "col"),
            P(),
            P(),
            P(),
            P(),
            P(None, "chan"),
            P("chan"),
            P("chan", None),
            P(),
            P(),
            P(None, "row", "col"),
        ),
        out_specs=(
            P(None, "row", "col"),
            P(None, "row", "col"),
            P(),
            P(),
            P(),
            P(),
            P(None, "chan"),
            P("chan"),
            P("chan", None),
            P(),
            P(),
        ),
        check_vma=False,
    )
```

```python
import jax
import jax.numpy as jnp
from jax import lax
from jax.experimental import pallas as pl
from jax.experimental.pallas import tpu as pltpu
from jax.sharding import PartitionSpec as P


def extended(x, sides, width):
    for axis, dim in sides:
        devices, length = (lax.axis_size(axis), x.shape[dim])
        up = [(i, (i + 1) % devices) for i in range(devices - 1)]
        down = [(j, i) for i, j in up]
        last = lax.slice_in_dim(x, length - width, length, axis=dim)
        leading = lax.slice_in_dim(x, 0, width, axis=dim)
        if devices == 2:
            first = lax.axis_index(axis) == 0
            got = lax.ppermute(jnp.where(first, last, leading), axis, [(0, 1), (1, 0)])
            nothing = jnp.zeros_like(got)
            before = jnp.where(first, nothing, got)
            after = jnp.where(first, got, nothing)
        else:
            before = lax.ppermute(last, axis, up)
            after = lax.ppermute(leading, axis, down)
        x = jnp.concatenate([before, x, after], axis=dim)
    return x


def shortened(x):
    return jax.tree.map(lambda a: a.astype(jnp.bfloat16) if a.dtype == jnp.float32 else a, x)


def depthwise(padded, kernel):
    channel_count = padded.shape[0]
    return lax.conv_general_dilated(
        padded[None],
        kernel[:, :, None, :],
        (1, 1),
        "VALID",
        dimension_numbers=("NCHW", "HWIO", "NCHW"),
        feature_group_count=channel_count,
        precision=lax.Precision.HIGHEST,
    )[0]


def gelu_parts(pre_act):
    cdf_val = 0.5 * (1.0 + lax.erf(pre_act * 0.7071067811865476))
    density = jnp.exp(-0.5 * pre_act * pre_act) * 0.3989422804014327
    return (pre_act * cdf_val, cdf_val + pre_act * density)


def contract(left, right, dim_left, dim_right):
    return lax.dot_general(
        left, right, (((dim_left,), (dim_right,)), ((), ())), preferred_element_type=jnp.float32
    )


def layer_norm_forward(conv_flat, norm_gain, norm_bias):
    mean_val = jnp.mean(conv_flat, axis=0)
    centered_values = conv_flat - mean_val
    variance = jnp.mean(centered_values * centered_values, axis=0)
    inverse_deviation = lax.rsqrt(variance + 1e-06)
    standardized_input = centered_values * inverse_deviation
    normalized_output = (standardized_input * norm_gain[:, None] + norm_bias[:, None]).astype(
        jnp.bfloat16
    )
    return (standardized_input, inverse_deviation, normalized_output)


def layer_norm_backward(normalized_gradient, standardized_input, inverse_deviation, norm_gain):
    standardized_gradient = normalized_gradient * norm_gain[:, None]
    initial_mean = jnp.mean(standardized_gradient, axis=0)
    product_mean = jnp.mean(standardized_gradient * standardized_input, axis=0)
    convolved_gradient = inverse_deviation * (
        standardized_gradient - initial_mean - standardized_input * product_mean
    )
    return (
        convolved_gradient,
        jnp.sum(normalized_gradient * standardized_input, axis=1),
        jnp.sum(normalized_gradient, axis=1),
    )


def kernel_grad_body(d_ref, p_ref, o_ref, shifted_ref):
    rows, cols, _ = d_ref.shape
    taps = o_ref.shape[0]
    side = int(round(taps ** 0.5))
    o_ref[...] = jnp.zeros(o_ref.shape, o_ref.dtype)
    for j in range(side):
        shifted_ref[j] = p_ref[:, j : j + cols, :]

    def row_step(h, carry):
        d_row = d_ref[h]
        for i in range(side):
            for j in range(side):
                prod = d_row * shifted_ref[j, h + i]
                part = jnp.sum(prod.reshape(cols // 8, 8, prod.shape[-1]), axis=0)
                o_ref[i * side + j] += part
        return carry

    lax.fori_loop(0, rows, row_step, 0)


def kernel_grad_minor(d_t, p_t):
    side = p_t.shape[0] - d_t.shape[0] + 1
    channel_count = d_t.shape[-1]
    partial = pl.pallas_call(
        kernel_grad_body,
        out_shape=jax.ShapeDtypeStruct((side * side, 8, channel_count), jnp.float32),
        scratch_shapes=[pltpu.VMEM((side,) + p_t.shape[:1] + d_t.shape[1:], jnp.float32)],
    )(d_t, p_t)
    return jnp.sum(partial, axis=1).reshape(side, side, channel_count)


def flat_pack(values):
    return jnp.concatenate([v.reshape(-1) for v in values])


def flat_unpack(flat, values):
    out = []
    offset = 0
    for v in values:
        out.append(flat[offset : offset + v.size].reshape(v.shape))
        offset += v.size
    return out


def butterfly_steps(axes):
    steps = []
    for axis in axes:
        devices = lax.axis_size(axis)
        if devices & (devices - 1):
            steps.append((axis, 0))
            continue
        step = 1
        while step < devices:
            steps.append((axis, step))
            step *= 2
    return steps


def butterfly_step(flat, axis, step):
    if step == 0:
        return lax.psum(flat, axis)
    devices = lax.axis_size(axis)
    return flat + lax.ppermute(flat, axis, [(i, i ^ step) for i in range(devices)])


def butterfly_sum(values, axes, late_count):
    flat = flat_pack(values)
    first = butterfly_steps(axes[:1])
    order_a = first + butterfly_steps(axes[1:])[::-1]
    order_b = order_a[len(first) :] + order_a[: len(first)]
    half = sum(v.size for v in values[:late_count])
    part_a, part_b = flat[:half], flat[half:]
    for step_a, step_b in zip(order_a, order_b):
        part_a, part_b = butterfly_step(part_a, *step_a), butterfly_step(part_b, *step_b)
    return flat_unpack(jnp.concatenate([part_a, part_b]), values)


def gathered_weights(w_in, b_in, w_out):
    channel_count = w_in.shape[0]
    pieces = []
    rest = b_in
    for _ in range(3):
        piece = rest.astype(jnp.bfloat16)
        rest = rest - piece.astype(jnp.float32)
        pieces.append(piece[:, None])
    packed = jnp.concatenate([w_in.T, w_out] + pieces, axis=1)
    full = lax.all_gather(packed, "chan", axis=0, tiled=True)
    w_in_all = full[:, :channel_count].T
    w_out_all = full[:, channel_count : 2 * channel_count]
    parts = full[:, 2 * channel_count :].astype(jnp.float32)
    b_in_all = (parts[:, 0] + parts[:, 1]) + parts[:, 2]
    return w_in_all, b_in_all, w_out_all


def depthwise_minor(padded_t, kernel):
    channel_count = padded_t.shape[-1]
    return lax.conv_general_dilated(
        padded_t[None],
        kernel[:, :, None, :],
        (1, 1),
        "VALID",
        dimension_numbers=("NHWC", "HWIO", "NHWC"),
        feature_group_count=channel_count,
        precision=lax.Precision.HIGHEST,
    )[0]


def shards(
    feature,
    kernel,
    conv_bias,
    norm_gain,
    norm_bias,
    w_in,
    b_in,
    w_out,
    b_out,
    layer_scale,
    cotangent,
):
    channel_count, tile_rows, tile_cols = feature.shape
    pixel_count = tile_rows * tile_cols
    blocks = lax.axis_size("chan")
    share = w_in.shape[1]
    own = lax.axis_index("chan")
    w_in_all, b_in_all, w_out_all = gathered_weights(w_in, b_in, w_out)
    padded_bf = extended(feature, (("row", 1), ("col", 2)), 3)
    padded_t = jnp.transpose(padded_bf, (1, 2, 0)).astype(jnp.float32)
    total_pixels = pixel_count * lax.axis_size("row") * lax.axis_size("col")
    norm_factor = 1.0 / jnp.sqrt(jnp.float32(total_pixels))
    conv_flat = (depthwise_minor(padded_t, kernel) + conv_bias).reshape(pixel_count, channel_count)
    mean_val = jnp.mean(conv_flat, axis=1, keepdims=True)
    centered_values = conv_flat - mean_val
    variance = jnp.mean(centered_values * centered_values, axis=1, keepdims=True)
    inverse_deviation = lax.rsqrt(variance + 1e-06)
    standardized_input = centered_values * inverse_deviation
    normalized_output = (standardized_input * norm_gain + norm_bias).astype(jnp.bfloat16)
    pre_act = contract(normalized_output, w_in_all, 1, 0) + b_in_all
    gelu_val, gelu_slope = gelu_parts(pre_act)
    hidden = gelu_val.astype(jnp.bfloat16)
    out_partials = lax.dot_general(
        hidden.reshape(pixel_count, blocks, share),
        w_out_all.reshape(blocks, share, channel_count),
        (((2,), (1,)), ((1,), (0,))),
        preferred_element_type=jnp.float32,
    )
    mixed_sum = jnp.sum(out_partials.astype(jnp.bfloat16).astype(jnp.float32), axis=0)
    branch = mixed_sum + b_out
    feature_t = jnp.transpose(feature, (1, 2, 0)).reshape(pixel_count, channel_count)
    result_t = (feature_t.astype(jnp.float32) + layer_scale * branch).astype(jnp.bfloat16)
    result = jnp.transpose(result_t.reshape(tile_rows, tile_cols, channel_count), (2, 0, 1))
    cotangent_t = jnp.transpose(cotangent, (1, 2, 0))
    grad_out = cotangent_t.reshape(pixel_count, channel_count).astype(jnp.float32)
    g_branch = grad_out * layer_scale
    grad_layer_scale = jnp.sum(grad_out * branch, axis=0)
    grad_b_out = jnp.sum(g_branch, axis=0)
    g_out = g_branch.astype(jnp.bfloat16)
    grad_layer_scale, grad_b_out, g_out = lax.optimization_barrier((grad_layer_scale, grad_b_out, g_out))
    d_pre = contract(g_out, w_out_all, 1, 1) * gelu_slope
    g_pre = d_pre.astype(jnp.bfloat16)
    hidden_own = lax.dynamic_slice_in_dim(hidden, own * share, share, axis=1)
    g_pre_own = lax.dynamic_slice_in_dim(g_pre, own * share, share, axis=1)
    d_pre_own = lax.dynamic_slice_in_dim(d_pre, own * share, share, axis=1)
    grad_w_out = contract(hidden_own, g_out, 0, 0)
    grad_b_in = jnp.sum(d_pre_own, axis=0)
    grad_b_in, g_pre = lax.optimization_barrier((grad_b_in, g_pre))
    grad_w_in = contract(normalized_output, g_pre_own, 0, 0)
    dn_partials = lax.dot_general(
        g_pre.reshape(pixel_count, blocks, share),
        w_in_all.reshape(channel_count, blocks, share),
        (((2,), (2,)), ((1,), (1,))),
        preferred_element_type=jnp.float32,
    )
    normalized_gradient = jnp.sum(dn_partials.astype(jnp.bfloat16).astype(jnp.float32), axis=0)
    standardized_gradient = normalized_gradient * norm_gain
    initial_mean = jnp.mean(standardized_gradient, axis=1, keepdims=True)
    product_mean = jnp.mean(standardized_gradient * standardized_input, axis=1, keepdims=True)
    convolved_gradient = inverse_deviation * (
        standardized_gradient - initial_mean - standardized_input * product_mean
    )
    gain_portion = jnp.sum(normalized_gradient * standardized_input, axis=0)
    bias_portion = jnp.sum(normalized_gradient, axis=0)
    grad_conv_bias = jnp.sum(convolved_gradient, axis=0)
    d_t = convolved_gradient.reshape(tile_rows, tile_cols, channel_count)
    d_padded = extended(d_t.astype(jnp.bfloat16), (("row", 0), ("col", 1)), 3)
    d_padded, d_t = lax.optimization_barrier((d_padded, d_t))
    grad_kernel = kernel_grad_minor(d_t, padded_t)
    (
        grad_kernel,
        grad_conv_bias,
        gain_portion,
        bias_portion,
        grad_w_in,
        grad_b_in,
        grad_w_out,
        grad_b_out,
        grad_layer_scale,
    ) = butterfly_sum(
        (
            grad_kernel,
            grad_conv_bias,
            gain_portion,
            bias_portion,
            grad_w_in,
            grad_b_in,
            grad_w_out,
            grad_b_out,
            grad_layer_scale,
        ),
        ("row", "col"),
        4,
    )
    d_padded = d_padded.astype(jnp.float32)
    grad_feature_t = (
        cotangent_t.astype(jnp.float32) + depthwise_minor(d_padded, kernel[::-1, ::-1])
    ).astype(jnp.bfloat16)
    grad_feature = jnp.transpose(grad_feature_t, (2, 0, 1))
    return (
        result,
        grad_feature,
        grad_kernel * norm_factor,
        grad_conv_bias * norm_factor,
        gain_portion * norm_factor,
        bias_portion * norm_factor,
        grad_w_in * norm_factor,
        grad_b_in * norm_factor,
        grad_w_out * norm_factor,
        grad_b_out * norm_factor,
        grad_layer_scale * norm_factor,
    )


def solution(mesh):
    return jax.shard_map(
        shards,
        mesh=mesh,
        in_specs=(
            P(None, "row", "col"),
            P(),
            P(),
            P(),
            P(),
            P(None, "chan"),
            P("chan"),
            P("chan", None),
            P(),
            P(),
            P(None, "row", "col"),
        ),
        out_specs=(
            P(None, "row", "col"),
            P(None, "row", "col"),
            P(),
            P(),
            P(),
            P(),
            P(None, "chan"),
            P("chan"),
            P("chan", None),
            P(),
            P(),
        ),
        check_vma=False,
    )
```

```python
import jax
import jax.numpy as jnp
from jax import lax
from jax.experimental import pallas as pl
from jax.experimental.pallas import tpu as pltpu
from jax.sharding import PartitionSpec as P


def extended(x, sides, width):
    for axis, dim in sides:
        devices, length = (lax.axis_size(axis), x.shape[dim])
        up = [(i, (i + 1) % devices) for i in range(devices - 1)]
        down = [(j, i) for i, j in up]
        last = lax.slice_in_dim(x, length - width, length, axis=dim)
        leading = lax.slice_in_dim(x, 0, width, axis=dim)
        if devices == 2:
            first = lax.axis_index(axis) == 0
            got = lax.ppermute(jnp.where(first, last, leading), axis, [(0, 1), (1, 0)])
            nothing = jnp.zeros_like(got)
            before = jnp.where(first, nothing, got)
            after = jnp.where(first, got, nothing)
        else:
            before = lax.ppermute(last, axis, up)
            after = lax.ppermute(leading, axis, down)
        x = jnp.concatenate([before, x, after], axis=dim)
    return x


def shortened(x):
    return jax.tree.map(lambda a: a.astype(jnp.bfloat16) if a.dtype == jnp.float32 else a, x)


def depthwise(padded, kernel):
    channel_count = padded.shape[0]
    return lax.conv_general_dilated(
        padded[None],
        kernel[:, :, None, :],
        (1, 1),
        "VALID",
        dimension_numbers=("NCHW", "HWIO", "NCHW"),
        feature_group_count=channel_count,
        precision=lax.Precision.HIGHEST,
    )[0]


def gelu_parts(pre_act):
    cdf_val = 0.5 * (1.0 + lax.erf(pre_act * 0.7071067811865476))
    density = jnp.exp(-0.5 * pre_act * pre_act) * 0.3989422804014327
    return (pre_act * cdf_val, cdf_val + pre_act * density)


def contract(left, right, dim_left, dim_right):
    return lax.dot_general(
        left, right, (((dim_left,), (dim_right,)), ((), ())), preferred_element_type=jnp.float32
    )


def layer_norm_forward(conv_flat, norm_gain, norm_bias):
    mean_val = jnp.mean(conv_flat, axis=0)
    centered_values = conv_flat - mean_val
    variance = jnp.mean(centered_values * centered_values, axis=0)
    inverse_deviation = lax.rsqrt(variance + 1e-06)
    standardized_input = centered_values * inverse_deviation
    normalized_output = (standardized_input * norm_gain[:, None] + norm_bias[:, None]).astype(
        jnp.bfloat16
    )
    return (standardized_input, inverse_deviation, normalized_output)


def layer_norm_backward(normalized_gradient, standardized_input, inverse_deviation, norm_gain):
    standardized_gradient = normalized_gradient * norm_gain[:, None]
    initial_mean = jnp.mean(standardized_gradient, axis=0)
    product_mean = jnp.mean(standardized_gradient * standardized_input, axis=0)
    convolved_gradient = inverse_deviation * (
        standardized_gradient - initial_mean - standardized_input * product_mean
    )
    return (
        convolved_gradient,
        jnp.sum(normalized_gradient * standardized_input, axis=1),
        jnp.sum(normalized_gradient, axis=1),
    )


def kernel_grad_body(d_ref, p_ref, o_ref, shifted_ref, acc_ref):
    rows, cols, _ = d_ref.shape
    taps = o_ref.shape[0]
    side = int(round(taps ** 0.5))
    acc_ref[...] = jnp.zeros(acc_ref.shape, acc_ref.dtype)
    for j in range(side):
        shifted_ref[j] = p_ref[:, j : j + cols, :]

    def row_step(h, carry):
        d_row = d_ref[h]
        for i in range(side):
            for j in range(side):
                prod = d_row * shifted_ref[j, h + i]
                part = jnp.sum(prod.reshape(cols // 8, 8, prod.shape[-1]), axis=0)
                acc_ref[i * side + j] += part
        return carry

    lax.fori_loop(0, rows, row_step, 0)
    o_ref[...] = jnp.sum(acc_ref[...], axis=1)


def kernel_grad_minor(d_t, p_t):
    side = p_t.shape[0] - d_t.shape[0] + 1
    channel_count = d_t.shape[-1]
    summed = pl.pallas_call(
        kernel_grad_body,
        out_shape=jax.ShapeDtypeStruct((side * side, channel_count), jnp.float32),
        scratch_shapes=[
            pltpu.VMEM((side,) + p_t.shape[:1] + d_t.shape[1:], jnp.float32),
            pltpu.VMEM((side * side, 8, channel_count), jnp.float32),
        ],
    )(d_t, p_t)
    return summed.reshape(side, side, channel_count)


def flat_pack(values):
    return jnp.concatenate([v.reshape(-1) for v in values])


def flat_unpack(flat, values):
    out = []
    offset = 0
    for v in values:
        out.append(flat[offset : offset + v.size].reshape(v.shape))
        offset += v.size
    return out


def butterfly_steps(axes):
    steps = []
    for axis in axes:
        devices = lax.axis_size(axis)
        if devices & (devices - 1):
            steps.append((axis, 0))
            continue
        step = 1
        while step < devices:
            steps.append((axis, step))
            step *= 2
    return steps


def butterfly_step(flat, axis, step):
    if step == 0:
        return lax.psum(flat, axis)
    devices = lax.axis_size(axis)
    return flat + lax.ppermute(flat, axis, [(i, i ^ step) for i in range(devices)])


def butterfly_sum(values, axes, late_count):
    flat = flat_pack(values)
    first = butterfly_steps(axes[:1])
    order_a = first + butterfly_steps(axes[1:])[::-1]
    order_b = order_a[len(first) :] + order_a[: len(first)]
    half = sum(v.size for v in values[:late_count])
    part_a, part_b = flat[:half], flat[half:]
    for step_a, step_b in zip(order_a, order_b):
        part_a, part_b = butterfly_step(part_a, *step_a), butterfly_step(part_b, *step_b)
    return flat_unpack(jnp.concatenate([part_a, part_b]), values)


def gathered_weights(w_in, b_in, w_out):
    channel_count = w_in.shape[0]
    pieces = []
    rest = b_in
    for _ in range(3):
        piece = rest.astype(jnp.bfloat16)
        rest = rest - piece.astype(jnp.float32)
        pieces.append(piece[:, None])
    packed = jnp.concatenate([w_in.T, w_out] + pieces, axis=1)
    full = lax.all_gather(packed, "chan", axis=0, tiled=True)
    w_in_all = full[:, :channel_count].T
    w_out_all = full[:, channel_count : 2 * channel_count]
    parts = full[:, 2 * channel_count :].astype(jnp.float32)
    b_in_all = (parts[:, 0] + parts[:, 1]) + parts[:, 2]
    return w_in_all, b_in_all, w_out_all


def depthwise_minor(padded_t, kernel):
    channel_count = padded_t.shape[-1]
    return lax.conv_general_dilated(
        padded_t[None],
        kernel[:, :, None, :],
        (1, 1),
        "VALID",
        dimension_numbers=("NHWC", "HWIO", "NHWC"),
        feature_group_count=channel_count,
        precision=lax.Precision.HIGHEST,
    )[0]


def shards(
    feature,
    kernel,
    conv_bias,
    norm_gain,
    norm_bias,
    w_in,
    b_in,
    w_out,
    b_out,
    layer_scale,
    cotangent,
):
    channel_count, tile_rows, tile_cols = feature.shape
    pixel_count = tile_rows * tile_cols
    blocks = lax.axis_size("chan")
    share = w_in.shape[1]
    own = lax.axis_index("chan")
    w_in_all, b_in_all, w_out_all = gathered_weights(w_in, b_in, w_out)
    padded_bf = extended(feature, (("row", 1), ("col", 2)), 3)
    padded_t = jnp.transpose(padded_bf, (1, 2, 0)).astype(jnp.float32)
    total_pixels = pixel_count * lax.axis_size("row") * lax.axis_size("col")
    norm_factor = 1.0 / jnp.sqrt(jnp.float32(total_pixels))
    conv_flat = (depthwise_minor(padded_t, kernel) + conv_bias).reshape(pixel_count, channel_count)
    mean_val = jnp.mean(conv_flat, axis=1, keepdims=True)
    centered_values = conv_flat - mean_val
    variance = jnp.mean(centered_values * centered_values, axis=1, keepdims=True)
    inverse_deviation = lax.rsqrt(variance + 1e-06)
    standardized_input = centered_values * inverse_deviation
    normalized_output = (standardized_input * norm_gain + norm_bias).astype(jnp.bfloat16)
    pre_act = contract(normalized_output, w_in_all, 1, 0) + b_in_all
    gelu_val, gelu_slope = gelu_parts(pre_act)
    hidden = gelu_val.astype(jnp.bfloat16)
    out_partials = lax.dot_general(
        hidden.reshape(pixel_count, blocks, share),
        w_out_all.reshape(blocks, share, channel_count),
        (((2,), (1,)), ((1,), (0,))),
        preferred_element_type=jnp.float32,
    )
    mixed_sum = jnp.sum(out_partials.astype(jnp.bfloat16).astype(jnp.float32), axis=0)
    branch = mixed_sum + b_out
    feature_t = jnp.transpose(feature, (1, 2, 0)).reshape(pixel_count, channel_count)
    result_t = (feature_t.astype(jnp.float32) + layer_scale * branch).astype(jnp.bfloat16)
    result = jnp.transpose(result_t.reshape(tile_rows, tile_cols, channel_count), (2, 0, 1))
    cotangent_t = jnp.transpose(cotangent, (1, 2, 0))
    grad_out = cotangent_t.reshape(pixel_count, channel_count).astype(jnp.float32)
    g_branch = grad_out * layer_scale
    grad_layer_scale = jnp.sum(grad_out * branch, axis=0)
    grad_b_out = jnp.sum(g_branch, axis=0)
    g_out = g_branch.astype(jnp.bfloat16)
    grad_layer_scale, grad_b_out, g_out = lax.optimization_barrier((grad_layer_scale, grad_b_out, g_out))
    d_pre = contract(g_out, w_out_all, 1, 1) * gelu_slope
    g_pre = d_pre.astype(jnp.bfloat16)
    hidden_own = lax.dynamic_slice_in_dim(hidden, own * share, share, axis=1)
    g_pre_own = lax.dynamic_slice_in_dim(g_pre, own * share, share, axis=1)
    d_pre_own = lax.dynamic_slice_in_dim(d_pre, own * share, share, axis=1)
    grad_w_out = contract(hidden_own, g_out, 0, 0)
    grad_b_in = jnp.sum(d_pre_own, axis=0)
    grad_b_in, g_pre = lax.optimization_barrier((grad_b_in, g_pre))
    grad_w_in = contract(normalized_output, g_pre_own, 0, 0)
    dn_partials = lax.dot_general(
        g_pre.reshape(pixel_count, blocks, share),
        w_in_all.reshape(channel_count, blocks, share),
        (((2,), (2,)), ((1,), (1,))),
        preferred_element_type=jnp.float32,
    )
    normalized_gradient = jnp.sum(dn_partials.astype(jnp.bfloat16).astype(jnp.float32), axis=0)
    standardized_gradient = normalized_gradient * norm_gain
    initial_mean = jnp.mean(standardized_gradient, axis=1, keepdims=True)
    product_mean = jnp.mean(standardized_gradient * standardized_input, axis=1, keepdims=True)
    convolved_gradient = inverse_deviation * (
        standardized_gradient - initial_mean - standardized_input * product_mean
    )
    gain_portion = jnp.sum(normalized_gradient * standardized_input, axis=0)
    bias_portion = jnp.sum(normalized_gradient, axis=0)
    grad_conv_bias = jnp.sum(convolved_gradient, axis=0)
    d_t = convolved_gradient.reshape(tile_rows, tile_cols, channel_count)
    grad_kernel = kernel_grad_minor(d_t, padded_t)
    (
        grad_kernel,
        grad_conv_bias,
        gain_portion,
        bias_portion,
        grad_w_in,
        grad_b_in,
        grad_w_out,
        grad_b_out,
        grad_layer_scale,
    ) = butterfly_sum(
        (
            grad_kernel,
            grad_conv_bias,
            gain_portion,
            bias_portion,
            grad_w_in,
            grad_b_in,
            grad_w_out,
            grad_b_out,
            grad_layer_scale,
        ),
        ("row", "col"),
        4,
    )
    d_padded = extended(d_t.astype(jnp.bfloat16), (("row", 0), ("col", 1)), 3).astype(jnp.float32)
    grad_feature_t = (
        cotangent_t.astype(jnp.float32) + depthwise_minor(d_padded, kernel[::-1, ::-1])
    ).astype(jnp.bfloat16)
    grad_feature = jnp.transpose(grad_feature_t, (2, 0, 1))
    return (
        result,
        grad_feature,
        grad_kernel * norm_factor,
        grad_conv_bias * norm_factor,
        gain_portion * norm_factor,
        bias_portion * norm_factor,
        grad_w_in * norm_factor,
        grad_b_in * norm_factor,
        grad_w_out * norm_factor,
        grad_b_out * norm_factor,
        grad_layer_scale * norm_factor,
    )


def solution(mesh):
    return jax.shard_map(
        shards,
        mesh=mesh,
        in_specs=(
            P(None, "row", "col"),
            P(),
            P(),
            P(),
            P(),
            P(None, "chan"),
            P("chan"),
            P("chan", None),
            P(),
            P(),
            P(None, "row", "col"),
        ),
        out_specs=(
            P(None, "row", "col"),
            P(None, "row", "col"),
            P(),
            P(),
            P(),
            P(),
            P(None, "chan"),
            P("chan"),
            P("chan", None),
            P(),
            P(),
        ),
        check_vma=False,
    )
```

```python
import jax
import jax.numpy as jnp
from jax import lax
from jax.experimental import pallas as pl
from jax.experimental.pallas import tpu as pltpu
from jax.sharding import PartitionSpec as P


def extended(x, sides, width):
    for axis, dim in sides:
        devices, length = (lax.axis_size(axis), x.shape[dim])
        up = [(i, (i + 1) % devices) for i in range(devices - 1)]
        down = [(j, i) for i, j in up]
        last = lax.slice_in_dim(x, length - width, length, axis=dim)
        leading = lax.slice_in_dim(x, 0, width, axis=dim)
        if devices == 2:
            first = lax.axis_index(axis) == 0
            got = lax.ppermute(jnp.where(first, last, leading), axis, [(0, 1), (1, 0)])
            nothing = jnp.zeros_like(got)
            before = jnp.where(first, nothing, got)
            after = jnp.where(first, got, nothing)
        else:
            before = lax.ppermute(last, axis, up)
            after = lax.ppermute(leading, axis, down)
        x = jnp.concatenate([before, x, after], axis=dim)
    return x


def shortened(x):
    return jax.tree.map(lambda a: a.astype(jnp.bfloat16) if a.dtype == jnp.float32 else a, x)


def depthwise(padded, kernel):
    channel_count = padded.shape[0]
    return lax.conv_general_dilated(
        padded[None],
        kernel[:, :, None, :],
        (1, 1),
        "VALID",
        dimension_numbers=("NCHW", "HWIO", "NCHW"),
        feature_group_count=channel_count,
        precision=lax.Precision.HIGHEST,
    )[0]


def gelu_parts(pre_act):
    cdf_val = 0.5 * (1.0 + lax.erf(pre_act * 0.7071067811865476))
    density = jnp.exp(-0.5 * pre_act * pre_act) * 0.3989422804014327
    return (pre_act * cdf_val, cdf_val + pre_act * density)


def contract(left, right, dim_left, dim_right):
    return lax.dot_general(
        left, right, (((dim_left,), (dim_right,)), ((), ())), preferred_element_type=jnp.float32
    )


def layer_norm_forward(conv_flat, norm_gain, norm_bias):
    mean_val = jnp.mean(conv_flat, axis=0)
    centered_values = conv_flat - mean_val
    variance = jnp.mean(centered_values * centered_values, axis=0)
    inverse_deviation = lax.rsqrt(variance + 1e-06)
    standardized_input = centered_values * inverse_deviation
    normalized_output = (standardized_input * norm_gain[:, None] + norm_bias[:, None]).astype(
        jnp.bfloat16
    )
    return (standardized_input, inverse_deviation, normalized_output)


def layer_norm_backward(normalized_gradient, standardized_input, inverse_deviation, norm_gain):
    standardized_gradient = normalized_gradient * norm_gain[:, None]
    initial_mean = jnp.mean(standardized_gradient, axis=0)
    product_mean = jnp.mean(standardized_gradient * standardized_input, axis=0)
    convolved_gradient = inverse_deviation * (
        standardized_gradient - initial_mean - standardized_input * product_mean
    )
    return (
        convolved_gradient,
        jnp.sum(normalized_gradient * standardized_input, axis=1),
        jnp.sum(normalized_gradient, axis=1),
    )


def kernel_grad_body(d_ref, p_ref, o_ref, shifted_ref):
    rows, cols, _ = d_ref.shape
    taps = o_ref.shape[0]
    side = int(round(taps ** 0.5))
    o_ref[...] = jnp.zeros(o_ref.shape, o_ref.dtype)
    for j in range(side):
        shifted_ref[j] = p_ref[:, j : j + cols, :]

    def row_step(h, carry):
        d_row = d_ref[h]
        for i in range(side):
            for j in range(side):
                prod = d_row * shifted_ref[j, h + i]
                part = jnp.sum(prod.reshape(cols // 8, 8, prod.shape[-1]), axis=0)
                o_ref[i * side + j] += part
        return carry

    lax.fori_loop(0, rows, row_step, 0)


def kernel_grad_minor(d_t, p_t):
    side = p_t.shape[0] - d_t.shape[0] + 1
    channel_count = d_t.shape[-1]
    partial = pl.pallas_call(
        kernel_grad_body,
        out_shape=jax.ShapeDtypeStruct((side * side, 8, channel_count), jnp.float32),
        scratch_shapes=[pltpu.VMEM((side,) + p_t.shape[:1] + d_t.shape[1:], jnp.float32)],
    )(d_t, p_t)
    return jnp.sum(partial, axis=1).reshape(side, side, channel_count)


def flat_pack(values):
    return jnp.concatenate([v.reshape(-1) for v in values])


def flat_unpack(flat, values):
    out = []
    offset = 0
    for v in values:
        out.append(flat[offset : offset + v.size].reshape(v.shape))
        offset += v.size
    return out


def butterfly_steps(axes):
    steps = []
    for axis in axes:
        devices = lax.axis_size(axis)
        if devices & (devices - 1):
            steps.append((axis, 0))
            continue
        step = 1
        while step < devices:
            steps.append((axis, step))
            step *= 2
    return steps


def butterfly_step(flat, axis, step):
    if step == 0:
        return lax.psum(flat, axis)
    devices = lax.axis_size(axis)
    return flat + lax.ppermute(flat, axis, [(i, i ^ step) for i in range(devices)])


def butterfly_sum(values, axes, late_count):
    flat = flat_pack(values)
    first = butterfly_steps(axes[:1])
    order_a = first + butterfly_steps(axes[1:])[::-1]
    order_b = order_a[len(first) :] + order_a[: len(first)]
    half = sum(v.size for v in values[:late_count])
    part_a, part_b = flat[:half], flat[half:]
    for step_b, step_a in zip(order_a, order_b):
        part_a, part_b = butterfly_step(part_a, *step_a), butterfly_step(part_b, *step_b)
    return flat_unpack(jnp.concatenate([part_a, part_b]), values)


def gathered_weights(w_in, b_in, w_out):
    channel_count = w_in.shape[0]
    pieces = []
    rest = b_in
    for _ in range(3):
        piece = rest.astype(jnp.bfloat16)
        rest = rest - piece.astype(jnp.float32)
        pieces.append(piece[:, None])
    packed = jnp.concatenate([w_in.T, w_out] + pieces, axis=1)
    full = lax.all_gather(packed, "chan", axis=0, tiled=True)
    w_in_all = full[:, :channel_count].T
    w_out_all = full[:, channel_count : 2 * channel_count]
    parts = full[:, 2 * channel_count :].astype(jnp.float32)
    b_in_all = (parts[:, 0] + parts[:, 1]) + parts[:, 2]
    return w_in_all, b_in_all, w_out_all


def depthwise_minor(padded_t, kernel):
    channel_count = padded_t.shape[-1]
    return lax.conv_general_dilated(
        padded_t[None],
        kernel[:, :, None, :],
        (1, 1),
        "VALID",
        dimension_numbers=("NHWC", "HWIO", "NHWC"),
        feature_group_count=channel_count,
        precision=lax.Precision.HIGHEST,
    )[0]


def shards(
    feature,
    kernel,
    conv_bias,
    norm_gain,
    norm_bias,
    w_in,
    b_in,
    w_out,
    b_out,
    layer_scale,
    cotangent,
):
    channel_count, tile_rows, tile_cols = feature.shape
    pixel_count = tile_rows * tile_cols
    blocks = lax.axis_size("chan")
    share = w_in.shape[1]
    own = lax.axis_index("chan")
    w_in_all, b_in_all, w_out_all = gathered_weights(w_in, b_in, w_out)
    padded_bf = extended(feature, (("row", 1), ("col", 2)), 3)
    padded_t = jnp.transpose(padded_bf, (1, 2, 0)).astype(jnp.float32)
    total_pixels = pixel_count * lax.axis_size("row") * lax.axis_size("col")
    norm_factor = 1.0 / jnp.sqrt(jnp.float32(total_pixels))
    conv_flat = (depthwise_minor(padded_t, kernel) + conv_bias).reshape(pixel_count, channel_count)
    mean_val = jnp.mean(conv_flat, axis=1, keepdims=True)
    centered_values = conv_flat - mean_val
    variance = jnp.mean(centered_values * centered_values, axis=1, keepdims=True)
    inverse_deviation = lax.rsqrt(variance + 1e-06)
    standardized_input = centered_values * inverse_deviation
    normalized_output = (standardized_input * norm_gain + norm_bias).astype(jnp.bfloat16)
    pre_act = contract(normalized_output, w_in_all, 1, 0) + b_in_all
    gelu_val, gelu_slope = gelu_parts(pre_act)
    hidden = gelu_val.astype(jnp.bfloat16)
    out_partials = lax.dot_general(
        hidden.reshape(pixel_count, blocks, share),
        w_out_all.reshape(blocks, share, channel_count),
        (((2,), (1,)), ((1,), (0,))),
        preferred_element_type=jnp.float32,
    )
    mixed_sum = jnp.sum(out_partials.astype(jnp.bfloat16).astype(jnp.float32), axis=0)
    branch = mixed_sum + b_out
    feature_t = jnp.transpose(feature, (1, 2, 0)).reshape(pixel_count, channel_count)
    result_t = (feature_t.astype(jnp.float32) + layer_scale * branch).astype(jnp.bfloat16)
    result = jnp.transpose(result_t.reshape(tile_rows, tile_cols, channel_count), (2, 0, 1))
    cotangent_t = jnp.transpose(cotangent, (1, 2, 0))
    grad_out = cotangent_t.reshape(pixel_count, channel_count).astype(jnp.float32)
    g_branch = grad_out * layer_scale
    grad_layer_scale = jnp.sum(grad_out * branch, axis=0)
    grad_b_out = jnp.sum(g_branch, axis=0)
    g_out = g_branch.astype(jnp.bfloat16)
    grad_layer_scale, grad_b_out, g_out = lax.optimization_barrier((grad_layer_scale, grad_b_out, g_out))
    d_pre = contract(g_out, w_out_all, 1, 1) * gelu_slope
    g_pre = d_pre.astype(jnp.bfloat16)
    hidden_own = lax.dynamic_slice_in_dim(hidden, own * share, share, axis=1)
    g_pre_own = lax.dynamic_slice_in_dim(g_pre, own * share, share, axis=1)
    d_pre_own = lax.dynamic_slice_in_dim(d_pre, own * share, share, axis=1)
    grad_w_out = contract(hidden_own, g_out, 0, 0)
    grad_b_in = jnp.sum(d_pre_own, axis=0)
    grad_b_in, g_pre = lax.optimization_barrier((grad_b_in, g_pre))
    grad_w_in = contract(normalized_output, g_pre_own, 0, 0)
    dn_partials = lax.dot_general(
        g_pre.reshape(pixel_count, blocks, share),
        w_in_all.reshape(channel_count, blocks, share),
        (((2,), (2,)), ((1,), (1,))),
        preferred_element_type=jnp.float32,
    )
    normalized_gradient = jnp.sum(dn_partials.astype(jnp.bfloat16).astype(jnp.float32), axis=0)
    standardized_gradient = normalized_gradient * norm_gain
    initial_mean = jnp.mean(standardized_gradient, axis=1, keepdims=True)
    product_mean = jnp.mean(standardized_gradient * standardized_input, axis=1, keepdims=True)
    convolved_gradient = inverse_deviation * (
        standardized_gradient - initial_mean - standardized_input * product_mean
    )
    gain_portion = jnp.sum(normalized_gradient * standardized_input, axis=0)
    bias_portion = jnp.sum(normalized_gradient, axis=0)
    grad_conv_bias = jnp.sum(convolved_gradient, axis=0)
    d_t = convolved_gradient.reshape(tile_rows, tile_cols, channel_count)
    grad_kernel = kernel_grad_minor(d_t, padded_t)
    (
        grad_kernel,
        grad_conv_bias,
        gain_portion,
        bias_portion,
        grad_w_in,
        grad_b_in,
        grad_w_out,
        grad_b_out,
        grad_layer_scale,
    ) = butterfly_sum(
        (
            grad_kernel,
            grad_conv_bias,
            gain_portion,
            bias_portion,
            grad_w_in,
            grad_b_in,
            grad_w_out,
            grad_b_out,
            grad_layer_scale,
        ),
        ("row", "col"),
        4,
    )
    d_padded = extended(d_t.astype(jnp.bfloat16), (("row", 0), ("col", 1)), 3).astype(jnp.float32)
    grad_feature_t = (
        cotangent_t.astype(jnp.float32) + depthwise_minor(d_padded, kernel[::-1, ::-1])
    ).astype(jnp.bfloat16)
    grad_feature = jnp.transpose(grad_feature_t, (2, 0, 1))
    return (
        result,
        grad_feature,
        grad_kernel * norm_factor,
        grad_conv_bias * norm_factor,
        gain_portion * norm_factor,
        bias_portion * norm_factor,
        grad_w_in * norm_factor,
        grad_b_in * norm_factor,
        grad_w_out * norm_factor,
        grad_b_out * norm_factor,
        grad_layer_scale * norm_factor,
    )


def solution(mesh):
    return jax.shard_map(
        shards,
        mesh=mesh,
        in_specs=(
            P(None, "row", "col"),
            P(),
            P(),
            P(),
            P(),
            P(None, "chan"),
            P("chan"),
            P("chan", None),
            P(),
            P(),
            P(None, "row", "col"),
        ),
        out_specs=(
            P(None, "row", "col"),
            P(None, "row", "col"),
            P(),
            P(),
            P(),
            P(),
            P(None, "chan"),
            P("chan"),
            P("chan", None),
            P(),
            P(),
        ),
        check_vma=False,
    )
```

```python
import jax
import jax.numpy as jnp
from jax import lax
from jax.experimental import pallas as pl
from jax.experimental.pallas import tpu as pltpu
from jax.sharding import PartitionSpec as P


def extended(x, sides, width):
    for axis, dim in sides:
        devices, length = (lax.axis_size(axis), x.shape[dim])
        up = [(i, (i + 1) % devices) for i in range(devices - 1)]
        down = [(j, i) for i, j in up]
        last = lax.slice_in_dim(x, length - width, length, axis=dim)
        leading = lax.slice_in_dim(x, 0, width, axis=dim)
        if devices == 2:
            first = lax.axis_index(axis) == 0
            got = lax.ppermute(jnp.where(first, last, leading), axis, [(0, 1), (1, 0)])
            nothing = jnp.zeros_like(got)
            before = jnp.where(first, nothing, got)
            after = jnp.where(first, got, nothing)
        else:
            before = lax.ppermute(last, axis, up)
            after = lax.ppermute(leading, axis, down)
        x = jnp.concatenate([before, x, after], axis=dim)
    return x


def shortened(x):
    return jax.tree.map(lambda a: a.astype(jnp.bfloat16) if a.dtype == jnp.float32 else a, x)


def depthwise(padded, kernel):
    channel_count = padded.shape[0]
    return lax.conv_general_dilated(
        padded[None],
        kernel[:, :, None, :],
        (1, 1),
        "VALID",
        dimension_numbers=("NCHW", "HWIO", "NCHW"),
        feature_group_count=channel_count,
        precision=lax.Precision.HIGHEST,
    )[0]


def gelu_parts(pre_act):
    cdf_val = 0.5 * (1.0 + lax.erf(pre_act * 0.7071067811865476))
    density = jnp.exp(-0.5 * pre_act * pre_act) * 0.3989422804014327
    return (pre_act * cdf_val, cdf_val + pre_act * density)


def contract(left, right, dim_left, dim_right):
    return lax.dot_general(
        left, right, (((dim_left,), (dim_right,)), ((), ())), preferred_element_type=jnp.float32
    )


def layer_norm_forward(conv_flat, norm_gain, norm_bias):
    mean_val = jnp.mean(conv_flat, axis=0)
    centered_values = conv_flat - mean_val
    variance = jnp.mean(centered_values * centered_values, axis=0)
    inverse_deviation = lax.rsqrt(variance + 1e-06)
    standardized_input = centered_values * inverse_deviation
    normalized_output = (standardized_input * norm_gain[:, None] + norm_bias[:, None]).astype(
        jnp.bfloat16
    )
    return (standardized_input, inverse_deviation, normalized_output)


def layer_norm_backward(normalized_gradient, standardized_input, inverse_deviation, norm_gain):
    standardized_gradient = normalized_gradient * norm_gain[:, None]
    initial_mean = jnp.mean(standardized_gradient, axis=0)
    product_mean = jnp.mean(standardized_gradient * standardized_input, axis=0)
    convolved_gradient = inverse_deviation * (
        standardized_gradient - initial_mean - standardized_input * product_mean
    )
    return (
        convolved_gradient,
        jnp.sum(normalized_gradient * standardized_input, axis=1),
        jnp.sum(normalized_gradient, axis=1),
    )


def kernel_grad_body(d_ref, p_ref, o_ref, shifted_ref):
    rows, cols, _ = d_ref.shape
    taps = o_ref.shape[0]
    side = int(round(taps ** 0.5))
    o_ref[...] = jnp.zeros(o_ref.shape, o_ref.dtype)
    for j in range(side):
        shifted_ref[j] = p_ref[:, j : j + cols, :]

    def row_step(h, carry):
        d_row = d_ref[h]
        for i in range(side):
            for j in range(side):
                prod = d_row * shifted_ref[j, h + i]
                part = jnp.sum(prod.reshape(cols // 8, 8, prod.shape[-1]), axis=0)
                o_ref[i * side + j] += part
        return carry

    lax.fori_loop(0, rows, row_step, 0)


def kernel_grad_minor(d_t, p_t):
    side = p_t.shape[0] - d_t.shape[0] + 1
    channel_count = d_t.shape[-1]
    partial = pl.pallas_call(
        kernel_grad_body,
        out_shape=jax.ShapeDtypeStruct((side * side, 8, channel_count), jnp.float32),
        scratch_shapes=[pltpu.VMEM((side,) + p_t.shape[:1] + d_t.shape[1:], jnp.float32)],
    )(d_t, p_t)
    return jnp.sum(partial, axis=1).reshape(side, side, channel_count)


def flat_pack(values):
    return jnp.concatenate([v.reshape(-1) for v in values])


def flat_unpack(flat, values):
    out = []
    offset = 0
    for v in values:
        out.append(flat[offset : offset + v.size].reshape(v.shape))
        offset += v.size
    return out


def butterfly_steps(axes):
    steps = []
    for axis in axes:
        devices = lax.axis_size(axis)
        if devices & (devices - 1):
            steps.append((axis, 0))
            continue
        step = 1
        while step < devices:
            steps.append((axis, step))
            step *= 2
    return steps


def butterfly_step(flat, axis, step):
    if step == 0:
        return lax.psum(flat, axis)
    devices = lax.axis_size(axis)
    return flat + lax.ppermute(flat, axis, [(i, i ^ step) for i in range(devices)])


def butterfly_sum(values, axes, late_count):
    flat = flat_pack(values)
    first = butterfly_steps(axes[:1])
    rotated = first + butterfly_steps(axes[1:])[::-1]
    order_a = first + butterfly_steps(axes[1:])
    order_b = rotated[len(first) :] + rotated[: len(first)]
    half = sum(v.size for v in values[:late_count])
    part_a, part_b = flat[:half], flat[half:]
    for step_a, step_b in zip(order_a, order_b):
        part_a, part_b = butterfly_step(part_a, *step_a), butterfly_step(part_b, *step_b)
    return flat_unpack(jnp.concatenate([part_a, part_b]), values)


def gathered_weights(w_in, b_in, w_out):
    channel_count = w_in.shape[0]
    pieces = []
    rest = b_in
    for _ in range(3):
        piece = rest.astype(jnp.bfloat16)
        rest = rest - piece.astype(jnp.float32)
        pieces.append(piece[:, None])
    packed = jnp.concatenate([w_in.T, w_out] + pieces, axis=1)
    full = lax.all_gather(packed, "chan", axis=0, tiled=True)
    w_in_all = full[:, :channel_count].T
    w_out_all = full[:, channel_count : 2 * channel_count]
    parts = full[:, 2 * channel_count :].astype(jnp.float32)
    b_in_all = (parts[:, 0] + parts[:, 1]) + parts[:, 2]
    return w_in_all, b_in_all, w_out_all


def depthwise_minor(padded_t, kernel):
    channel_count = padded_t.shape[-1]
    return lax.conv_general_dilated(
        padded_t[None],
        kernel[:, :, None, :],
        (1, 1),
        "VALID",
        dimension_numbers=("NHWC", "HWIO", "NHWC"),
        feature_group_count=channel_count,
        precision=lax.Precision.HIGHEST,
    )[0]


def shards(
    feature,
    kernel,
    conv_bias,
    norm_gain,
    norm_bias,
    w_in,
    b_in,
    w_out,
    b_out,
    layer_scale,
    cotangent,
):
    channel_count, tile_rows, tile_cols = feature.shape
    pixel_count = tile_rows * tile_cols
    blocks = lax.axis_size("chan")
    share = w_in.shape[1]
    own = lax.axis_index("chan")
    w_in_all, b_in_all, w_out_all = gathered_weights(w_in, b_in, w_out)
    padded_bf = extended(feature, (("row", 1), ("col", 2)), 3)
    padded_t = jnp.transpose(padded_bf, (1, 2, 0)).astype(jnp.float32)
    total_pixels = pixel_count * lax.axis_size("row") * lax.axis_size("col")
    norm_factor = 1.0 / jnp.sqrt(jnp.float32(total_pixels))
    conv_flat = (depthwise_minor(padded_t, kernel) + conv_bias).reshape(pixel_count, channel_count)
    mean_val = jnp.mean(conv_flat, axis=1, keepdims=True)
    centered_values = conv_flat - mean_val
    variance = jnp.mean(centered_values * centered_values, axis=1, keepdims=True)
    inverse_deviation = lax.rsqrt(variance + 1e-06)
    standardized_input = centered_values * inverse_deviation
    normalized_output = (standardized_input * norm_gain + norm_bias).astype(jnp.bfloat16)
    pre_act = contract(normalized_output, w_in_all, 1, 0) + b_in_all
    gelu_val, gelu_slope = gelu_parts(pre_act)
    hidden = gelu_val.astype(jnp.bfloat16)
    out_partials = lax.dot_general(
        hidden.reshape(pixel_count, blocks, share),
        w_out_all.reshape(blocks, share, channel_count),
        (((2,), (1,)), ((1,), (0,))),
        preferred_element_type=jnp.float32,
    )
    mixed_sum = jnp.sum(out_partials.astype(jnp.bfloat16).astype(jnp.float32), axis=0)
    branch = mixed_sum + b_out
    feature_t = jnp.transpose(feature, (1, 2, 0)).reshape(pixel_count, channel_count)
    result_t = (feature_t.astype(jnp.float32) + layer_scale * branch).astype(jnp.bfloat16)
    result = jnp.transpose(result_t.reshape(tile_rows, tile_cols, channel_count), (2, 0, 1))
    cotangent_t = jnp.transpose(cotangent, (1, 2, 0))
    grad_out = cotangent_t.reshape(pixel_count, channel_count).astype(jnp.float32)
    g_branch = grad_out * layer_scale
    grad_layer_scale = jnp.sum(grad_out * branch, axis=0)
    grad_b_out = jnp.sum(g_branch, axis=0)
    g_out = g_branch.astype(jnp.bfloat16)
    grad_layer_scale, grad_b_out, g_out = lax.optimization_barrier((grad_layer_scale, grad_b_out, g_out))
    d_pre = contract(g_out, w_out_all, 1, 1) * gelu_slope
    g_pre = d_pre.astype(jnp.bfloat16)
    hidden_own = lax.dynamic_slice_in_dim(hidden, own * share, share, axis=1)
    g_pre_own = lax.dynamic_slice_in_dim(g_pre, own * share, share, axis=1)
    d_pre_own = lax.dynamic_slice_in_dim(d_pre, own * share, share, axis=1)
    grad_w_out = contract(hidden_own, g_out, 0, 0)
    grad_b_in = jnp.sum(d_pre_own, axis=0)
    grad_b_in, g_pre = lax.optimization_barrier((grad_b_in, g_pre))
    grad_w_in = contract(normalized_output, g_pre_own, 0, 0)
    dn_partials = lax.dot_general(
        g_pre.reshape(pixel_count, blocks, share),
        w_in_all.reshape(channel_count, blocks, share),
        (((2,), (2,)), ((1,), (1,))),
        preferred_element_type=jnp.float32,
    )
    normalized_gradient = jnp.sum(dn_partials.astype(jnp.bfloat16).astype(jnp.float32), axis=0)
    standardized_gradient = normalized_gradient * norm_gain
    initial_mean = jnp.mean(standardized_gradient, axis=1, keepdims=True)
    product_mean = jnp.mean(standardized_gradient * standardized_input, axis=1, keepdims=True)
    convolved_gradient = inverse_deviation * (
        standardized_gradient - initial_mean - standardized_input * product_mean
    )
    gain_portion = jnp.sum(normalized_gradient * standardized_input, axis=0)
    bias_portion = jnp.sum(normalized_gradient, axis=0)
    grad_conv_bias = jnp.sum(convolved_gradient, axis=0)
    d_t = convolved_gradient.reshape(tile_rows, tile_cols, channel_count)
    grad_kernel = kernel_grad_minor(d_t, padded_t)
    (
        grad_kernel,
        grad_conv_bias,
        gain_portion,
        bias_portion,
        grad_w_in,
        grad_b_in,
        grad_w_out,
        grad_b_out,
        grad_layer_scale,
    ) = butterfly_sum(
        (
            grad_kernel,
            grad_conv_bias,
            gain_portion,
            bias_portion,
            grad_w_in,
            grad_b_in,
            grad_w_out,
            grad_b_out,
            grad_layer_scale,
        ),
        ("row", "col"),
        4,
    )
    d_padded = extended(d_t.astype(jnp.bfloat16), (("row", 0), ("col", 1)), 3).astype(jnp.float32)
    grad_feature_t = (
        cotangent_t.astype(jnp.float32) + depthwise_minor(d_padded, kernel[::-1, ::-1])
    ).astype(jnp.bfloat16)
    grad_feature = jnp.transpose(grad_feature_t, (2, 0, 1))
    return (
        result,
        grad_feature,
        grad_kernel * norm_factor,
        grad_conv_bias * norm_factor,
        gain_portion * norm_factor,
        bias_portion * norm_factor,
        grad_w_in * norm_factor,
        grad_b_in * norm_factor,
        grad_w_out * norm_factor,
        grad_b_out * norm_factor,
        grad_layer_scale * norm_factor,
    )


def solution(mesh):
    return jax.shard_map(
        shards,
        mesh=mesh,
        in_specs=(
            P(None, "row", "col"),
            P(),
            P(),
            P(),
            P(),
            P(None, "chan"),
            P("chan"),
            P("chan", None),
            P(),
            P(),
            P(None, "row", "col"),
        ),
        out_specs=(
            P(None, "row", "col"),
            P(None, "row", "col"),
            P(),
            P(),
            P(),
            P(),
            P(None, "chan"),
            P("chan"),
            P("chan", None),
            P(),
            P(),
        ),
        check_vma=False,
    )
```
